32 devices in a mesh: win: 8 (over y, x, core), seq: 4 (over z).
Axes of the slice: x: 2, y: 2, z: 4, core: 2. Of those that a mesh axis runs over, the one named last changes fastest.
Arguments:
- embeddings: bfloat16 [8, 512, 768], P('win', 'seq'), may hold values from -6 to 6
- norm_gain: float32 [768], replicated, may hold values from 0.5 to 2
- conv_weight: bfloat16 [3, 768, 768], replicated, may hold values from -0.125 to 0.125
- conv_bias: float32 [768], replicated, may hold values from -3 to 3
- dilation: int32 [8], P('win'), may hold values from 1 to 64, as said below
- donor_bins: int32 [8, 256], P('win'), may hold values from 0 to 511
- acceptor_bins: int32 [8, 256], P('win'), may hold values from 0 to 511
- junction_count: int32 [8], P('win'), may hold values from 0 to 256, as said below
- donor_proj: bfloat16 [768, 512], replicated, may hold values from -0.21875 to 0.21875
- acceptor_proj: bfloat16 [768, 512], replicated, may hold values from -0.21875 to 0.21875
- out_cotangent: bfloat16 [8, 512, 768], P('win', 'seq'), may hold values from -6 to 6
- score_cotangent: float32 [8, 256], P('win'), may hold values from -6 to 6
Outputs:
- block_out: bfloat16 [8, 512, 768], P('win', 'seq')
- junction_scores: float32 [8, 256], P('win', 'seq')
- input_grad: bfloat16 [8, 512, 768], P('win', 'seq')
- weight_grad: float32 [589824], P(('win', 'seq'))
The draws below stay inside these ranges and needn't reach their ends.
Inputs may be any that keep to these rules, and one draw needn't show every extreme that they name: `dilation`: one rate a window; some window has the rate 64. `junction_count`: slots at list positions under the count are live, the others padding; some window has all 256 slots live.
All inputs are finite; a program needn't handle non-finite values.
Results may differ from the reference program's by a relative error of at most 0.014.
Values may be sent and summed in bfloat16 or wider, within the bound.
No kernel may reach another device: no remote copies, remote signals or barrier semaphores. Data moves between devices by JAX's collectives and lax.ppermute only.
A program may use at most 64 MiB of HBM per device.

```python
import math
import jax
import jax.numpy as jnp
from jax import lax

C = 768
HJ = 512
MAXDIL = 64
BINS = 512
NJ = 256
WINDOWS = 8


def draw_dilation(key, part):
    key_rates, key_where = jax.random.split(key)
    rates = jax.random.randint(key_rates, (WINDOWS,), 1, MAXDIL + 1)
    chosen = jax.random.randint(key_where, (), 0, WINDOWS)
    return jnp.where(jnp.arange(WINDOWS) == chosen, MAXDIL, rates).astype(jnp.int32)


def draw_junction_count(key, part):
    key_counts, key_where = jax.random.split(jax.random.fold_in(key, 7))
    counts = jax.random.randint(key_counts, (WINDOWS,), 0, NJ + 1)
    chosen = jax.random.randint(key_where, (), 0, WINDOWS)
    return jnp.where(jnp.arange(WINDOWS) == chosen, NJ, counts).astype(jnp.int32)


def set_ends(array, stream_key, low, high):
    dims = array.shape
    spot = [jax.random.randint(jax.random.fold_in(stream_key, axis), (), 0, dims[axis]) for axis in range(len(dims))]
    array = array.at[tuple(spot)].set(low)
    longest = dims.index(max(dims))
    spot[longest] = (spot[longest] + 1) % dims[longest]
    return array.at[tuple(spot)].set(high)


def levels(stream_key, dims, pieces, least, largest):
    gain, own = 1.0, jax.random.fold_in(stream_key, 6)
    for axis_at, parts in pieces:
        steps = jnp.exp(jax.random.uniform(jax.random.fold_in(own, axis_at), (parts,), jnp.float32, least / len(pieces), largest / len(pieces)))
        gain = gain * jnp.repeat(steps, dims[axis_at] // parts).reshape([-1 if axis == axis_at else 1 for axis in range(len(dims))])
    return gain


def bell_draw(rng, shape, scale, reach, pieces=(), kind=jnp.bfloat16):
    array = scale * jax.random.normal(rng, shape, jnp.float32)
    if pieces:
        array = array * levels(rng, shape, pieces, -0.22, 0.18)
    return jnp.clip(array, -reach, reach).astype(kind)


def setup_inputs(seed: int = 0) -> dict:
    streams_of = jax.random.split(jax.random.key(seed), 13)
    return {
        "embeddings": bell_draw(streams_of[0], (WINDOWS, BINS, C), 1.0, 6.0, ((0, 8), (1, 4))),
        "norm_gain": jnp.clip(jnp.exp(jax.random.uniform(streams_of[1], (C,), jnp.float32, math.log(0.5), math.log(2.0))), 0.5, 2.0),
        "conv_weight": bell_draw(streams_of[2], (3, C, C), (3 * C) ** -0.5, 0.125),
        "conv_bias": bell_draw(streams_of[3], (C,), 0.5, 3.0, (), jnp.float32),
        "dilation": draw_dilation(jax.random.fold_in(streams_of[12], 71), 0),
        "donor_bins": set_ends(jax.random.randint(streams_of[5], (WINDOWS, NJ), 0, BINS), jax.random.fold_in(streams_of[5], 1), 0, BINS - 1).astype(jnp.int32),
        "acceptor_bins": set_ends(jax.random.randint(streams_of[6], (WINDOWS, NJ), 0, BINS), jax.random.fold_in(streams_of[6], 1), 0, BINS - 1).astype(jnp.int32),
        "junction_count": draw_junction_count(jax.random.fold_in(streams_of[12], 71), 0),
        "donor_proj": bell_draw(streams_of[8], (C, HJ), C ** -0.5, 0.21875),
        "acceptor_proj": bell_draw(streams_of[9], (C, HJ), C ** -0.5, 0.21875),
        "out_cotangent": bell_draw(streams_of[10], (WINDOWS, BINS, C), 1.0, 6.0, ((0, 8), (1, 4))),
        "score_cotangent": bell_draw(streams_of[11], (WINDOWS, NJ), 1.0, 6.0, ((0, 8),), jnp.float32),
    }


epsilon = 1e-06
gelu_scale = 0.7978845608028654
gelu_cubic = 0.044715

def gelu_value(inputs):
    inner = gelu_scale * (inputs + gelu_cubic * inputs * inputs * inputs)
    return 0.5 * inputs * (1.0 + jnp.tanh(inner))

def gelu_slope(inputs):
    inner = gelu_scale * (inputs + gelu_cubic * inputs * inputs * inputs)
    tangent = jnp.tanh(inner)
    return 0.5 * (1.0 + tangent) + 0.5 * inputs * (1.0 - tangent * tangent) * gelu_scale * (1.0 + 3.0 * gelu_cubic * inputs * inputs)

def flip_strand(values):
    return values[:, ::-1, ::-1]

def shifted(values, dilation, sign):
    padded = jnp.pad(values, ((0, 0), (MAXDIL, MAXDIL), (0, 0)))

    def one_window(window_rows, rate):
        slices = [lax.dynamic_slice_in_dim(window_rows, MAXDIL + sign * (tap_index - 1) * rate, BINS, 0) for tap_index in range(3)]
        return jnp.concatenate(slices, axis=1)
    return jax.vmap(one_window)(padded, dilation).reshape(-1, 3 * C)

def pick_rows(table, indices):
    return jnp.take(table, indices, axis=0)

def reference(embeddings, norm_gain, conv_weight, conv_bias, dilation, donor_bins, acceptor_bins, junction_count, donor_proj, acceptor_proj, out_cotangent, score_cotangent):
    as_float = embeddings.astype(jnp.float32)
    inverse = lax.rsqrt(lax.optimization_barrier(jnp.mean(as_float * as_float, axis=2, keepdims=True)) + epsilon)
    normed = as_float * inverse
    pre_fwd = normed * norm_gain
    pre_rev = flip_strand(normed) * norm_gain
    act_fwd = gelu_value(pre_fwd).astype(jnp.bfloat16)
    act_rev = gelu_value(pre_rev).astype(jnp.bfloat16)
    flat_weight = conv_weight.reshape(3 * C, C)
    taps_fwd = shifted(act_fwd, dilation, 1)
    taps_rev = shifted(act_rev, dilation, 1)
    conv_fwd = (jnp.dot(taps_fwd, flat_weight, preferred_element_type=jnp.float32) + conv_bias).astype(jnp.bfloat16).reshape(WINDOWS, BINS, C)
    conv_rev = (jnp.dot(taps_rev, flat_weight, preferred_element_type=jnp.float32) + conv_bias).astype(jnp.bfloat16).reshape(WINDOWS, BINS, C)
    block_float = as_float + 0.5 * (conv_fwd.astype(jnp.float32) + flip_strand(conv_rev).astype(jnp.float32))
    block_out = block_float.astype(jnp.bfloat16)
    flat_out = block_out.reshape(-1, C)
    proj_donor = jnp.dot(flat_out, donor_proj, preferred_element_type=jnp.float32).astype(jnp.bfloat16).reshape(WINDOWS, BINS, HJ)
    proj_acceptor = jnp.dot(flat_out, acceptor_proj, preferred_element_type=jnp.float32).astype(jnp.bfloat16).reshape(WINDOWS, BINS, HJ)
    rows_donor = jax.vmap(pick_rows)(proj_donor, donor_bins).astype(jnp.float32)
    rows_acceptor = jax.vmap(pick_rows)(proj_acceptor, acceptor_bins).astype(jnp.float32)
    live_mask = (jnp.arange(NJ)[None, :] < junction_count[:, None]).astype(jnp.float32)
    score_scale = HJ ** (-0.5)
    junction_scores = live_mask * lax.optimization_barrier(jnp.sum(rows_donor * rows_acceptor, axis=2)) * score_scale
    pair_weight = score_cotangent * live_mask * score_scale

    def add_rows(indices, values):
        return jnp.zeros((BINS, HJ), jnp.float32).at[indices].add(values)
    grad_donor = jax.vmap(add_rows)(donor_bins, pair_weight[:, :, None] * rows_acceptor).astype(jnp.bfloat16)
    grad_acceptor = jax.vmap(add_rows)(acceptor_bins, pair_weight[:, :, None] * rows_donor).astype(jnp.bfloat16)
    out_grad = out_cotangent.astype(jnp.float32).reshape(-1, C)
    out_grad = out_grad + jnp.dot(grad_donor.reshape(-1, HJ), donor_proj.T, preferred_element_type=jnp.float32)
    out_grad = out_grad + jnp.dot(grad_acceptor.reshape(-1, HJ), acceptor_proj.T, preferred_element_type=jnp.float32)
    out_grad = out_grad.reshape(WINDOWS, BINS, C)
    conv_grad = (0.5 * out_grad).astype(jnp.bfloat16)
    conv_grad_rev = flip_strand(conv_grad)
    back_fwd = shifted(conv_grad, dilation, -1)
    back_rev = shifted(conv_grad_rev, dilation, -1)
    dact_fwd = jnp.zeros((WINDOWS * BINS, C), jnp.float32)
    dact_rev = jnp.zeros((WINDOWS * BINS, C), jnp.float32)
    for tap_index in range(3):
        dact_fwd = dact_fwd + jnp.dot(back_fwd[:, tap_index * C:(tap_index + 1) * C], conv_weight[tap_index].T, preferred_element_type=jnp.float32)
        dact_rev = dact_rev + jnp.dot(back_rev[:, tap_index * C:(tap_index + 1) * C], conv_weight[tap_index].T, preferred_element_type=jnp.float32)
    dact_fwd = dact_fwd.reshape(WINDOWS, BINS, C)
    dact_rev = dact_rev.reshape(WINDOWS, BINS, C)
    norm_rev = flip_strand(dact_rev * gelu_slope(pre_rev) * norm_gain).astype(jnp.bfloat16)
    norm_grad = dact_fwd * gelu_slope(pre_fwd) * norm_gain + norm_rev.astype(jnp.float32)
    input_grad = (out_grad + inverse * (norm_grad - normed * lax.optimization_barrier(jnp.mean(norm_grad * normed, axis=2, keepdims=True)))).astype(jnp.bfloat16)
    contract = (((0,), (0,)), ((), ()))
    term_fwd = lax.dot_general(taps_fwd[:, C:2 * C], conv_grad.reshape(-1, C), contract, preferred_element_type=jnp.float32)
    term_rev = lax.dot_general(taps_rev[:, C:2 * C], conv_grad_rev.reshape(-1, C), contract, preferred_element_type=jnp.float32)
    weight_grad = ((term_fwd + term_rev) / WINDOWS).reshape(C * C)
    return (block_out, junction_scores, input_grad, weight_grad)
```

```python
import jax
import jax.numpy as jnp
from jax import lax
from jax.sharding import PartitionSpec as P

epsilon = 1e-06
gelu_scale = 0.7978845608028654
gelu_cubic = 0.044715


def with_halo(block, sides, width):
    for axis, dim in sides:
        count = lax.axis_size(axis)
        forward = [(i, i + 1) for i in range(count - 1)]
        backward = [(target, source) for source, target in forward]
        low = lax.ppermute(
            lax.slice_in_dim(block, block.shape[dim] - width, None, axis=dim), axis, forward
        )
        high = lax.ppermute(lax.slice_in_dim(block, 0, width, axis=dim), axis, backward)
        block = jnp.concatenate([low, block, high], axis=dim)
    return block


def gelu_value(inputs):
    inner = gelu_scale * (inputs + gelu_cubic * inputs * inputs * inputs)
    return 0.5 * inputs * (1.0 + jnp.tanh(inner))


def gelu_slope(inputs):
    inner = gelu_scale * (inputs + gelu_cubic * inputs * inputs * inputs)
    tangent = jnp.tanh(inner)
    return 0.5 * (1.0 + tangent) + 0.5 * inputs * (1.0 - tangent * tangent) * gelu_scale * (
        1.0 + 3.0 * gelu_cubic * inputs * inputs
    )


def tap_stack(padded, dilate, rim_width, bin_count, sign):
    slices = [
        lax.dynamic_slice_in_dim(padded, rim_width + sign * (tap_index - 1) * dilate, bin_count, 0)
        for tap_index in range(3)
    ]
    return jnp.concatenate(slices, axis=1)


def flip_channels(values, mirror):
    return jnp.dot(values, mirror, preferred_element_type=jnp.float32).astype(jnp.bfloat16)


def spread_back(back_taps, weight, channels):
    result = jnp.zeros((back_taps.shape[0], channels), jnp.float32)
    for tap_index in range(3):
        result = result + lax.dot_general(
            back_taps[:, tap_index * channels : (tap_index + 1) * channels],
            weight[tap_index],
            (((1,), (1,)), ((), ())),
            preferred_element_type=jnp.float32,
        )
    return result


def per_device(
    embeddings,
    norm_gain,
    conv_weight,
    conv_bias,
    dilation,
    donor_bins,
    acceptor_bins,
    junction_count,
    donor_proj,
    acceptor_proj,
    out_cotangent,
    score_cotangent,
):
    bin_count = embeddings.shape[1]
    channels = embeddings.shape[2]
    rim_width = bin_count // 2
    dilate = dilation[0]
    lanes = lax.broadcasted_iota(jnp.int32, (channels, channels), 0)
    mirror = (
        lanes + lax.broadcasted_iota(jnp.int32, (channels, channels), 1) == channels - 1
    ).astype(jnp.bfloat16)

    emb = embeddings[0]
    emb_rev = flip_channels(emb, mirror)
    as_float = emb.astype(jnp.float32)
    inverse = lax.rsqrt(jnp.mean(as_float * as_float, axis=1, keepdims=True) + epsilon)
    normed = as_float * inverse
    normed_rev = emb_rev.astype(jnp.float32) * inverse
    pre_fwd = normed * norm_gain
    pre_rev = normed_rev * norm_gain
    act_fwd = gelu_value(pre_fwd).astype(jnp.bfloat16)
    act_rev = gelu_value(pre_rev).astype(jnp.bfloat16)

    padded = with_halo(jnp.stack([act_fwd, act_rev]), (("seq", 1),), rim_width)
    taps_fwd = tap_stack(padded[0], dilate, rim_width, bin_count, 1)
    taps_rev = tap_stack(padded[1], dilate, rim_width, bin_count, -1)
    conv_all = (
        jnp.dot(
            jnp.concatenate([taps_fwd, taps_rev], axis=0),
            conv_weight.reshape(3 * channels, channels),
            preferred_element_type=jnp.float32,
        )
        + conv_bias
    ).astype(jnp.bfloat16)
    conv_fwd = conv_all[:bin_count]
    conv_rev = flip_channels(conv_all[bin_count:], mirror)
    block_flat = (
        as_float + 0.5 * (conv_fwd.astype(jnp.float32) + conv_rev.astype(jnp.float32))
    ).astype(jnp.bfloat16)

    both_proj = jnp.concatenate([donor_proj, acceptor_proj], axis=1)
    hidden = donor_proj.shape[1]
    local_proj = jnp.dot(block_flat, both_proj, preferred_element_type=jnp.float32).astype(
        jnp.bfloat16
    )
    window_proj = lax.all_gather(local_proj, "seq", axis=0, tiled=True)
    rows_donor = jnp.take(window_proj[:, :hidden], donor_bins[0], axis=0).astype(jnp.float32)
    rows_acceptor = jnp.take(window_proj[:, hidden:], acceptor_bins[0], axis=0).astype(jnp.float32)
    pair_total = donor_bins.shape[1]
    pair_share = pair_total // lax.axis_size("seq")
    pair_first = lax.axis_index("seq") * pair_share
    live_mask = (jnp.arange(pair_total) < junction_count[0]).astype(jnp.float32)
    score_scale = hidden ** (-0.5)
    products = jnp.sum(
        lax.dynamic_slice_in_dim(rows_donor, pair_first, pair_share, 0)
        * lax.dynamic_slice_in_dim(rows_acceptor, pair_first, pair_share, 0),
        axis=1,
    )
    junction_scores = (
        lax.dynamic_slice_in_dim(live_mask, pair_first, pair_share, 0) * products * score_scale
    )[None]
    pair_weight = score_cotangent[0] * live_mask * score_scale
    positions = lax.axis_index("seq") * bin_count + jnp.arange(bin_count)
    pick_donor = (positions[:, None] == donor_bins[0][None, :]).astype(jnp.float32)
    pick_acceptor = (positions[:, None] == acceptor_bins[0][None, :]).astype(jnp.float32)
    grad_donor = jnp.dot(
        pick_donor, pair_weight[:, None] * rows_acceptor, precision=lax.Precision.HIGHEST
    ).astype(jnp.bfloat16)
    grad_acceptor = jnp.dot(
        pick_acceptor, pair_weight[:, None] * rows_donor, precision=lax.Precision.HIGHEST
    ).astype(jnp.bfloat16)
    out_grad = out_cotangent[0].astype(jnp.float32) + lax.dot_general(
        jnp.concatenate([grad_donor, grad_acceptor], axis=1),
        both_proj,
        (((1,), (1,)), ((), ())),
        preferred_element_type=jnp.float32,
    )
    conv_grad = (0.5 * out_grad).astype(jnp.bfloat16)
    padded_back = with_halo(conv_grad[None], (("seq", 1),), rim_width)[0]
    padded_back_rev = flip_channels(padded_back, mirror)
    back_fwd = tap_stack(padded_back, dilate, rim_width, bin_count, -1)
    back_rev = tap_stack(padded_back_rev, dilate, rim_width, bin_count, 1)
    dact_all = spread_back(jnp.concatenate([back_fwd, back_rev], axis=0), conv_weight, channels)
    dact_fwd = dact_all[:bin_count]
    dact_rev = dact_all[bin_count:]
    norm_rev = flip_channels(
        (dact_rev * gelu_slope(pre_rev) * norm_gain).astype(jnp.bfloat16), mirror
    )
    norm_grad = dact_fwd * gelu_slope(pre_fwd) * norm_gain + norm_rev.astype(jnp.float32)
    input_grad = (
        out_grad
        + inverse * (norm_grad - normed * jnp.mean(norm_grad * normed, axis=1, keepdims=True))
    ).astype(jnp.bfloat16)[None]
    grad_rev = lax.slice_in_dim(padded_back_rev, rim_width, rim_width + bin_count, axis=0)
    grad_term = lax.dot_general(
        jnp.concatenate([act_fwd, act_rev], axis=0),
        jnp.concatenate([conv_grad, grad_rev], axis=0),
        (((0,), (0,)), ((), ())),
        preferred_element_type=jnp.float32,
    )
    grad_term = (grad_term / lax.axis_size("win")).reshape(channels * channels)
    weight_grad = lax.psum_scatter(grad_term, ("win", "seq"), scatter_dimension=0, tiled=True)
    return (block_flat[None], junction_scores, input_grad, weight_grad)


def solution(mesh):
    return jax.shard_map(
        per_device,
        mesh=mesh,
        in_specs=(
            P("win", "seq", None),
            P(),
            P(),
            P(),
            P("win"),
            P("win", None),
            P("win", None),
            P("win"),
            P(),
            P(),
            P("win", "seq", None),
            P("win", None),
        ),
        out_specs=(
            P("win", "seq", None),
            P("win", "seq"),
            P("win", "seq", None),
            P(("win", "seq")),
        ),
        check_vma=False,
    )
```

```python
import jax
import jax.numpy as jnp
from jax import lax
from jax.sharding import PartitionSpec as P

epsilon = 1e-06
gelu_scale = 0.7978845608028654
gelu_cubic = 0.044715


def with_halo(block, sides, width):
    for axis, dim in sides:
        count = lax.axis_size(axis)
        forward = [(i, i + 1) for i in range(count - 1)]
        backward = [(target, source) for source, target in forward]
        low = lax.ppermute(
            lax.slice_in_dim(block, block.shape[dim] - width, None, axis=dim), axis, forward
        )
        high = lax.ppermute(lax.slice_in_dim(block, 0, width, axis=dim), axis, backward)
        block = jnp.concatenate([low, block, high], axis=dim)
    return block


def gelu_value(inputs):
    inner = gelu_scale * (inputs + gelu_cubic * inputs * inputs * inputs)
    return 0.5 * inputs * (1.0 + jnp.tanh(inner))


def gelu_slope(inputs):
    inner = gelu_scale * (inputs + gelu_cubic * inputs * inputs * inputs)
    tangent = jnp.tanh(inner)
    return 0.5 * (1.0 + tangent) + 0.5 * inputs * (1.0 - tangent * tangent) * gelu_scale * (
        1.0 + 3.0 * gelu_cubic * inputs * inputs
    )


def tap_stack(padded, dilate, rim_width, bin_count, sign):
    slices = [
        lax.dynamic_slice_in_dim(padded, rim_width + sign * (tap_index - 1) * dilate, bin_count, 0)
        for tap_index in range(3)
    ]
    return jnp.concatenate(slices, axis=1)


def flip_channels(values, mirror):
    return jnp.dot(values, mirror, preferred_element_type=jnp.float32).astype(jnp.bfloat16)


def spread_back(back_taps, weight, channels):
    result = jnp.zeros((back_taps.shape[0], channels), jnp.float32)
    for tap_index in range(3):
        result = result + lax.dot_general(
            back_taps[:, tap_index * channels : (tap_index + 1) * channels],
            weight[tap_index],
            (((1,), (1,)), ((), ())),
            preferred_element_type=jnp.float32,
        )
    return result


def per_device(
    embeddings,
    norm_gain,
    conv_weight,
    conv_bias,
    dilation,
    donor_bins,
    acceptor_bins,
    junction_count,
    donor_proj,
    acceptor_proj,
    out_cotangent,
    score_cotangent,
):
    bin_count = embeddings.shape[1]
    channels = embeddings.shape[2]
    rim_width = bin_count // 2
    dilate = dilation[0]
    lanes = lax.broadcasted_iota(jnp.int32, (channels, channels), 0)
    mirror = (
        lanes + lax.broadcasted_iota(jnp.int32, (channels, channels), 1) == channels - 1
    ).astype(jnp.bfloat16)

    emb = embeddings[0]
    emb_rev = flip_channels(emb, mirror)
    as_float = emb.astype(jnp.float32)
    inverse = lax.rsqrt(jnp.mean(as_float * as_float, axis=1, keepdims=True) + epsilon)
    normed = as_float * inverse
    normed_rev = emb_rev.astype(jnp.float32) * inverse
    pre_fwd = normed * norm_gain
    pre_rev = normed_rev * norm_gain
    act_fwd = gelu_value(pre_fwd).astype(jnp.bfloat16)
    act_rev = gelu_value(pre_rev).astype(jnp.bfloat16)

    padded = with_halo(jnp.stack([act_fwd, act_rev]), (("seq", 1),), rim_width)
    taps_fwd = tap_stack(padded[0], dilate, rim_width, bin_count, 1)
    taps_rev = tap_stack(padded[1], dilate, rim_width, bin_count, -1)
    conv_all = (
        jnp.dot(
            jnp.concatenate([taps_fwd, taps_rev], axis=0),
            conv_weight.reshape(3 * channels, channels),
            preferred_element_type=jnp.float32,
        )
        + conv_bias
    ).astype(jnp.bfloat16)
    conv_fwd = conv_all[:bin_count]
    conv_rev = flip_channels(conv_all[bin_count:], mirror)
    block_flat = (
        as_float + 0.5 * (conv_fwd.astype(jnp.float32) + conv_rev.astype(jnp.float32))
    ).astype(jnp.bfloat16)

    both_proj = jnp.concatenate([donor_proj, acceptor_proj], axis=1)
    hidden = donor_proj.shape[1]
    local_proj = jnp.dot(block_flat, both_proj, preferred_element_type=jnp.float32).astype(
        jnp.bfloat16
    )
    window_proj = lax.all_gather(local_proj, "seq", axis=0, tiled=True)
    rows_donor = jnp.take(window_proj[:, :hidden], donor_bins[0], axis=0).astype(jnp.float32)
    rows_acceptor = jnp.take(window_proj[:, hidden:], acceptor_bins[0], axis=0).astype(jnp.float32)
    pair_total = donor_bins.shape[1]
    pair_share = pair_total // lax.axis_size("seq")
    pair_first = lax.axis_index("seq") * pair_share
    live_mask = (jnp.arange(pair_total) < junction_count[0]).astype(jnp.float32)
    score_scale = hidden ** (-0.5)
    products = jnp.sum(
        lax.dynamic_slice_in_dim(rows_donor, pair_first, pair_share, 0)
        * lax.dynamic_slice_in_dim(rows_acceptor, pair_first, pair_share, 0),
        axis=1,
    )
    junction_scores = (
        lax.dynamic_slice_in_dim(live_mask, pair_first, pair_share, 0) * products * score_scale
    )[None]
    pair_weight = score_cotangent[0] * live_mask * score_scale
    positions = lax.axis_index("seq") * bin_count + jnp.arange(bin_count)
    pick_donor = (positions[:, None] == donor_bins[0][None, :]).astype(jnp.float32)
    pick_acceptor = (positions[:, None] == acceptor_bins[0][None, :]).astype(jnp.float32)
    grad_donor = jnp.dot(
        pick_donor, pair_weight[:, None] * rows_acceptor, precision=lax.Precision.HIGHEST
    ).astype(jnp.bfloat16)
    grad_acceptor = jnp.dot(
        pick_acceptor, pair_weight[:, None] * rows_donor, precision=lax.Precision.HIGHEST
    ).astype(jnp.bfloat16)
    out_grad = out_cotangent[0].astype(jnp.float32) + lax.dot_general(
        jnp.concatenate([grad_donor, grad_acceptor], axis=1),
        both_proj,
        (((1,), (1,)), ((), ())),
        preferred_element_type=jnp.float32,
    )
    conv_grad = (0.5 * out_grad).astype(jnp.bfloat16)
    padded_back = with_halo(conv_grad[None], (("seq", 1),), rim_width)[0]
    padded_back_rev = flip_channels(padded_back, mirror)
    back_fwd = tap_stack(padded_back, dilate, rim_width, bin_count, -1)
    back_rev = tap_stack(padded_back_rev, dilate, rim_width, bin_count, 1)
    dact_all = spread_back(jnp.concatenate([back_fwd, back_rev], axis=0), conv_weight, channels)
    dact_fwd = dact_all[:bin_count]
    dact_rev = dact_all[bin_count:]
    norm_rev = flip_channels(
        (dact_rev * gelu_slope(pre_rev) * norm_gain).astype(jnp.bfloat16), mirror
    )
    norm_grad = dact_fwd * gelu_slope(pre_fwd) * norm_gain + norm_rev.astype(jnp.float32)
    input_grad = (
        out_grad
        + inverse * (norm_grad - normed * jnp.mean(norm_grad * normed, axis=1, keepdims=True))
    ).astype(jnp.bfloat16)[None]
    grad_rev = lax.slice_in_dim(padded_back_rev, rim_width, rim_width + bin_count, axis=0)
    grad_term = lax.dot_general(
        jnp.concatenate([act_fwd, act_rev], axis=0),
        jnp.concatenate([conv_grad, grad_rev], axis=0),
        (((0,), (0,)), ((), ())),
        preferred_element_type=jnp.float32,
    )
    grad_term = grad_term / lax.axis_size("win")
    weight_grad = lax.psum_scatter(grad_term, ("win", "seq"), scatter_dimension=0, tiled=True).reshape(-1)
    return (block_flat[None], junction_scores, input_grad, weight_grad)


def solution(mesh):
    return jax.shard_map(
        per_device,
        mesh=mesh,
        in_specs=(
            P("win", "seq", None),
            P(),
            P(),
            P(),
            P("win"),
            P("win", None),
            P("win", None),
            P("win"),
            P(),
            P(),
            P("win", "seq", None),
            P("win", None),
        ),
        out_specs=(
            P("win", "seq", None),
            P("win", "seq"),
            P("win", "seq", None),
            P(("win", "seq")),
        ),
        check_vma=False,
    )
```

```python
import jax
import jax.numpy as jnp
from jax import lax
from jax.sharding import PartitionSpec as P

epsilon = 1e-06
gelu_scale = 0.7978845608028654
gelu_cubic = 0.044715


def with_halo(block, sides, width):
    for axis, dim in sides:
        count = lax.axis_size(axis)
        forward = [(i, i + 1) for i in range(count - 1)]
        backward = [(target, source) for source, target in forward]
        low = lax.ppermute(
            lax.slice_in_dim(block, block.shape[dim] - width, None, axis=dim), axis, forward
        )
        high = lax.ppermute(lax.slice_in_dim(block, 0, width, axis=dim), axis, backward)
        block = jnp.concatenate([low, block, high], axis=dim)
    return block


def gelu_value(inputs):
    inner = gelu_scale * (inputs + gelu_cubic * inputs * inputs * inputs)
    return 0.5 * inputs * (1.0 + jnp.tanh(inner))


def gelu_slope(inputs):
    inner = gelu_scale * (inputs + gelu_cubic * inputs * inputs * inputs)
    tangent = jnp.tanh(inner)
    return 0.5 * (1.0 + tangent) + 0.5 * inputs * (1.0 - tangent * tangent) * gelu_scale * (
        1.0 + 3.0 * gelu_cubic * inputs * inputs
    )


def tap_stack(padded, dilate, rim_width, bin_count, sign):
    slices = [
        lax.dynamic_slice_in_dim(padded, rim_width + sign * (tap_index - 1) * dilate, bin_count, 0)
        for tap_index in range(3)
    ]
    return jnp.concatenate(slices, axis=1)


def flip_channels(values, mirror):
    return jnp.dot(values, mirror, preferred_element_type=jnp.float32).astype(jnp.bfloat16)


def spread_back(back_taps, weight, channels):
    result = jnp.zeros((back_taps.shape[0], channels), jnp.float32)
    for tap_index in range(3):
        result = result + lax.dot_general(
            back_taps[:, tap_index * channels : (tap_index + 1) * channels],
            weight[tap_index],
            (((1,), (1,)), ((), ())),
            preferred_element_type=jnp.float32,
        )
    return result


def halve_sum(blocks, axis):
    size = lax.axis_size(axis)
    if size & (size - 1):
        flat = blocks.reshape((-1,) + blocks.shape[2:])
        return lax.psum_scatter(flat, axis, scatter_dimension=0, tiled=True).reshape(blocks.shape[1:])
    me = lax.axis_index(axis)
    bit = 1
    while bit < size:
        blocks = blocks.reshape((blocks.shape[0] // 2, 2) + blocks.shape[1:])
        mine = (me // bit) % 2
        keep = lax.dynamic_index_in_dim(blocks, mine, 1, keepdims=False)
        send = lax.dynamic_index_in_dim(blocks, 1 - mine, 1, keepdims=False)
        pairs = [(i, i ^ bit) for i in range(size)]
        blocks = keep + lax.ppermute(send, axis, pairs)
        bit *= 2
    return blocks[0]


def gather_rows(block, axis):
    size = lax.axis_size(axis)
    me = lax.axis_index(axis)
    whole = jnp.zeros((size,) + block.shape, block.dtype)
    whole = lax.dynamic_update_index_in_dim(whole, block, me, 0)
    for shift in range(1, size):
        pairs = [(i, (i + shift) % size) for i in range(size)]
        got = lax.ppermute(block, axis, pairs)
        whole = lax.dynamic_update_index_in_dim(whole, got, (me - shift) % size, 0)
    return whole.reshape((-1,) + block.shape[1:])


def per_device(
    embeddings,
    norm_gain,
    conv_weight,
    conv_bias,
    dilation,
    donor_bins,
    acceptor_bins,
    junction_count,
    donor_proj,
    acceptor_proj,
    out_cotangent,
    score_cotangent,
):
    bin_count = embeddings.shape[1]
    channels = embeddings.shape[2]
    rim_width = bin_count // 2
    dilate = dilation[0]
    lanes = lax.broadcasted_iota(jnp.int32, (channels, channels), 0)
    mirror = (
        lanes + lax.broadcasted_iota(jnp.int32, (channels, channels), 1) == channels - 1
    ).astype(jnp.bfloat16)

    emb = embeddings[0]
    emb_rev = flip_channels(emb, mirror)
    as_float = emb.astype(jnp.float32)
    inverse = lax.rsqrt(jnp.mean(as_float * as_float, axis=1, keepdims=True) + epsilon)
    normed = as_float * inverse
    normed_rev = emb_rev.astype(jnp.float32) * inverse
    pre_fwd = normed * norm_gain
    pre_rev = normed_rev * norm_gain
    act_fwd = gelu_value(pre_fwd).astype(jnp.bfloat16)
    act_rev = gelu_value(pre_rev).astype(jnp.bfloat16)

    padded = with_halo(jnp.stack([act_fwd, act_rev]), (("seq", 1),), rim_width)
    taps_fwd = tap_stack(padded[0], dilate, rim_width, bin_count, 1)
    taps_rev = tap_stack(padded[1], dilate, rim_width, bin_count, -1)
    conv_all = (
        jnp.dot(
            jnp.concatenate([taps_fwd, taps_rev], axis=0),
            conv_weight.reshape(3 * channels, channels),
            preferred_element_type=jnp.float32,
        )
        + conv_bias
    ).astype(jnp.bfloat16)
    conv_fwd = conv_all[:bin_count]
    conv_rev = flip_channels(conv_all[bin_count:], mirror)
    block_flat = (
        as_float + 0.5 * (conv_fwd.astype(jnp.float32) + conv_rev.astype(jnp.float32))
    ).astype(jnp.bfloat16)

    both_proj = jnp.concatenate([donor_proj, acceptor_proj], axis=1)
    hidden = donor_proj.shape[1]
    local_proj = jnp.dot(block_flat, both_proj, preferred_element_type=jnp.float32).astype(
        jnp.bfloat16
    )
    window_proj = gather_rows(local_proj, "seq")
    rows_donor = jnp.take(window_proj[:, :hidden], donor_bins[0], axis=0).astype(jnp.float32)
    rows_acceptor = jnp.take(window_proj[:, hidden:], acceptor_bins[0], axis=0).astype(jnp.float32)
    pair_total = donor_bins.shape[1]
    pair_share = pair_total // lax.axis_size("seq")
    pair_first = lax.axis_index("seq") * pair_share
    live_mask = (jnp.arange(pair_total) < junction_count[0]).astype(jnp.float32)
    score_scale = hidden ** (-0.5)
    products = jnp.sum(
        lax.dynamic_slice_in_dim(rows_donor, pair_first, pair_share, 0)
        * lax.dynamic_slice_in_dim(rows_acceptor, pair_first, pair_share, 0),
        axis=1,
    )
    junction_scores = (
        lax.dynamic_slice_in_dim(live_mask, pair_first, pair_share, 0) * products * score_scale
    )[None]
    pair_weight = score_cotangent[0] * live_mask * score_scale
    positions = lax.axis_index("seq") * bin_count + jnp.arange(bin_count)
    pick_donor = (positions[:, None] == donor_bins[0][None, :]).astype(jnp.float32)
    pick_acceptor = (positions[:, None] == acceptor_bins[0][None, :]).astype(jnp.float32)
    grad_donor = jnp.dot(
        pick_donor, pair_weight[:, None] * rows_acceptor, precision=lax.Precision.HIGHEST
    ).astype(jnp.bfloat16)
    grad_acceptor = jnp.dot(
        pick_acceptor, pair_weight[:, None] * rows_donor, precision=lax.Precision.HIGHEST
    ).astype(jnp.bfloat16)
    out_grad = out_cotangent[0].astype(jnp.float32) + lax.dot_general(
        jnp.concatenate([grad_donor, grad_acceptor], axis=1),
        both_proj,
        (((1,), (1,)), ((), ())),
        preferred_element_type=jnp.float32,
    )
    conv_grad = (0.5 * out_grad).astype(jnp.bfloat16)
    padded_back = with_halo(conv_grad[None], (("seq", 1),), rim_width)[0]
    padded_back_rev = flip_channels(padded_back, mirror)
    back_fwd = tap_stack(padded_back, dilate, rim_width, bin_count, -1)
    back_rev = tap_stack(padded_back_rev, dilate, rim_width, bin_count, 1)
    dact_all = spread_back(jnp.concatenate([back_fwd, back_rev], axis=0), conv_weight, channels)
    dact_fwd = dact_all[:bin_count]
    dact_rev = dact_all[bin_count:]
    norm_rev = flip_channels(
        (dact_rev * gelu_slope(pre_rev) * norm_gain).astype(jnp.bfloat16), mirror
    )
    norm_grad = dact_fwd * gelu_slope(pre_fwd) * norm_gain + norm_rev.astype(jnp.float32)
    input_grad = (
        out_grad
        + inverse * (norm_grad - normed * jnp.mean(norm_grad * normed, axis=1, keepdims=True))
    ).astype(jnp.bfloat16)[None]
    grad_rev = lax.slice_in_dim(padded_back_rev, rim_width, rim_width + bin_count, axis=0)
    grad_term = lax.dot_general(
        jnp.concatenate([act_fwd, act_rev], axis=0),
        jnp.concatenate([conv_grad, grad_rev], axis=0),
        (((0,), (0,)), ((), ())),
        preferred_element_type=jnp.float32,
    )
    win_count = lax.axis_size("win")
    seq_count = lax.axis_size("seq")
    grad_term = (grad_term / win_count).reshape(win_count, seq_count, -1, channels)
    weight_grad = halve_sum(halve_sum(grad_term, "win"), "seq").reshape(-1)
    return (block_flat[None], junction_scores, input_grad, weight_grad)


def solution(mesh):
    return jax.shard_map(
        per_device,
        mesh=mesh,
        in_specs=(
            P("win", "seq", None),
            P(),
            P(),
            P(),
            P("win"),
            P("win", None),
            P("win", None),
            P("win"),
            P(),
            P(),
            P("win", "seq", None),
            P("win", None),
        ),
        out_specs=(
            P("win", "seq", None),
            P("win", "seq"),
            P("win", "seq", None),
            P(("win", "seq")),
        ),
        check_vma=False,
    )
```

```python
import jax
import jax.numpy as jnp
from jax import lax
from jax.sharding import PartitionSpec as P

epsilon = 1e-06
gelu_scale = 0.7978845608028654
gelu_cubic = 0.044715


def with_halo(block, sides, width):
    for axis, dim in sides:
        count = lax.axis_size(axis)
        forward = [(i, i + 1) for i in range(count - 1)]
        backward = [(target, source) for source, target in forward]
        low = lax.ppermute(
            lax.slice_in_dim(block, block.shape[dim] - width, None, axis=dim), axis, forward
        )
        high = lax.ppermute(lax.slice_in_dim(block, 0, width, axis=dim), axis, backward)
        block = jnp.concatenate([low, block, high], axis=dim)
    return block


def gelu_value(inputs):
    inner = gelu_scale * (inputs + gelu_cubic * inputs * inputs * inputs)
    return 0.5 * inputs * (1.0 + jnp.tanh(inner))


def gelu_slope(inputs):
    inner = gelu_scale * (inputs + gelu_cubic * inputs * inputs * inputs)
    tangent = jnp.tanh(inner)
    return 0.5 * (1.0 + tangent) + 0.5 * inputs * (1.0 - tangent * tangent) * gelu_scale * (
        1.0 + 3.0 * gelu_cubic * inputs * inputs
    )


def tap_stack(padded, dilate, rim_width, bin_count, sign):
    slices = [
        lax.dynamic_slice_in_dim(padded, rim_width + sign * (tap_index - 1) * dilate, bin_count, 0)
        for tap_index in range(3)
    ]
    return jnp.concatenate(slices, axis=1)


def flip_channels(values, mirror):
    return jnp.dot(values, mirror, preferred_element_type=jnp.float32).astype(jnp.bfloat16)


def spread_back(back_taps, weight, channels):
    result = jnp.zeros((back_taps.shape[0], channels), jnp.float32)
    for tap_index in range(3):
        result = result + lax.dot_general(
            back_taps[:, tap_index * channels : (tap_index + 1) * channels],
            weight[tap_index],
            (((1,), (1,)), ((), ())),
            preferred_element_type=jnp.float32,
        )
    return result


def halve_sum(blocks, axis):
    size = lax.axis_size(axis)
    if size & (size - 1):
        flat = blocks.reshape((-1,) + blocks.shape[2:])
        return lax.psum_scatter(flat, axis, scatter_dimension=0, tiled=True).reshape(blocks.shape[1:])
    me = lax.axis_index(axis)
    bit = 1
    while bit < size:
        blocks = blocks.reshape((blocks.shape[0] // 2, 2) + blocks.shape[1:])
        mine = (me // bit) % 2
        keep = lax.dynamic_index_in_dim(blocks, mine, 1, keepdims=False)
        send = lax.dynamic_index_in_dim(blocks, 1 - mine, 1, keepdims=False)
        pairs = [(i, i ^ bit) for i in range(size)]
        blocks = keep + lax.ppermute(send, axis, pairs)
        bit *= 2
    return blocks[0]


def scatter_sum(term, channels):
    win_count = lax.axis_size("win")
    seq_count = lax.axis_size("seq")
    blocks = term.reshape(win_count, seq_count, -1, channels)
    rows = blocks.shape[2]
    if (win_count & (win_count - 1)) or (seq_count & (seq_count - 1)) or rows % 3:
        return halve_sum(halve_sum(blocks, "win"), "seq")
    win_bits = [("win", 1 << k) for k in range(win_count.bit_length() - 1)]
    seq_bits = [("seq", 1 << k) for k in range(seq_count.bit_length() - 1)]
    names = [f"{a}{b}" for a, b in reversed(win_bits)] + [f"{a}{b}" for a, b in reversed(seq_bits)]
    shape = [2] * len(names) + [rows // 3, channels]
    parts = blocks.reshape(win_count, seq_count, 3, rows // 3, channels)
    first, middle, last = win_bits[:1], win_bits[1:] + seq_bits[:-1], seq_bits[-1:]
    orders, states = [], []
    for part in range(3):
        turn = part % max(len(middle), 1)
        orders.append(first + middle[turn:] + middle[:turn] + last)
        states.append((parts[:, :, part].reshape(shape), list(names)))
    for step in range(len(orders[0])):
        for part in range(3):
            axis, bit = orders[part][step]
            values, dims = states[part]
            where = dims.index(f"{axis}{bit}")
            mine = (lax.axis_index(axis) // bit) % 2
            keep = lax.dynamic_index_in_dim(values, mine, where, keepdims=False)
            send = lax.dynamic_index_in_dim(values, 1 - mine, where, keepdims=False)
            size = lax.axis_size(axis)
            got = lax.ppermute(send, axis, [(i, i ^ bit) for i in range(size)])
            states[part] = (keep + got, dims[:where] + dims[where + 1 :])
    return jnp.concatenate([values for values, _ in states], axis=0)


def gather_rows(block, axis):
    size = lax.axis_size(axis)
    me = lax.axis_index(axis)
    whole = jnp.zeros((size,) + block.shape, block.dtype)
    whole = lax.dynamic_update_index_in_dim(whole, block, me, 0)
    for shift in range(1, size):
        pairs = [(i, (i + shift) % size) for i in range(size)]
        got = lax.ppermute(block, axis, pairs)
        whole = lax.dynamic_update_index_in_dim(whole, got, (me - shift) % size, 0)
    return whole.reshape((-1,) + block.shape[1:])


def per_device(
    embeddings,
    norm_gain,
    conv_weight,
    conv_bias,
    dilation,
    donor_bins,
    acceptor_bins,
    junction_count,
    donor_proj,
    acceptor_proj,
    out_cotangent,
    score_cotangent,
):
    bin_count = embeddings.shape[1]
    channels = embeddings.shape[2]
    rim_width = bin_count // 2
    dilate = dilation[0]
    lanes = lax.broadcasted_iota(jnp.int32, (channels, channels), 0)
    mirror = (
        lanes + lax.broadcasted_iota(jnp.int32, (channels, channels), 1) == channels - 1
    ).astype(jnp.bfloat16)

    emb = embeddings[0]
    emb_rev = flip_channels(emb, mirror)
    as_float = emb.astype(jnp.float32)
    inverse = lax.rsqrt(jnp.mean(as_float * as_float, axis=1, keepdims=True) + epsilon)
    normed = as_float * inverse
    normed_rev = emb_rev.astype(jnp.float32) * inverse
    pre_fwd = normed * norm_gain
    pre_rev = normed_rev * norm_gain
    act_fwd = gelu_value(pre_fwd).astype(jnp.bfloat16)
    act_rev = gelu_value(pre_rev).astype(jnp.bfloat16)

    padded = with_halo(jnp.stack([act_fwd, act_rev]), (("seq", 1),), rim_width)
    taps_fwd = tap_stack(padded[0], dilate, rim_width, bin_count, 1)
    taps_rev = tap_stack(padded[1], dilate, rim_width, bin_count, -1)
    conv_all = (
        jnp.dot(
            jnp.concatenate([taps_fwd, taps_rev], axis=0),
            conv_weight.reshape(3 * channels, channels),
            preferred_element_type=jnp.float32,
        )
        + conv_bias
    ).astype(jnp.bfloat16)
    conv_fwd = conv_all[:bin_count]
    conv_rev = flip_channels(conv_all[bin_count:], mirror)
    block_flat = (
        as_float + 0.5 * (conv_fwd.astype(jnp.float32) + conv_rev.astype(jnp.float32))
    ).astype(jnp.bfloat16)

    both_proj = jnp.concatenate([donor_proj, acceptor_proj], axis=1)
    hidden = donor_proj.shape[1]
    local_proj = jnp.dot(block_flat, both_proj, preferred_element_type=jnp.float32).astype(
        jnp.bfloat16
    )
    window_proj = gather_rows(local_proj, "seq")
    rows_donor = jnp.take(window_proj[:, :hidden], donor_bins[0], axis=0).astype(jnp.float32)
    rows_acceptor = jnp.take(window_proj[:, hidden:], acceptor_bins[0], axis=0).astype(jnp.float32)
    pair_total = donor_bins.shape[1]
    pair_share = pair_total // lax.axis_size("seq")
    pair_first = lax.axis_index("seq") * pair_share
    live_mask = (jnp.arange(pair_total) < junction_count[0]).astype(jnp.float32)
    score_scale = hidden ** (-0.5)
    products = jnp.sum(
        lax.dynamic_slice_in_dim(rows_donor, pair_first, pair_share, 0)
        * lax.dynamic_slice_in_dim(rows_acceptor, pair_first, pair_share, 0),
        axis=1,
    )
    junction_scores = (
        lax.dynamic_slice_in_dim(live_mask, pair_first, pair_share, 0) * products * score_scale
    )[None]
    pair_weight = score_cotangent[0] * live_mask * score_scale
    positions = lax.axis_index("seq") * bin_count + jnp.arange(bin_count)
    pick_donor = (positions[:, None] == donor_bins[0][None, :]).astype(jnp.float32)
    pick_acceptor = (positions[:, None] == acceptor_bins[0][None, :]).astype(jnp.float32)
    grad_donor = jnp.dot(
        pick_donor, pair_weight[:, None] * rows_acceptor, precision=lax.Precision.HIGHEST
    ).astype(jnp.bfloat16)
    grad_acceptor = jnp.dot(
        pick_acceptor, pair_weight[:, None] * rows_donor, precision=lax.Precision.HIGHEST
    ).astype(jnp.bfloat16)
    out_grad = out_cotangent[0].astype(jnp.float32) + lax.dot_general(
        jnp.concatenate([grad_donor, grad_acceptor], axis=1),
        both_proj,
        (((1,), (1,)), ((), ())),
        preferred_element_type=jnp.float32,
    )
    conv_grad = (0.5 * out_grad).astype(jnp.bfloat16)
    padded_back = with_halo(conv_grad[None], (("seq", 1),), rim_width)[0]
    padded_back_rev = flip_channels(padded_back, mirror)
    back_fwd = tap_stack(padded_back, dilate, rim_width, bin_count, -1)
    back_rev = tap_stack(padded_back_rev, dilate, rim_width, bin_count, 1)
    dact_all = spread_back(jnp.concatenate([back_fwd, back_rev], axis=0), conv_weight, channels)
    dact_fwd = dact_all[:bin_count]
    dact_rev = dact_all[bin_count:]
    norm_rev = flip_channels(
        (dact_rev * gelu_slope(pre_rev) * norm_gain).astype(jnp.bfloat16), mirror
    )
    norm_grad = dact_fwd * gelu_slope(pre_fwd) * norm_gain + norm_rev.astype(jnp.float32)
    input_grad = (
        out_grad
        + inverse * (norm_grad - normed * jnp.mean(norm_grad * normed, axis=1, keepdims=True))
    ).astype(jnp.bfloat16)[None]
    grad_rev = lax.slice_in_dim(padded_back_rev, rim_width, rim_width + bin_count, axis=0)
    grad_term = lax.dot_general(
        jnp.concatenate([act_fwd, act_rev], axis=0),
        jnp.concatenate([conv_grad, grad_rev], axis=0),
        (((0,), (0,)), ((), ())),
        preferred_element_type=jnp.float32,
    )
    grad_term = grad_term / lax.axis_size("win")
    weight_grad = scatter_sum(grad_term, channels).reshape(-1)
    return (block_flat[None], junction_scores, input_grad, weight_grad)


def solution(mesh):
    return jax.shard_map(
        per_device,
        mesh=mesh,
        in_specs=(
            P("win", "seq", None),
            P(),
            P(),
            P(),
            P("win"),
            P("win", None),
            P("win", None),
            P("win"),
            P(),
            P(),
            P("win", "seq", None),
            P("win", None),
        ),
        out_specs=(
            P("win", "seq", None),
            P("win", "seq"),
            P("win", "seq", None),
            P(("win", "seq")),
        ),
        check_vma=False,
    )
```

```python
import jax
import jax.numpy as jnp
from jax import lax
from jax.sharding import PartitionSpec as P

epsilon = 1e-06
gelu_scale = 0.7978845608028654
gelu_cubic = 0.044715


def with_halo(block, sides, width):
    for axis, dim in sides:
        count = lax.axis_size(axis)
        forward = [(i, i + 1) for i in range(count - 1)]
        backward = [(target, source) for source, target in forward]
        low = lax.ppermute(
            lax.slice_in_dim(block, block.shape[dim] - width, None, axis=dim), axis, forward
        )
        high = lax.ppermute(lax.slice_in_dim(block, 0, width, axis=dim), axis, backward)
        block = jnp.concatenate([low, block, high], axis=dim)
    return block


def gelu_value(inputs):
    inner = gelu_scale * (inputs + gelu_cubic * inputs * inputs * inputs)
    return 0.5 * inputs * (1.0 + jnp.tanh(inner))


def gelu_slope(inputs):
    inner = gelu_scale * (inputs + gelu_cubic * inputs * inputs * inputs)
    tangent = jnp.tanh(inner)
    return 0.5 * (1.0 + tangent) + 0.5 * inputs * (1.0 - tangent * tangent) * gelu_scale * (
        1.0 + 3.0 * gelu_cubic * inputs * inputs
    )


def tap_stack(padded, dilate, rim_width, bin_count, sign):
    slices = [
        lax.dynamic_slice_in_dim(padded, rim_width + sign * (tap_index - 1) * dilate, bin_count, 0)
        for tap_index in range(3)
    ]
    return jnp.concatenate(slices, axis=1)


def flip_channels(values, mirror):
    return jnp.dot(values, mirror, preferred_element_type=jnp.float32).astype(jnp.bfloat16)


def spread_back(back_taps, weight, channels):
    result = jnp.zeros((back_taps.shape[0], channels), jnp.float32)
    for tap_index in range(3):
        result = result + lax.dot_general(
            back_taps[:, tap_index * channels : (tap_index + 1) * channels],
            weight[tap_index],
            (((1,), (1,)), ((), ())),
            preferred_element_type=jnp.float32,
        )
    return result


def halve_sum(blocks, axis):
    size = lax.axis_size(axis)
    if size & (size - 1):
        flat = blocks.reshape((-1,) + blocks.shape[2:])
        return lax.psum_scatter(flat, axis, scatter_dimension=0, tiled=True).reshape(blocks.shape[1:])
    me = lax.axis_index(axis)
    bit = 1
    while bit < size:
        blocks = blocks.reshape((blocks.shape[0] // 2, 2) + blocks.shape[1:])
        mine = (me // bit) % 2
        keep = lax.dynamic_index_in_dim(blocks, mine, 1, keepdims=False)
        send = lax.dynamic_index_in_dim(blocks, 1 - mine, 1, keepdims=False)
        pairs = [(i, i ^ bit) for i in range(size)]
        blocks = keep + lax.ppermute(send, axis, pairs)
        bit *= 2
    return blocks[0]


def scatter_sum(term, channels):
    win_count = lax.axis_size("win")
    seq_count = lax.axis_size("seq")
    blocks = term.reshape(win_count, seq_count, -1, channels)
    rows = blocks.shape[2]
    if (win_count & (win_count - 1)) or (seq_count & (seq_count - 1)) or rows % 3:
        return halve_sum(halve_sum(blocks, "win"), "seq")
    win_bits = [("win", 1 << k) for k in range(win_count.bit_length() - 1)]
    seq_bits = [("seq", 1 << k) for k in range(seq_count.bit_length() - 1)]
    names = [f"{a}{b}" for a, b in reversed(win_bits)] + [f"{a}{b}" for a, b in reversed(seq_bits)]
    shape = [2] * len(names) + [rows // 3, channels]
    parts = blocks.reshape(win_count, seq_count, 3, rows // 3, channels)
    first, middle, last = win_bits[:1], win_bits[1:] + seq_bits[:-1], seq_bits[-1:]
    orders, states = [], []
    for part in range(3):
        turn = part % max(len(middle), 1)
        orders.append(first + middle[turn:] + middle[:turn] + last)
        states.append((parts[:, :, part].reshape(shape), list(names)))
    for step in range(len(orders[0])):
        for part in range(3):
            axis, bit = orders[part][step]
            values, dims = states[part]
            where = dims.index(f"{axis}{bit}")
            mine = (lax.axis_index(axis) // bit) % 2
            keep = lax.dynamic_index_in_dim(values, mine, where, keepdims=False)
            send = lax.dynamic_index_in_dim(values, 1 - mine, where, keepdims=False)
            size = lax.axis_size(axis)
            got = lax.ppermute(send, axis, [(i, i ^ bit) for i in range(size)])
            states[part] = (keep + got, dims[:where] + dims[where + 1 :])
    return jnp.concatenate([values for values, _ in states], axis=0)


def gather_rows(block, axis):
    size = lax.axis_size(axis)
    me = lax.axis_index(axis)
    whole = jnp.zeros((size,) + block.shape, block.dtype)
    whole = lax.dynamic_update_index_in_dim(whole, block, me, 0)
    for shift in range(1, size):
        pairs = [(i, (i + shift) % size) for i in range(size)]
        got = lax.ppermute(block, axis, pairs)
        whole = lax.dynamic_update_index_in_dim(whole, got, (me - shift) % size, 0)
    return whole.reshape((-1,) + block.shape[1:])


def per_device(
    embeddings,
    norm_gain,
    conv_weight,
    conv_bias,
    dilation,
    donor_bins,
    acceptor_bins,
    junction_count,
    donor_proj,
    acceptor_proj,
    out_cotangent,
    score_cotangent,
):
    bin_count = embeddings.shape[1]
    channels = embeddings.shape[2]
    rim_width = bin_count // 2
    dilate = dilation[0]
    lanes = lax.broadcasted_iota(jnp.int32, (channels, channels), 0)
    mirror = (
        lanes + lax.broadcasted_iota(jnp.int32, (channels, channels), 1) == channels - 1
    ).astype(jnp.bfloat16)
    own = slice(rim_width, rim_width + bin_count)

    padded_in = with_halo(jnp.stack([embeddings[0], out_cotangent[0]]), (("seq", 1),), rim_width)
    emb = padded_in[0]
    emb_rev = flip_channels(emb, mirror)
    as_float = emb.astype(jnp.float32)
    inverse = lax.rsqrt(jnp.mean(as_float * as_float, axis=1, keepdims=True) + epsilon)
    normed = as_float * inverse
    normed_rev = emb_rev.astype(jnp.float32) * inverse
    pre_fwd = normed * norm_gain
    pre_rev = normed_rev * norm_gain
    act_fwd = gelu_value(pre_fwd).astype(jnp.bfloat16)
    act_rev = gelu_value(pre_rev).astype(jnp.bfloat16)

    taps_fwd = tap_stack(act_fwd, dilate, rim_width, bin_count, 1)
    taps_rev = tap_stack(act_rev, dilate, rim_width, bin_count, -1)
    conv_all = (
        jnp.dot(
            jnp.concatenate([taps_fwd, taps_rev], axis=0),
            conv_weight.reshape(3 * channels, channels),
            preferred_element_type=jnp.float32,
        )
        + conv_bias
    ).astype(jnp.bfloat16)
    conv_fwd = conv_all[:bin_count]
    conv_rev = flip_channels(conv_all[bin_count:], mirror)
    block_flat = (
        as_float[own] + 0.5 * (conv_fwd.astype(jnp.float32) + conv_rev.astype(jnp.float32))
    ).astype(jnp.bfloat16)

    both_proj = jnp.concatenate([donor_proj, acceptor_proj], axis=1)
    hidden = donor_proj.shape[1]
    window_out = gather_rows(block_flat, "seq")
    window_proj = jnp.dot(window_out, both_proj, preferred_element_type=jnp.float32).astype(
        jnp.bfloat16
    )
    rows_donor = jnp.take(window_proj[:, :hidden], donor_bins[0], axis=0).astype(jnp.float32)
    rows_acceptor = jnp.take(window_proj[:, hidden:], acceptor_bins[0], axis=0).astype(jnp.float32)
    pair_total = donor_bins.shape[1]
    pair_share = pair_total // lax.axis_size("seq")
    pair_first = lax.axis_index("seq") * pair_share
    live_mask = (jnp.arange(pair_total) < junction_count[0]).astype(jnp.float32)
    score_scale = hidden ** (-0.5)
    products = jnp.sum(
        lax.dynamic_slice_in_dim(rows_donor, pair_first, pair_share, 0)
        * lax.dynamic_slice_in_dim(rows_acceptor, pair_first, pair_share, 0),
        axis=1,
    )
    junction_scores = (
        lax.dynamic_slice_in_dim(live_mask, pair_first, pair_share, 0) * products * score_scale
    )[None]
    pair_weight = score_cotangent[0] * live_mask * score_scale
    positions = lax.axis_index("seq") * bin_count - rim_width + jnp.arange(emb.shape[0])
    pick_donor = (positions[:, None] == donor_bins[0][None, :]).astype(jnp.float32)
    pick_acceptor = (positions[:, None] == acceptor_bins[0][None, :]).astype(jnp.float32)
    grad_donor = jnp.dot(
        pick_donor, pair_weight[:, None] * rows_acceptor, precision=lax.Precision.HIGHEST
    ).astype(jnp.bfloat16)
    grad_acceptor = jnp.dot(
        pick_acceptor, pair_weight[:, None] * rows_donor, precision=lax.Precision.HIGHEST
    ).astype(jnp.bfloat16)
    out_grad = padded_in[1].astype(jnp.float32) + lax.dot_general(
        jnp.concatenate([grad_donor, grad_acceptor], axis=1),
        both_proj,
        (((1,), (1,)), ((), ())),
        preferred_element_type=jnp.float32,
    )
    conv_grad = (0.5 * out_grad).astype(jnp.bfloat16)
    conv_grad_rev = flip_channels(conv_grad, mirror)
    back_fwd = tap_stack(conv_grad, dilate, rim_width, bin_count, -1)
    back_rev = tap_stack(conv_grad_rev, dilate, rim_width, bin_count, 1)
    dact_all = spread_back(jnp.concatenate([back_fwd, back_rev], axis=0), conv_weight, channels)
    dact_fwd = dact_all[:bin_count]
    dact_rev = dact_all[bin_count:]
    norm_rev = flip_channels(
        (dact_rev * gelu_slope(pre_rev[own]) * norm_gain).astype(jnp.bfloat16), mirror
    )
    norm_grad = dact_fwd * gelu_slope(pre_fwd[own]) * norm_gain + norm_rev.astype(jnp.float32)
    normed_own = normed[own]
    input_grad = (
        out_grad[own]
        + inverse[own]
        * (norm_grad - normed_own * jnp.mean(norm_grad * normed_own, axis=1, keepdims=True))
    ).astype(jnp.bfloat16)[None]
    grad_term = lax.dot_general(
        jnp.concatenate([act_fwd[own], act_rev[own]], axis=0),
        jnp.concatenate([conv_grad[own], conv_grad_rev[own]], axis=0),
        (((0,), (0,)), ((), ())),
        preferred_element_type=jnp.float32,
    )
    grad_term = grad_term / lax.axis_size("win")
    weight_grad = scatter_sum(grad_term, channels).reshape(-1)
    return (block_flat[None], junction_scores, input_grad, weight_grad)


def solution(mesh):
    return jax.shard_map(
        per_device,
        mesh=mesh,
        in_specs=(
            P("win", "seq", None),
            P(),
            P(),
            P(),
            P("win"),
            P("win", None),
            P("win", None),
            P("win"),
            P(),
            P(),
            P("win", "seq", None),
            P("win", None),
        ),
        out_specs=(
            P("win", "seq", None),
            P("win", "seq"),
            P("win", "seq", None),
            P(("win", "seq")),
        ),
        check_vma=False,
    )
```

```python
import jax
import jax.numpy as jnp
from jax import lax
from jax.sharding import PartitionSpec as P

epsilon = 1e-06
gelu_scale = 0.7978845608028654
gelu_cubic = 0.044715


def with_halo(block, sides, width):
    for axis, dim in sides:
        count = lax.axis_size(axis)
        forward = [(i, i + 1) for i in range(count - 1)]
        backward = [(target, source) for source, target in forward]
        low = lax.ppermute(
            lax.slice_in_dim(block, block.shape[dim] - width, None, axis=dim), axis, forward
        )
        high = lax.ppermute(lax.slice_in_dim(block, 0, width, axis=dim), axis, backward)
        block = jnp.concatenate([low, block, high], axis=dim)
    return block


def gelu_value(inputs):
    inner = gelu_scale * (inputs + gelu_cubic * inputs * inputs * inputs)
    return 0.5 * inputs * (1.0 + jnp.tanh(inner))


def gelu_slope(inputs):
    inner = gelu_scale * (inputs + gelu_cubic * inputs * inputs * inputs)
    tangent = jnp.tanh(inner)
    return 0.5 * (1.0 + tangent) + 0.5 * inputs * (1.0 - tangent * tangent) * gelu_scale * (
        1.0 + 3.0 * gelu_cubic * inputs * inputs
    )


def tap_stack(padded, dilate, rim_width, bin_count, sign):
    slices = [
        lax.dynamic_slice_in_dim(padded, rim_width + sign * (tap_index - 1) * dilate, bin_count, 0)
        for tap_index in range(3)
    ]
    return jnp.concatenate(slices, axis=1)


def flip_channels(values, mirror):
    return jnp.dot(values, mirror, preferred_element_type=jnp.float32).astype(jnp.bfloat16)


def spread_back(back_taps, weight, channels):
    result = jnp.zeros((back_taps.shape[0], channels), jnp.float32)
    for tap_index in range(3):
        result = result + lax.dot_general(
            back_taps[:, tap_index * channels : (tap_index + 1) * channels],
            weight[tap_index],
            (((1,), (1,)), ((), ())),
            preferred_element_type=jnp.float32,
        )
    return result


def halve_sum(blocks, axis):
    size = lax.axis_size(axis)
    if size & (size - 1):
        flat = blocks.reshape((-1,) + blocks.shape[2:])
        return lax.psum_scatter(flat, axis, scatter_dimension=0, tiled=True).reshape(blocks.shape[1:])
    me = lax.axis_index(axis)
    bit = 1
    while bit < size:
        blocks = blocks.reshape((blocks.shape[0] // 2, 2) + blocks.shape[1:])
        mine = (me // bit) % 2
        keep = lax.dynamic_index_in_dim(blocks, mine, 1, keepdims=False)
        send = lax.dynamic_index_in_dim(blocks, 1 - mine, 1, keepdims=False)
        pairs = [(i, i ^ bit) for i in range(size)]
        blocks = keep + lax.ppermute(send, axis, pairs)
        bit *= 2
    return blocks[0]


def halve_step(values, dims, axis, bit):
    where = dims.index(f"{axis}{bit}")
    mine = (lax.axis_index(axis) // bit) % 2
    keep = lax.dynamic_index_in_dim(values, mine, where, keepdims=False)
    send = lax.dynamic_index_in_dim(values, 1 - mine, where, keepdims=False)
    size = lax.axis_size(axis)
    got = lax.ppermute(send, axis, [(i, i ^ bit) for i in range(size)])
    return keep + got, dims[:where] + dims[where + 1 :]


def scatter_sum(term, channels):
    win_count = lax.axis_size("win")
    seq_count = lax.axis_size("seq")
    blocks = term.reshape(win_count, seq_count, -1, channels)
    rows = blocks.shape[2]
    if (win_count & (win_count - 1)) or (seq_count & (seq_count - 1)) or rows % 3:
        return halve_sum(halve_sum(blocks, "win"), "seq")
    win_bits = [("win", 1 << k) for k in range(win_count.bit_length() - 1)]
    seq_bits = [("seq", 1 << k) for k in range(seq_count.bit_length() - 1)]
    names = [f"{a}{b}" for a, b in reversed(win_bits)] + [f"{a}{b}" for a, b in reversed(seq_bits)]
    values = blocks.reshape([2] * len(names) + [rows, channels])
    first, middle, last = win_bits[:1], win_bits[1:] + seq_bits[:-1], seq_bits[-1:]
    dims = list(names)
    for axis, bit in first:
        values, dims = halve_step(values, dims, axis, bit)
    lead = len(dims)
    parts = values.reshape(values.shape[:lead] + (3, rows // 3, channels))
    states = [(lax.index_in_dim(parts, part, lead, keepdims=False), list(dims)) for part in range(3)]
    for step in range(len(middle)):
        for part in range(3):
            axis, bit = middle[(step + part) % len(middle)]
            states[part] = halve_step(states[part][0], states[part][1], axis, bit)
    values = jnp.concatenate([part for part, _ in states], axis=-2)
    dims = states[0][1]
    for axis, bit in last:
        values, dims = halve_step(values, dims, axis, bit)
    return values


def gather_rows(block, axis):
    size = lax.axis_size(axis)
    me = lax.axis_index(axis)
    whole = jnp.zeros((size,) + block.shape, block.dtype)
    whole = lax.dynamic_update_index_in_dim(whole, block, me, 0)
    for shift in range(1, size):
        pairs = [(i, (i + shift) % size) for i in range(size)]
        got = lax.ppermute(block, axis, pairs)
        whole = lax.dynamic_update_index_in_dim(whole, got, (me - shift) % size, 0)
    return whole.reshape((-1,) + block.shape[1:])


def per_device(
    embeddings,
    norm_gain,
    conv_weight,
    conv_bias,
    dilation,
    donor_bins,
    acceptor_bins,
    junction_count,
    donor_proj,
    acceptor_proj,
    out_cotangent,
    score_cotangent,
):
    bin_count = embeddings.shape[1]
    channels = embeddings.shape[2]
    rim_width = bin_count // 2
    dilate = dilation[0]
    lanes = lax.broadcasted_iota(jnp.int32, (channels, channels), 0)
    mirror = (
        lanes + lax.broadcasted_iota(jnp.int32, (channels, channels), 1) == channels - 1
    ).astype(jnp.bfloat16)
    own = slice(rim_width, rim_width + bin_count)

    padded_in = with_halo(jnp.stack([embeddings[0], out_cotangent[0]]), (("seq", 1),), rim_width)
    emb = padded_in[0]
    emb_rev = flip_channels(emb, mirror)
    as_float = emb.astype(jnp.float32)
    inverse = lax.rsqrt(jnp.mean(as_float * as_float, axis=1, keepdims=True) + epsilon)
    normed = as_float * inverse
    normed_rev = emb_rev.astype(jnp.float32) * inverse
    pre_fwd = normed * norm_gain
    pre_rev = normed_rev * norm_gain
    act_fwd = gelu_value(pre_fwd).astype(jnp.bfloat16)
    act_rev = gelu_value(pre_rev).astype(jnp.bfloat16)

    taps_fwd = tap_stack(act_fwd, dilate, rim_width, bin_count, 1)
    taps_rev = tap_stack(act_rev, dilate, rim_width, bin_count, -1)
    conv_all = (
        jnp.dot(
            jnp.concatenate([taps_fwd, taps_rev], axis=0),
            conv_weight.reshape(3 * channels, channels),
            preferred_element_type=jnp.float32,
        )
        + conv_bias
    ).astype(jnp.bfloat16)
    conv_fwd = conv_all[:bin_count]
    conv_rev = flip_channels(conv_all[bin_count:], mirror)
    block_flat = (
        as_float[own] + 0.5 * (conv_fwd.astype(jnp.float32) + conv_rev.astype(jnp.float32))
    ).astype(jnp.bfloat16)

    both_proj = jnp.concatenate([donor_proj, acceptor_proj], axis=1)
    hidden = donor_proj.shape[1]
    window_out = gather_rows(block_flat, "seq")
    window_proj = jnp.dot(window_out, both_proj, preferred_element_type=jnp.float32).astype(
        jnp.bfloat16
    )
    rows_donor = jnp.take(window_proj[:, :hidden], donor_bins[0], axis=0).astype(jnp.float32)
    rows_acceptor = jnp.take(window_proj[:, hidden:], acceptor_bins[0], axis=0).astype(jnp.float32)
    pair_total = donor_bins.shape[1]
    pair_share = pair_total // lax.axis_size("seq")
    pair_first = lax.axis_index("seq") * pair_share
    live_mask = (jnp.arange(pair_total) < junction_count[0]).astype(jnp.float32)
    score_scale = hidden ** (-0.5)
    products = jnp.sum(
        lax.dynamic_slice_in_dim(rows_donor, pair_first, pair_share, 0)
        * lax.dynamic_slice_in_dim(rows_acceptor, pair_first, pair_share, 0),
        axis=1,
    )
    junction_scores = (
        lax.dynamic_slice_in_dim(live_mask, pair_first, pair_share, 0) * products * score_scale
    )[None]
    pair_weight = score_cotangent[0] * live_mask * score_scale
    positions = lax.axis_index("seq") * bin_count - rim_width + jnp.arange(emb.shape[0])
    pick_donor = (positions[:, None] == donor_bins[0][None, :]).astype(jnp.float32)
    pick_acceptor = (positions[:, None] == acceptor_bins[0][None, :]).astype(jnp.float32)
    grad_donor = jnp.dot(
        pick_donor, pair_weight[:, None] * rows_acceptor, precision=lax.Precision.HIGHEST
    ).astype(jnp.bfloat16)
    grad_acceptor = jnp.dot(
        pick_acceptor, pair_weight[:, None] * rows_donor, precision=lax.Precision.HIGHEST
    ).astype(jnp.bfloat16)
    out_grad = padded_in[1].astype(jnp.float32) + lax.dot_general(
        jnp.concatenate([grad_donor, grad_acceptor], axis=1),
        both_proj,
        (((1,), (1,)), ((), ())),
        preferred_element_type=jnp.float32,
    )
    conv_grad = (0.5 * out_grad).astype(jnp.bfloat16)
    conv_grad_rev = flip_channels(conv_grad, mirror)
    back_fwd = tap_stack(conv_grad, dilate, rim_width, bin_count, -1)
    back_rev = tap_stack(conv_grad_rev, dilate, rim_width, bin_count, 1)
    dact_all = spread_back(jnp.concatenate([back_fwd, back_rev], axis=0), conv_weight, channels)
    dact_fwd = dact_all[:bin_count]
    dact_rev = dact_all[bin_count:]
    norm_rev = flip_channels(
        (dact_rev * gelu_slope(pre_rev[own]) * norm_gain).astype(jnp.bfloat16), mirror
    )
    norm_grad = dact_fwd * gelu_slope(pre_fwd[own]) * norm_gain + norm_rev.astype(jnp.float32)
    normed_own = normed[own]
    input_grad = (
        out_grad[own]
        + inverse[own]
        * (norm_grad - normed_own * jnp.mean(norm_grad * normed_own, axis=1, keepdims=True))
    ).astype(jnp.bfloat16)[None]
    grad_term = lax.dot_general(
        jnp.concatenate([act_fwd[own], act_rev[own]], axis=0),
        jnp.concatenate([conv_grad[own], conv_grad_rev[own]], axis=0),
        (((0,), (0,)), ((), ())),
        preferred_element_type=jnp.float32,
    )
    grad_term = grad_term / lax.axis_size("win")
    weight_grad = scatter_sum(grad_term, channels).reshape(-1)
    return (block_flat[None], junction_scores, input_grad, weight_grad)


def solution(mesh):
    return jax.shard_map(
        per_device,
        mesh=mesh,
        in_specs=(
            P("win", "seq", None),
            P(),
            P(),
            P(),
            P("win"),
            P("win", None),
            P("win", None),
            P("win"),
            P(),
            P(),
            P("win", "seq", None),
            P("win", None),
        ),
        out_specs=(
            P("win", "seq", None),
            P("win", "seq"),
            P("win", "seq", None),
            P(("win", "seq")),
        ),
        check_vma=False,
    )
```

```python
import jax
import jax.numpy as jnp
from jax import lax
from jax.sharding import PartitionSpec as P

epsilon = 1e-06
gelu_scale = 0.7978845608028654
gelu_cubic = 0.044715


def with_halo(block, sides, width):
    for axis, dim in sides:
        count = lax.axis_size(axis)
        forward = [(i, i + 1) for i in range(count - 1)]
        backward = [(target, source) for source, target in forward]
        low = lax.ppermute(
            lax.slice_in_dim(block, block.shape[dim] - width, None, axis=dim), axis, forward
        )
        high = lax.ppermute(lax.slice_in_dim(block, 0, width, axis=dim), axis, backward)
        block = jnp.concatenate([low, block, high], axis=dim)
    return block


def gelu_value(inputs):
    inner = gelu_scale * (inputs + gelu_cubic * inputs * inputs * inputs)
    return 0.5 * inputs * (1.0 + jnp.tanh(inner))


def gelu_slope(inputs):
    inner = gelu_scale * (inputs + gelu_cubic * inputs * inputs * inputs)
    tangent = jnp.tanh(inner)
    return 0.5 * (1.0 + tangent) + 0.5 * inputs * (1.0 - tangent * tangent) * gelu_scale * (
        1.0 + 3.0 * gelu_cubic * inputs * inputs
    )


def tap_stack(padded, dilate, rim_width, bin_count, sign):
    slices = [
        lax.dynamic_slice_in_dim(padded, rim_width + sign * (tap_index - 1) * dilate, bin_count, 0)
        for tap_index in range(3)
    ]
    return jnp.concatenate(slices, axis=1)


def flip_channels(values, mirror):
    return jnp.dot(values, mirror, preferred_element_type=jnp.float32).astype(jnp.bfloat16)


def spread_back(back_taps, weight, channels):
    result = jnp.zeros((back_taps.shape[0], channels), jnp.float32)
    for tap_index in range(3):
        result = result + lax.dot_general(
            back_taps[:, tap_index * channels : (tap_index + 1) * channels],
            weight[tap_index],
            (((1,), (1,)), ((), ())),
            preferred_element_type=jnp.float32,
        )
    return result


def halve_sum(blocks, axis):
    size = lax.axis_size(axis)
    if size & (size - 1):
        flat = blocks.reshape((-1,) + blocks.shape[2:])
        return lax.psum_scatter(flat, axis, scatter_dimension=0, tiled=True).reshape(blocks.shape[1:])
    me = lax.axis_index(axis)
    bit = 1
    while bit < size:
        blocks = blocks.reshape((blocks.shape[0] // 2, 2) + blocks.shape[1:])
        mine = (me // bit) % 2
        keep = lax.dynamic_index_in_dim(blocks, mine, 1, keepdims=False)
        send = lax.dynamic_index_in_dim(blocks, 1 - mine, 1, keepdims=False)
        pairs = [(i, i ^ bit) for i in range(size)]
        blocks = keep + lax.ppermute(send, axis, pairs)
        bit *= 2
    return blocks[0]


def halve_step(values, dims, axis, bit):
    where = dims.index(f"{axis}{bit}")
    mine = (lax.axis_index(axis) // bit) % 2
    keep = lax.dynamic_index_in_dim(values, mine, where, keepdims=False)
    send = lax.dynamic_index_in_dim(values, 1 - mine, where, keepdims=False)
    size = lax.axis_size(axis)
    got = lax.ppermute(send, axis, [(i, i ^ bit) for i in range(size)])
    return keep + got, dims[:where] + dims[where + 1 :]


def scatter_sum(term, channels):
    win_count = lax.axis_size("win")
    seq_count = lax.axis_size("seq")
    blocks = term.reshape(win_count, seq_count, -1, channels)
    rows = blocks.shape[2]
    if (win_count & (win_count - 1)) or (seq_count & (seq_count - 1)) or rows % 2:
        return halve_sum(halve_sum(blocks, "win"), "seq")
    win_bits = [("win", 1 << k) for k in range(win_count.bit_length() - 1)]
    seq_bits = [("seq", 1 << k) for k in range(seq_count.bit_length() - 1)]
    names = [f"{a}{b}" for a, b in reversed(win_bits)] + [f"{a}{b}" for a, b in reversed(seq_bits)]
    values = blocks.reshape([2] * len(names) + [rows, channels])
    first, middle, last = win_bits[:1], win_bits[1:], seq_bits
    ways = 2 if len(middle) >= 2 else 1
    dims = list(names)
    for axis, bit in first:
        values, dims = halve_step(values, dims, axis, bit)
    lead = len(dims)
    parts = values.reshape(values.shape[:lead] + (ways, rows // ways, channels))
    states = [(lax.index_in_dim(parts, part, lead, keepdims=False), list(dims)) for part in range(ways)]
    for step in range(len(middle)):
        for part in range(ways):
            axis, bit = middle[(step + part) % len(middle)]
            states[part] = halve_step(states[part][0], states[part][1], axis, bit)
    values = jnp.concatenate([part for part, _ in states], axis=-2)
    dims = states[0][1]
    for axis, bit in last:
        values, dims = halve_step(values, dims, axis, bit)
    return values


def gather_rows(block, axis):
    size = lax.axis_size(axis)
    me = lax.axis_index(axis)
    whole = jnp.zeros((size,) + block.shape, block.dtype)
    whole = lax.dynamic_update_index_in_dim(whole, block, me, 0)
    for shift in range(1, size):
        pairs = [(i, (i + shift) % size) for i in range(size)]
        got = lax.ppermute(block, axis, pairs)
        whole = lax.dynamic_update_index_in_dim(whole, got, (me - shift) % size, 0)
    return whole.reshape((-1,) + block.shape[1:])


def per_device(
    embeddings,
    norm_gain,
    conv_weight,
    conv_bias,
    dilation,
    donor_bins,
    acceptor_bins,
    junction_count,
    donor_proj,
    acceptor_proj,
    out_cotangent,
    score_cotangent,
):
    bin_count = embeddings.shape[1]
    channels = embeddings.shape[2]
    rim_width = bin_count // 2
    dilate = dilation[0]
    lanes = lax.broadcasted_iota(jnp.int32, (channels, channels), 0)
    mirror = (
        lanes + lax.broadcasted_iota(jnp.int32, (channels, channels), 1) == channels - 1
    ).astype(jnp.bfloat16)
    own = slice(rim_width, rim_width + bin_count)

    padded_in = with_halo(jnp.stack([embeddings[0], out_cotangent[0]]), (("seq", 1),), rim_width)
    emb = padded_in[0]
    emb_rev = flip_channels(emb, mirror)
    as_float = emb.astype(jnp.float32)
    inverse = lax.rsqrt(jnp.mean(as_float * as_float, axis=1, keepdims=True) + epsilon)
    normed = as_float * inverse
    normed_rev = emb_rev.astype(jnp.float32) * inverse
    pre_fwd = normed * norm_gain
    pre_rev = normed_rev * norm_gain
    act_fwd = gelu_value(pre_fwd).astype(jnp.bfloat16)
    act_rev = gelu_value(pre_rev).astype(jnp.bfloat16)

    taps_fwd = tap_stack(act_fwd, dilate, rim_width, bin_count, 1)
    taps_rev = tap_stack(act_rev, dilate, rim_width, bin_count, -1)
    conv_all = (
        jnp.dot(
            jnp.concatenate([taps_fwd, taps_rev], axis=0),
            conv_weight.reshape(3 * channels, channels),
            preferred_element_type=jnp.float32,
        )
        + conv_bias
    ).astype(jnp.bfloat16)
    conv_fwd = conv_all[:bin_count]
    conv_rev = flip_channels(conv_all[bin_count:], mirror)
    block_flat = (
        as_float[own] + 0.5 * (conv_fwd.astype(jnp.float32) + conv_rev.astype(jnp.float32))
    ).astype(jnp.bfloat16)

    both_proj = jnp.concatenate([donor_proj, acceptor_proj], axis=1)
    hidden = donor_proj.shape[1]
    window_out = gather_rows(block_flat, "seq")
    window_proj = jnp.dot(window_out, both_proj, preferred_element_type=jnp.float32).astype(
        jnp.bfloat16
    )
    rows_donor = jnp.take(window_proj[:, :hidden], donor_bins[0], axis=0).astype(jnp.float32)
    rows_acceptor = jnp.take(window_proj[:, hidden:], acceptor_bins[0], axis=0).astype(jnp.float32)
    pair_total = donor_bins.shape[1]
    pair_share = pair_total // lax.axis_size("seq")
    pair_first = lax.axis_index("seq") * pair_share
    live_mask = (jnp.arange(pair_total) < junction_count[0]).astype(jnp.float32)
    score_scale = hidden ** (-0.5)
    products = jnp.sum(
        lax.dynamic_slice_in_dim(rows_donor, pair_first, pair_share, 0)
        * lax.dynamic_slice_in_dim(rows_acceptor, pair_first, pair_share, 0),
        axis=1,
    )
    junction_scores = (
        lax.dynamic_slice_in_dim(live_mask, pair_first, pair_share, 0) * products * score_scale
    )[None]
    pair_weight = score_cotangent[0] * live_mask * score_scale
    positions = lax.axis_index("seq") * bin_count - rim_width + jnp.arange(emb.shape[0])
    pick_donor = (positions[:, None] == donor_bins[0][None, :]).astype(jnp.float32)
    pick_acceptor = (positions[:, None] == acceptor_bins[0][None, :]).astype(jnp.float32)
    grad_donor = jnp.dot(
        pick_donor, pair_weight[:, None] * rows_acceptor, precision=lax.Precision.HIGHEST
    ).astype(jnp.bfloat16)
    grad_acceptor = jnp.dot(
        pick_acceptor, pair_weight[:, None] * rows_donor, precision=lax.Precision.HIGHEST
    ).astype(jnp.bfloat16)
    out_grad = padded_in[1].astype(jnp.float32) + lax.dot_general(
        jnp.concatenate([grad_donor, grad_acceptor], axis=1),
        both_proj,
        (((1,), (1,)), ((), ())),
        preferred_element_type=jnp.float32,
    )
    conv_grad = (0.5 * out_grad).astype(jnp.bfloat16)
    conv_grad_rev = flip_channels(conv_grad, mirror)
    back_fwd = tap_stack(conv_grad, dilate, rim_width, bin_count, -1)
    back_rev = tap_stack(conv_grad_rev, dilate, rim_width, bin_count, 1)
    dact_all = spread_back(jnp.concatenate([back_fwd, back_rev], axis=0), conv_weight, channels)
    dact_fwd = dact_all[:bin_count]
    dact_rev = dact_all[bin_count:]
    norm_rev = flip_channels(
        (dact_rev * gelu_slope(pre_rev[own]) * norm_gain).astype(jnp.bfloat16), mirror
    )
    norm_grad = dact_fwd * gelu_slope(pre_fwd[own]) * norm_gain + norm_rev.astype(jnp.float32)
    normed_own = normed[own]
    input_grad = (
        out_grad[own]
        + inverse[own]
        * (norm_grad - normed_own * jnp.mean(norm_grad * normed_own, axis=1, keepdims=True))
    ).astype(jnp.bfloat16)[None]
    grad_term = lax.dot_general(
        jnp.concatenate([act_fwd[own], act_rev[own]], axis=0),
        jnp.concatenate([conv_grad[own], conv_grad_rev[own]], axis=0),
        (((0,), (0,)), ((), ())),
        preferred_element_type=jnp.float32,
    )
    grad_term = grad_term / lax.axis_size("win")
    weight_grad = scatter_sum(grad_term, channels).reshape(-1)
    return (block_flat[None], junction_scores, input_grad, weight_grad)


def solution(mesh):
    return jax.shard_map(
        per_device,
        mesh=mesh,
        in_specs=(
            P("win", "seq", None),
            P(),
            P(),
            P(),
            P("win"),
            P("win", None),
            P("win", None),
            P("win"),
            P(),
            P(),
            P("win", "seq", None),
            P("win", None),
        ),
        out_specs=(
            P("win", "seq", None),
            P("win", "seq"),
            P("win", "seq", None),
            P(("win", "seq")),
        ),
        check_vma=False,
    )
```

```python
import jax
import jax.numpy as jnp
from jax import lax
from jax.sharding import PartitionSpec as P

epsilon = 1e-06
gelu_scale = 0.7978845608028654
gelu_cubic = 0.044715


def with_halo(block, sides, width):
    for axis, dim in sides:
        count = lax.axis_size(axis)
        forward = [(i, i + 1) for i in range(count - 1)]
        backward = [(target, source) for source, target in forward]
        low = lax.ppermute(
            lax.slice_in_dim(block, block.shape[dim] - width, None, axis=dim), axis, forward
        )
        high = lax.ppermute(lax.slice_in_dim(block, 0, width, axis=dim), axis, backward)
        block = jnp.concatenate([low, block, high], axis=dim)
    return block


def halo_rows(block, axis, width):
    count = lax.axis_size(axis)
    forward = [(i, i + 1) for i in range(count - 1)]
    backward = [(target, source) for source, target in forward]
    low = lax.ppermute(lax.slice_in_dim(block, block.shape[1] - width, None, axis=1), axis, forward)
    high = lax.ppermute(lax.slice_in_dim(block, 0, width, axis=1), axis, backward)
    return low, high


def gelu_value(inputs):
    inner = gelu_scale * (inputs + gelu_cubic * inputs * inputs * inputs)
    return 0.5 * inputs * (1.0 + jnp.tanh(inner))


def gelu_slope(inputs):
    inner = gelu_scale * (inputs + gelu_cubic * inputs * inputs * inputs)
    tangent = jnp.tanh(inner)
    return 0.5 * (1.0 + tangent) + 0.5 * inputs * (1.0 - tangent * tangent) * gelu_scale * (
        1.0 + 3.0 * gelu_cubic * inputs * inputs
    )


def forward_rows(emb, mirror, norm_gain):
    emb_rev = flip_channels(emb, mirror)
    as_float = emb.astype(jnp.float32)
    inverse = lax.rsqrt(jnp.mean(as_float * as_float, axis=1, keepdims=True) + epsilon)
    normed = as_float * inverse
    normed_rev = emb_rev.astype(jnp.float32) * inverse
    pre_fwd = normed * norm_gain
    pre_rev = normed_rev * norm_gain
    act_fwd = gelu_value(pre_fwd).astype(jnp.bfloat16)
    act_rev = gelu_value(pre_rev).astype(jnp.bfloat16)
    return as_float, inverse, normed, pre_fwd, pre_rev, act_fwd, act_rev


def tap_stack(padded, dilate, rim_width, bin_count, sign):
    slices = [
        lax.dynamic_slice_in_dim(padded, rim_width + sign * (tap_index - 1) * dilate, bin_count, 0)
        for tap_index in range(3)
    ]
    return jnp.concatenate(slices, axis=1)


def flip_channels(values, mirror):
    return jnp.dot(values, mirror, preferred_element_type=jnp.float32).astype(jnp.bfloat16)


def spread_back(back_taps, weight, channels):
    result = jnp.zeros((back_taps.shape[0], channels), jnp.float32)
    for tap_index in range(3):
        result = result + lax.dot_general(
            back_taps[:, tap_index * channels : (tap_index + 1) * channels],
            weight[tap_index],
            (((1,), (1,)), ((), ())),
            preferred_element_type=jnp.float32,
        )
    return result


def halve_sum(blocks, axis):
    size = lax.axis_size(axis)
    if size & (size - 1):
        flat = blocks.reshape((-1,) + blocks.shape[2:])
        return lax.psum_scatter(flat, axis, scatter_dimension=0, tiled=True).reshape(blocks.shape[1:])
    me = lax.axis_index(axis)
    bit = 1
    while bit < size:
        blocks = blocks.reshape((blocks.shape[0] // 2, 2) + blocks.shape[1:])
        mine = (me // bit) % 2
        keep = lax.dynamic_index_in_dim(blocks, mine, 1, keepdims=False)
        send = lax.dynamic_index_in_dim(blocks, 1 - mine, 1, keepdims=False)
        pairs = [(i, i ^ bit) for i in range(size)]
        blocks = keep + lax.ppermute(send, axis, pairs)
        bit *= 2
    return blocks[0]


def halve_step(values, dims, axis, bit):
    where = dims.index(f"{axis}{bit}")
    mine = (lax.axis_index(axis) // bit) % 2
    keep = lax.dynamic_index_in_dim(values, mine, where, keepdims=False)
    send = lax.dynamic_index_in_dim(values, 1 - mine, where, keepdims=False)
    size = lax.axis_size(axis)
    got = lax.ppermute(send, axis, [(i, i ^ bit) for i in range(size)])
    return keep + got, dims[:where] + dims[where + 1 :]


def scatter_sum(term, channels):
    win_count = lax.axis_size("win")
    seq_count = lax.axis_size("seq")
    blocks = term.reshape(win_count, seq_count, -1, channels)
    rows = blocks.shape[2]
    if (win_count & (win_count - 1)) or (seq_count & (seq_count - 1)) or rows % 2:
        return halve_sum(halve_sum(blocks, "win"), "seq")
    win_bits = [("win", 1 << k) for k in range(win_count.bit_length() - 1)]
    seq_bits = [("seq", 1 << k) for k in range(seq_count.bit_length() - 1)]
    names = [f"{a}{b}" for a, b in reversed(win_bits)] + [f"{a}{b}" for a, b in reversed(seq_bits)]
    values = blocks.reshape([2] * len(names) + [rows, channels])
    first, middle, last = win_bits[:1], win_bits[1:], seq_bits
    ways = 2 if len(middle) >= 2 else 1
    dims = list(names)
    for axis, bit in first:
        values, dims = halve_step(values, dims, axis, bit)
    lead = len(dims)
    parts = values.reshape(values.shape[:lead] + (ways, rows // ways, channels))
    states = [(lax.index_in_dim(parts, part, lead, keepdims=False), list(dims)) for part in range(ways)]
    for step in range(len(middle)):
        for part in range(ways):
            axis, bit = middle[(step + part) % len(middle)]
            states[part] = halve_step(states[part][0], states[part][1], axis, bit)
    values = jnp.concatenate([part for part, _ in states], axis=-2)
    dims = states[0][1]
    for axis, bit in last:
        values, dims = halve_step(values, dims, axis, bit)
    return values


def gather_rows(block, axis):
    size = lax.axis_size(axis)
    me = lax.axis_index(axis)
    whole = jnp.zeros((size,) + block.shape, block.dtype)
    whole = lax.dynamic_update_index_in_dim(whole, block, me, 0)
    for shift in range(1, size):
        pairs = [(i, (i + shift) % size) for i in range(size)]
        got = lax.ppermute(block, axis, pairs)
        whole = lax.dynamic_update_index_in_dim(whole, got, (me - shift) % size, 0)
    return whole.reshape((-1,) + block.shape[1:])


def per_device(
    embeddings,
    norm_gain,
    conv_weight,
    conv_bias,
    dilation,
    donor_bins,
    acceptor_bins,
    junction_count,
    donor_proj,
    acceptor_proj,
    out_cotangent,
    score_cotangent,
):
    bin_count = embeddings.shape[1]
    channels = embeddings.shape[2]
    rim_width = bin_count // 2
    dilate = dilation[0]
    lanes = lax.broadcasted_iota(jnp.int32, (channels, channels), 0)
    mirror = (
        lanes + lax.broadcasted_iota(jnp.int32, (channels, channels), 1) == channels - 1
    ).astype(jnp.bfloat16)
    own = slice(rim_width, rim_width + bin_count)

    low, high = halo_rows(jnp.stack([embeddings[0], out_cotangent[0]]), "seq", rim_width)
    as_float, inverse, normed, pre_fwd, pre_rev, own_fwd, own_rev = forward_rows(
        embeddings[0], mirror, norm_gain
    )
    rim_acts = forward_rows(jnp.concatenate([low[0], high[0]]), mirror, norm_gain)
    act_fwd = jnp.concatenate([rim_acts[5][:rim_width], own_fwd, rim_acts[5][rim_width:]])
    act_rev = jnp.concatenate([rim_acts[6][:rim_width], own_rev, rim_acts[6][rim_width:]])
    cot_pad = jnp.concatenate([low[1], out_cotangent[0], high[1]])

    taps_fwd = tap_stack(act_fwd, dilate, rim_width, bin_count, 1)
    taps_rev = tap_stack(act_rev, dilate, rim_width, bin_count, -1)
    conv_all = (
        jnp.dot(
            jnp.concatenate([taps_fwd, taps_rev], axis=0),
            conv_weight.reshape(3 * channels, channels),
            preferred_element_type=jnp.float32,
        )
        + conv_bias
    ).astype(jnp.bfloat16)
    conv_fwd = conv_all[:bin_count]
    conv_rev = flip_channels(conv_all[bin_count:], mirror)
    block_flat = (
        as_float + 0.5 * (conv_fwd.astype(jnp.float32) + conv_rev.astype(jnp.float32))
    ).astype(jnp.bfloat16)

    both_proj = jnp.concatenate([donor_proj, acceptor_proj], axis=1)
    hidden = donor_proj.shape[1]
    window_out = gather_rows(block_flat, "seq")
    window_proj = jnp.dot(window_out, both_proj, preferred_element_type=jnp.float32).astype(
        jnp.bfloat16
    )
    rows_donor = jnp.take(window_proj[:, :hidden], donor_bins[0], axis=0).astype(jnp.float32)
    rows_acceptor = jnp.take(window_proj[:, hidden:], acceptor_bins[0], axis=0).astype(jnp.float32)
    pair_total = donor_bins.shape[1]
    pair_share = pair_total // lax.axis_size("seq")
    pair_first = lax.axis_index("seq") * pair_share
    live_mask = (jnp.arange(pair_total) < junction_count[0]).astype(jnp.float32)
    score_scale = hidden ** (-0.5)
    products = jnp.sum(
        lax.dynamic_slice_in_dim(rows_donor, pair_first, pair_share, 0)
        * lax.dynamic_slice_in_dim(rows_acceptor, pair_first, pair_share, 0),
        axis=1,
    )
    junction_scores = (
        lax.dynamic_slice_in_dim(live_mask, pair_first, pair_share, 0) * products * score_scale
    )[None]
    pair_weight = score_cotangent[0] * live_mask * score_scale
    positions = lax.axis_index("seq") * bin_count - rim_width + jnp.arange(cot_pad.shape[0])
    pick_donor = (positions[:, None] == donor_bins[0][None, :]).astype(jnp.float32)
    pick_acceptor = (positions[:, None] == acceptor_bins[0][None, :]).astype(jnp.float32)
    grad_donor = jnp.dot(
        pick_donor, pair_weight[:, None] * rows_acceptor, precision=lax.Precision.HIGHEST
    ).astype(jnp.bfloat16)
    grad_acceptor = jnp.dot(
        pick_acceptor, pair_weight[:, None] * rows_donor, precision=lax.Precision.HIGHEST
    ).astype(jnp.bfloat16)
    out_grad = cot_pad.astype(jnp.float32) + lax.dot_general(
        jnp.concatenate([grad_donor, grad_acceptor], axis=1),
        both_proj,
        (((1,), (1,)), ((), ())),
        preferred_element_type=jnp.float32,
    )
    conv_grad = (0.5 * out_grad).astype(jnp.bfloat16)
    conv_grad_rev = flip_channels(conv_grad, mirror)
    back_fwd = tap_stack(conv_grad, dilate, rim_width, bin_count, -1)
    back_rev = tap_stack(conv_grad_rev, dilate, rim_width, bin_count, 1)
    dact_all = spread_back(jnp.concatenate([back_fwd, back_rev], axis=0), conv_weight, channels)
    dact_fwd = dact_all[:bin_count]
    dact_rev = dact_all[bin_count:]
    norm_rev = flip_channels(
        (dact_rev * gelu_slope(pre_rev) * norm_gain).astype(jnp.bfloat16), mirror
    )
    norm_grad = dact_fwd * gelu_slope(pre_fwd) * norm_gain + norm_rev.astype(jnp.float32)
    input_grad = (
        out_grad[own]
        + inverse
        * (norm_grad - normed * jnp.mean(norm_grad * normed, axis=1, keepdims=True))
    ).astype(jnp.bfloat16)[None]
    grad_term = lax.dot_general(
        jnp.concatenate([own_fwd, own_rev], axis=0),
        jnp.concatenate([conv_grad[own], conv_grad_rev[own]], axis=0),
        (((0,), (0,)), ((), ())),
        preferred_element_type=jnp.float32,
    )
    grad_term = grad_term / lax.axis_size("win")
    weight_grad = scatter_sum(grad_term, channels).reshape(-1)
    return (block_flat[None], junction_scores, input_grad, weight_grad)


def solution(mesh):
    return jax.shard_map(
        per_device,
        mesh=mesh,
        in_specs=(
            P("win", "seq", None),
            P(),
            P(),
            P(),
            P("win"),
            P("win", None),
            P("win", None),
            P("win"),
            P(),
            P(),
            P("win", "seq", None),
            P("win", None),
        ),
        out_specs=(
            P("win", "seq", None),
            P("win", "seq"),
            P("win", "seq", None),
            P(("win", "seq")),
        ),
        check_vma=False,
    )
```

```python
import jax
import jax.numpy as jnp
from jax import lax
from jax.sharding import PartitionSpec as P

epsilon = 1e-06
gelu_scale = 0.7978845608028654
gelu_cubic = 0.044715


def with_halo(block, sides, width):
    for axis, dim in sides:
        count = lax.axis_size(axis)
        forward = [(i, i + 1) for i in range(count - 1)]
        backward = [(target, source) for source, target in forward]
        low = lax.ppermute(
            lax.slice_in_dim(block, block.shape[dim] - width, None, axis=dim), axis, forward
        )
        high = lax.ppermute(lax.slice_in_dim(block, 0, width, axis=dim), axis, backward)
        block = jnp.concatenate([low, block, high], axis=dim)
    return block


def halo_rows(block, axis, width):
    count = lax.axis_size(axis)
    forward = [(i, i + 1) for i in range(count - 1)]
    backward = [(target, source) for source, target in forward]
    low = lax.ppermute(lax.slice_in_dim(block, block.shape[1] - width, None, axis=1), axis, forward)
    high = lax.ppermute(lax.slice_in_dim(block, 0, width, axis=1), axis, backward)
    return low, high


def gelu_value(inputs):
    inner = gelu_scale * (inputs + gelu_cubic * inputs * inputs * inputs)
    return 0.5 * inputs * (1.0 + jnp.tanh(inner))


def gelu_slope(inputs):
    inner = gelu_scale * (inputs + gelu_cubic * inputs * inputs * inputs)
    tangent = jnp.tanh(inner)
    return 0.5 * (1.0 + tangent) + 0.5 * inputs * (1.0 - tangent * tangent) * gelu_scale * (
        1.0 + 3.0 * gelu_cubic * inputs * inputs
    )


def forward_rows(emb, mirror, norm_gain):
    emb_rev = flip_channels(emb, mirror)
    as_float = emb.astype(jnp.float32)
    inverse = lax.rsqrt(jnp.mean(as_float * as_float, axis=1, keepdims=True) + epsilon)
    normed = as_float * inverse
    normed_rev = emb_rev.astype(jnp.float32) * inverse
    pre_fwd = normed * norm_gain
    pre_rev = normed_rev * norm_gain
    act_fwd = gelu_value(pre_fwd).astype(jnp.bfloat16)
    act_rev = gelu_value(pre_rev).astype(jnp.bfloat16)
    return as_float, inverse, normed, pre_fwd, pre_rev, act_fwd, act_rev


def tap_stack(padded, dilate, rim_width, bin_count, sign):
    slices = [
        lax.dynamic_slice_in_dim(padded, rim_width + sign * (tap_index - 1) * dilate, bin_count, 0)
        for tap_index in range(3)
    ]
    return jnp.concatenate(slices, axis=1)


def flip_channels(values, mirror):
    return jnp.dot(values, mirror, preferred_element_type=jnp.float32).astype(jnp.bfloat16)


def spread_back(back_taps, weight, channels):
    result = jnp.zeros((back_taps.shape[0], channels), jnp.float32)
    for tap_index in range(3):
        result = result + lax.dot_general(
            back_taps[:, tap_index * channels : (tap_index + 1) * channels],
            weight[tap_index],
            (((1,), (1,)), ((), ())),
            preferred_element_type=jnp.float32,
        )
    return result


def halve_sum(blocks, axis):
    size = lax.axis_size(axis)
    if size & (size - 1):
        flat = blocks.reshape((-1,) + blocks.shape[2:])
        return lax.psum_scatter(flat, axis, scatter_dimension=0, tiled=True).reshape(blocks.shape[1:])
    me = lax.axis_index(axis)
    bit = 1
    while bit < size:
        blocks = blocks.reshape((blocks.shape[0] // 2, 2) + blocks.shape[1:])
        mine = (me // bit) % 2
        keep = lax.dynamic_index_in_dim(blocks, mine, 1, keepdims=False)
        send = lax.dynamic_index_in_dim(blocks, 1 - mine, 1, keepdims=False)
        pairs = [(i, i ^ bit) for i in range(size)]
        blocks = keep + lax.ppermute(send, axis, pairs)
        bit *= 2
    return blocks[0]


def halve_step(values, dims, axis, bit):
    where = dims.index(f"{axis}{bit}")
    mine = (lax.axis_index(axis) // bit) % 2
    keep = lax.dynamic_index_in_dim(values, mine, where, keepdims=False)
    send = lax.dynamic_index_in_dim(values, 1 - mine, where, keepdims=False)
    size = lax.axis_size(axis)
    got = lax.ppermute(send, axis, [(i, i ^ bit) for i in range(size)])
    return keep + got, dims[:where] + dims[where + 1 :]


def scatter_sum(term, channels):
    win_count = lax.axis_size("win")
    seq_count = lax.axis_size("seq")
    blocks = term.reshape(win_count, seq_count, -1, channels)
    rows = blocks.shape[2]
    if (win_count & (win_count - 1)) or (seq_count & (seq_count - 1)) or rows % 2:
        return halve_sum(halve_sum(blocks, "win"), "seq")
    win_bits = [("win", 1 << k) for k in range(win_count.bit_length() - 1)]
    seq_bits = [("seq", 1 << k) for k in range(seq_count.bit_length() - 1)]
    names = [f"{a}{b}" for a, b in reversed(win_bits)] + [f"{a}{b}" for a, b in reversed(seq_bits)]
    values = blocks.reshape([2] * len(names) + [rows, channels])
    first, middle, last = win_bits[:1], win_bits[1:], seq_bits
    ways = 2 if len(middle) >= 2 else 1
    dims = list(names)
    for axis, bit in first:
        values, dims = halve_step(values, dims, axis, bit)
    lead = len(dims)
    parts = values.reshape(values.shape[:lead] + (ways, rows // ways, channels))
    states = [(lax.index_in_dim(parts, part, lead, keepdims=False), list(dims)) for part in range(ways)]
    for step in range(len(middle)):
        for part in range(ways):
            axis, bit = middle[(step + part) % len(middle)]
            states[part] = halve_step(states[part][0], states[part][1], axis, bit)
    values = jnp.concatenate([part for part, _ in states], axis=-2)
    dims = states[0][1]
    for axis, bit in last:
        values, dims = halve_step(values, dims, axis, bit)
    return values


def gather_rows(block, axis):
    size = lax.axis_size(axis)
    me = lax.axis_index(axis)
    whole = jnp.zeros((size,) + block.shape, block.dtype)
    whole = lax.dynamic_update_index_in_dim(whole, block, me, 0)
    for shift in range(1, size):
        pairs = [(i, (i + shift) % size) for i in range(size)]
        got = lax.ppermute(block, axis, pairs)
        whole = lax.dynamic_update_index_in_dim(whole, got, (me - shift) % size, 0)
    return whole.reshape((-1,) + block.shape[1:])


def per_device(
    embeddings,
    norm_gain,
    conv_weight,
    conv_bias,
    dilation,
    donor_bins,
    acceptor_bins,
    junction_count,
    donor_proj,
    acceptor_proj,
    out_cotangent,
    score_cotangent,
):
    bin_count = embeddings.shape[1]
    channels = embeddings.shape[2]
    rim_width = bin_count // 2
    dilate = dilation[0]
    lanes = lax.broadcasted_iota(jnp.int32, (channels, channels), 0)
    mirror = (
        lanes + lax.broadcasted_iota(jnp.int32, (channels, channels), 1) == channels - 1
    ).astype(jnp.bfloat16)
    own = slice(rim_width, rim_width + bin_count)

    window_bins = bin_count * lax.axis_size("seq")
    first_bin = lax.axis_index("seq") * bin_count
    window_emb = gather_rows(embeddings[0], "seq")
    low, high = halo_rows(out_cotangent[0][None], "seq", rim_width)
    cot_pad = jnp.concatenate([low[0], out_cotangent[0], high[0]])
    window_float, window_inverse, window_normed, window_fwd, window_rev, act_fwd, act_rev = (
        forward_rows(window_emb, mirror, norm_gain)
    )

    def own_rows(values):
        return lax.dynamic_slice_in_dim(values, first_bin, bin_count, 0)

    inverse, normed = own_rows(window_inverse), own_rows(window_normed)
    pre_fwd, pre_rev = own_rows(window_fwd), own_rows(window_rev)
    own_fwd, own_rev = own_rows(act_fwd), own_rows(act_rev)
    edge = ((rim_width, rim_width), (0, 0))
    taps_fwd = tap_stack(jnp.pad(act_fwd, edge), dilate, rim_width, window_bins, 1)
    taps_rev = tap_stack(jnp.pad(act_rev, edge), dilate, rim_width, window_bins, -1)
    conv_all = (
        jnp.dot(
            jnp.concatenate([taps_fwd, taps_rev], axis=0),
            conv_weight.reshape(3 * channels, channels),
            preferred_element_type=jnp.float32,
        )
        + conv_bias
    ).astype(jnp.bfloat16)
    conv_fwd = conv_all[:window_bins]
    conv_rev = flip_channels(conv_all[window_bins:], mirror)
    window_out = (
        window_float + 0.5 * (conv_fwd.astype(jnp.float32) + conv_rev.astype(jnp.float32))
    ).astype(jnp.bfloat16)
    block_flat = own_rows(window_out)

    both_proj = jnp.concatenate([donor_proj, acceptor_proj], axis=1)
    hidden = donor_proj.shape[1]
    window_proj = jnp.dot(window_out, both_proj, preferred_element_type=jnp.float32).astype(
        jnp.bfloat16
    )
    rows_donor = jnp.take(window_proj[:, :hidden], donor_bins[0], axis=0).astype(jnp.float32)
    rows_acceptor = jnp.take(window_proj[:, hidden:], acceptor_bins[0], axis=0).astype(jnp.float32)
    pair_total = donor_bins.shape[1]
    pair_share = pair_total // lax.axis_size("seq")
    pair_first = lax.axis_index("seq") * pair_share
    live_mask = (jnp.arange(pair_total) < junction_count[0]).astype(jnp.float32)
    score_scale = hidden ** (-0.5)
    products = jnp.sum(
        lax.dynamic_slice_in_dim(rows_donor, pair_first, pair_share, 0)
        * lax.dynamic_slice_in_dim(rows_acceptor, pair_first, pair_share, 0),
        axis=1,
    )
    junction_scores = (
        lax.dynamic_slice_in_dim(live_mask, pair_first, pair_share, 0) * products * score_scale
    )[None]
    pair_weight = score_cotangent[0] * live_mask * score_scale
    positions = lax.axis_index("seq") * bin_count - rim_width + jnp.arange(cot_pad.shape[0])
    pick_donor = (positions[:, None] == donor_bins[0][None, :]).astype(jnp.float32)
    pick_acceptor = (positions[:, None] == acceptor_bins[0][None, :]).astype(jnp.float32)
    grad_donor = jnp.dot(
        pick_donor, pair_weight[:, None] * rows_acceptor, precision=lax.Precision.HIGHEST
    ).astype(jnp.bfloat16)
    grad_acceptor = jnp.dot(
        pick_acceptor, pair_weight[:, None] * rows_donor, precision=lax.Precision.HIGHEST
    ).astype(jnp.bfloat16)
    out_grad = cot_pad.astype(jnp.float32) + lax.dot_general(
        jnp.concatenate([grad_donor, grad_acceptor], axis=1),
        both_proj,
        (((1,), (1,)), ((), ())),
        preferred_element_type=jnp.float32,
    )
    conv_grad = (0.5 * out_grad).astype(jnp.bfloat16)
    conv_grad_rev = flip_channels(conv_grad, mirror)
    back_fwd = tap_stack(conv_grad, dilate, rim_width, bin_count, -1)
    back_rev = tap_stack(conv_grad_rev, dilate, rim_width, bin_count, 1)
    dact_all = spread_back(jnp.concatenate([back_fwd, back_rev], axis=0), conv_weight, channels)
    dact_fwd = dact_all[:bin_count]
    dact_rev = dact_all[bin_count:]
    norm_rev = flip_channels(
        (dact_rev * gelu_slope(pre_rev) * norm_gain).astype(jnp.bfloat16), mirror
    )
    norm_grad = dact_fwd * gelu_slope(pre_fwd) * norm_gain + norm_rev.astype(jnp.float32)
    input_grad = (
        out_grad[own]
        + inverse
        * (norm_grad - normed * jnp.mean(norm_grad * normed, axis=1, keepdims=True))
    ).astype(jnp.bfloat16)[None]
    grad_term = lax.dot_general(
        jnp.concatenate([own_fwd, own_rev], axis=0),
        jnp.concatenate([conv_grad[own], conv_grad_rev[own]], axis=0),
        (((0,), (0,)), ((), ())),
        preferred_element_type=jnp.float32,
    )
    grad_term = grad_term / lax.axis_size("win")
    weight_grad = scatter_sum(grad_term, channels).reshape(-1)
    return (block_flat[None], junction_scores, input_grad, weight_grad)


def solution(mesh):
    return jax.shard_map(
        per_device,
        mesh=mesh,
        in_specs=(
            P("win", "seq", None),
            P(),
            P(),
            P(),
            P("win"),
            P("win", None),
            P("win", None),
            P("win"),
            P(),
            P(),
            P("win", "seq", None),
            P("win", None),
        ),
        out_specs=(
            P("win", "seq", None),
            P("win", "seq"),
            P("win", "seq", None),
            P(("win", "seq")),
        ),
        check_vma=False,
    )
```

```python
import jax
import jax.numpy as jnp
from jax import lax
from jax.sharding import PartitionSpec as P

epsilon = 1e-06
gelu_scale = 0.7978845608028654
gelu_cubic = 0.044715


def with_halo(block, sides, width):
    for axis, dim in sides:
        count = lax.axis_size(axis)
        forward = [(i, i + 1) for i in range(count - 1)]
        backward = [(target, source) for source, target in forward]
        low = lax.ppermute(
            lax.slice_in_dim(block, block.shape[dim] - width, None, axis=dim), axis, forward
        )
        high = lax.ppermute(lax.slice_in_dim(block, 0, width, axis=dim), axis, backward)
        block = jnp.concatenate([low, block, high], axis=dim)
    return block


def gelu_value(inputs):
    inner = gelu_scale * (inputs + gelu_cubic * inputs * inputs * inputs)
    return 0.5 * inputs * (1.0 + jnp.tanh(inner))


def gelu_slope(inputs):
    inner = gelu_scale * (inputs + gelu_cubic * inputs * inputs * inputs)
    tangent = jnp.tanh(inner)
    return 0.5 * (1.0 + tangent) + 0.5 * inputs * (1.0 - tangent * tangent) * gelu_scale * (
        1.0 + 3.0 * gelu_cubic * inputs * inputs
    )


def tap_stack(padded, dilate, rim_width, bin_count, sign):
    slices = [
        lax.dynamic_slice_in_dim(padded, rim_width + sign * (tap_index - 1) * dilate, bin_count, 0)
        for tap_index in range(3)
    ]
    return jnp.concatenate(slices, axis=1)


def flip_channels(values, mirror):
    return jnp.dot(values, mirror, preferred_element_type=jnp.float32).astype(jnp.bfloat16)


def spread_back(back_taps, weight, channels):
    result = jnp.zeros((back_taps.shape[0], channels), jnp.float32)
    for tap_index in range(3):
        result = result + lax.dot_general(
            back_taps[:, tap_index * channels : (tap_index + 1) * channels],
            weight[tap_index],
            (((1,), (1,)), ((), ())),
            preferred_element_type=jnp.float32,
        )
    return result


def halve_sum(blocks, axis):
    size = lax.axis_size(axis)
    if size & (size - 1):
        flat = blocks.reshape((-1,) + blocks.shape[2:])
        return lax.psum_scatter(flat, axis, scatter_dimension=0, tiled=True).reshape(blocks.shape[1:])
    me = lax.axis_index(axis)
    bit = 1
    while bit < size:
        blocks = blocks.reshape((blocks.shape[0] // 2, 2) + blocks.shape[1:])
        mine = (me // bit) % 2
        keep = lax.dynamic_index_in_dim(blocks, mine, 1, keepdims=False)
        send = lax.dynamic_index_in_dim(blocks, 1 - mine, 1, keepdims=False)
        pairs = [(i, i ^ bit) for i in range(size)]
        blocks = keep + lax.ppermute(send, axis, pairs)
        bit *= 2
    return blocks[0]


def halve_step(values, dims, axis, bit):
    where = dims.index(f"{axis}{bit}")
    mine = (lax.axis_index(axis) // bit) % 2
    keep = lax.dynamic_index_in_dim(values, mine, where, keepdims=False)
    send = lax.dynamic_index_in_dim(values, 1 - mine, where, keepdims=False)
    size = lax.axis_size(axis)
    got = lax.ppermute(send, axis, [(i, i ^ bit) for i in range(size)])
    return keep + got, dims[:where] + dims[where + 1 :]


def scatter_sum(term, channels):
    win_count = lax.axis_size("win")
    seq_count = lax.axis_size("seq")
    blocks = term.reshape(win_count, seq_count, -1, channels)
    rows = blocks.shape[2]
    if (win_count & (win_count - 1)) or (seq_count & (seq_count - 1)) or rows % 2:
        return halve_sum(halve_sum(blocks, "win"), "seq")
    win_bits = [("win", 1 << k) for k in range(win_count.bit_length() - 1)]
    seq_bits = [("seq", 1 << k) for k in range(seq_count.bit_length() - 1)]
    names = [f"{a}{b}" for a, b in reversed(win_bits)] + [f"{a}{b}" for a, b in reversed(seq_bits)]
    values = blocks.reshape([2] * len(names) + [rows, channels])
    first, middle, last = win_bits[:1], win_bits[1:], seq_bits
    ways = 2 if len(middle) >= 2 else 1
    dims = list(names)
    for axis, bit in first:
        values, dims = halve_step(values, dims, axis, bit)
    lead = len(dims)
    parts = values.reshape(values.shape[:lead] + (ways, rows // ways, channels))
    states = [(lax.index_in_dim(parts, part, lead, keepdims=False), list(dims)) for part in range(ways)]
    for step in range(len(middle)):
        for part in range(ways):
            axis, bit = middle[(step + part) % len(middle)]
            states[part] = halve_step(states[part][0], states[part][1], axis, bit)
    values = jnp.concatenate([part for part, _ in states], axis=-2)
    dims = states[0][1]
    values = values.reshape((seq_count,) + values.shape[len(last) :])
    me = lax.axis_index("seq")
    total = lax.dynamic_index_in_dim(values, me, 0, keepdims=False)
    for shift in range(1, seq_count):
        send = lax.dynamic_index_in_dim(values, (me + shift) % seq_count, 0, keepdims=False)
        total = total + lax.ppermute(
            send, "seq", [(i, (i + shift) % seq_count) for i in range(seq_count)]
        )
    return total


def gather_rows(block, axis):
    size = lax.axis_size(axis)
    me = lax.axis_index(axis)
    whole = jnp.zeros((size,) + block.shape, block.dtype)
    whole = lax.dynamic_update_index_in_dim(whole, block, me, 0)
    for shift in range(1, size):
        pairs = [(i, (i + shift) % size) for i in range(size)]
        got = lax.ppermute(block, axis, pairs)
        whole = lax.dynamic_update_index_in_dim(whole, got, (me - shift) % size, 0)
    return whole.reshape((-1,) + block.shape[1:])


def per_device(
    embeddings,
    norm_gain,
    conv_weight,
    conv_bias,
    dilation,
    donor_bins,
    acceptor_bins,
    junction_count,
    donor_proj,
    acceptor_proj,
    out_cotangent,
    score_cotangent,
):
    bin_count = embeddings.shape[1]
    channels = embeddings.shape[2]
    rim_width = bin_count // 2
    dilate = dilation[0]
    lanes = lax.broadcasted_iota(jnp.int32, (channels, channels), 0)
    mirror = (
        lanes + lax.broadcasted_iota(jnp.int32, (channels, channels), 1) == channels - 1
    ).astype(jnp.bfloat16)
    own = slice(rim_width, rim_width + bin_count)

    padded_in = with_halo(jnp.stack([embeddings[0], out_cotangent[0]]), (("seq", 1),), rim_width)
    emb = padded_in[0]
    emb_rev = flip_channels(emb, mirror)
    as_float = emb.astype(jnp.float32)
    inverse = lax.rsqrt(jnp.mean(as_float * as_float, axis=1, keepdims=True) + epsilon)
    normed = as_float * inverse
    normed_rev = emb_rev.astype(jnp.float32) * inverse
    pre_fwd = normed * norm_gain
    pre_rev = normed_rev * norm_gain
    act_fwd = gelu_value(pre_fwd).astype(jnp.bfloat16)
    act_rev = gelu_value(pre_rev).astype(jnp.bfloat16)

    taps_fwd = tap_stack(act_fwd, dilate, rim_width, bin_count, 1)
    taps_rev = tap_stack(act_rev, dilate, rim_width, bin_count, -1)
    conv_all = (
        jnp.dot(
            jnp.concatenate([taps_fwd, taps_rev], axis=0),
            conv_weight.reshape(3 * channels, channels),
            preferred_element_type=jnp.float32,
        )
        + conv_bias
    ).astype(jnp.bfloat16)
    conv_fwd = conv_all[:bin_count]
    conv_rev = flip_channels(conv_all[bin_count:], mirror)
    block_flat = (
        as_float[own] + 0.5 * (conv_fwd.astype(jnp.float32) + conv_rev.astype(jnp.float32))
    ).astype(jnp.bfloat16)

    both_proj = jnp.concatenate([donor_proj, acceptor_proj], axis=1)
    hidden = donor_proj.shape[1]
    window_out = gather_rows(block_flat, "seq")
    window_proj = jnp.dot(window_out, both_proj, preferred_element_type=jnp.float32).astype(
        jnp.bfloat16
    )
    rows_donor = jnp.take(window_proj[:, :hidden], donor_bins[0], axis=0).astype(jnp.float32)
    rows_acceptor = jnp.take(window_proj[:, hidden:], acceptor_bins[0], axis=0).astype(jnp.float32)
    pair_total = donor_bins.shape[1]
    pair_share = pair_total // lax.axis_size("seq")
    pair_first = lax.axis_index("seq") * pair_share
    live_mask = (jnp.arange(pair_total) < junction_count[0]).astype(jnp.float32)
    score_scale = hidden ** (-0.5)
    products = jnp.sum(
        lax.dynamic_slice_in_dim(rows_donor, pair_first, pair_share, 0)
        * lax.dynamic_slice_in_dim(rows_acceptor, pair_first, pair_share, 0),
        axis=1,
    )
    junction_scores = (
        lax.dynamic_slice_in_dim(live_mask, pair_first, pair_share, 0) * products * score_scale
    )[None]
    pair_weight = score_cotangent[0] * live_mask * score_scale
    positions = lax.axis_index("seq") * bin_count - rim_width + jnp.arange(emb.shape[0])
    pick_donor = (positions[:, None] == donor_bins[0][None, :]).astype(jnp.float32)
    pick_acceptor = (positions[:, None] == acceptor_bins[0][None, :]).astype(jnp.float32)
    grad_donor = jnp.dot(
        pick_donor, pair_weight[:, None] * rows_acceptor, precision=lax.Precision.HIGHEST
    ).astype(jnp.bfloat16)
    grad_acceptor = jnp.dot(
        pick_acceptor, pair_weight[:, None] * rows_donor, precision=lax.Precision.HIGHEST
    ).astype(jnp.bfloat16)
    out_grad = padded_in[1].astype(jnp.float32) + lax.dot_general(
        jnp.concatenate([grad_donor, grad_acceptor], axis=1),
        both_proj,
        (((1,), (1,)), ((), ())),
        preferred_element_type=jnp.float32,
    )
    conv_grad = (0.5 * out_grad).astype(jnp.bfloat16)
    conv_grad_rev = flip_channels(conv_grad, mirror)
    back_fwd = tap_stack(conv_grad, dilate, rim_width, bin_count, -1)
    back_rev = tap_stack(conv_grad_rev, dilate, rim_width, bin_count, 1)
    dact_all = spread_back(jnp.concatenate([back_fwd, back_rev], axis=0), conv_weight, channels)
    dact_fwd = dact_all[:bin_count]
    dact_rev = dact_all[bin_count:]
    norm_rev = flip_channels(
        (dact_rev * gelu_slope(pre_rev[own]) * norm_gain).astype(jnp.bfloat16), mirror
    )
    norm_grad = dact_fwd * gelu_slope(pre_fwd[own]) * norm_gain + norm_rev.astype(jnp.float32)
    normed_own = normed[own]
    input_grad = (
        out_grad[own]
        + inverse[own]
        * (norm_grad - normed_own * jnp.mean(norm_grad * normed_own, axis=1, keepdims=True))
    ).astype(jnp.bfloat16)[None]
    grad_term = lax.dot_general(
        jnp.concatenate([act_fwd[own], act_rev[own]], axis=0),
        jnp.concatenate([conv_grad[own], conv_grad_rev[own]], axis=0),
        (((0,), (0,)), ((), ())),
        preferred_element_type=jnp.float32,
    )
    grad_term = grad_term / lax.axis_size("win")
    weight_grad = scatter_sum(grad_term, channels).reshape(-1)
    return (block_flat[None], junction_scores, input_grad, weight_grad)


def solution(mesh):
    return jax.shard_map(
        per_device,
        mesh=mesh,
        in_specs=(
            P("win", "seq", None),
            P(),
            P(),
            P(),
            P("win"),
            P("win", None),
            P("win", None),
            P("win"),
            P(),
            P(),
            P("win", "seq", None),
            P("win", None),
        ),
        out_specs=(
            P("win", "seq", None),
            P("win", "seq"),
            P("win", "seq", None),
            P(("win", "seq")),
        ),
        check_vma=False,
    )
```

```python
import jax
import jax.numpy as jnp
from jax import lax
from jax.sharding import PartitionSpec as P

epsilon = 1e-06
gelu_scale = 0.7978845608028654
gelu_cubic = 0.044715


def with_halo(block, sides, width):
    for axis, dim in sides:
        count = lax.axis_size(axis)
        forward = [(i, i + 1) for i in range(count - 1)]
        backward = [(target, source) for source, target in forward]
        low = lax.ppermute(
            lax.slice_in_dim(block, block.shape[dim] - width, None, axis=dim), axis, forward
        )
        high = lax.ppermute(lax.slice_in_dim(block, 0, width, axis=dim), axis, backward)
        block = jnp.concatenate([low, block, high], axis=dim)
    return block


def gelu_value(inputs):
    inner = gelu_scale * (inputs + gelu_cubic * inputs * inputs * inputs)
    return 0.5 * inputs * (1.0 + jnp.tanh(inner))


def gelu_slope(inputs):
    inner = gelu_scale * (inputs + gelu_cubic * inputs * inputs * inputs)
    tangent = jnp.tanh(inner)
    return 0.5 * (1.0 + tangent) + 0.5 * inputs * (1.0 - tangent * tangent) * gelu_scale * (
        1.0 + 3.0 * gelu_cubic * inputs * inputs
    )


def tap_stack(padded, dilate, rim_width, bin_count, sign):
    slices = [
        lax.dynamic_slice_in_dim(padded, rim_width + sign * (tap_index - 1) * dilate, bin_count, 0)
        for tap_index in range(3)
    ]
    return jnp.concatenate(slices, axis=1)


def flip_channels(values, mirror):
    return jnp.dot(values, mirror, preferred_element_type=jnp.float32).astype(jnp.bfloat16)


def spread_back(back_taps, weight, channels):
    result = jnp.zeros((back_taps.shape[0], channels), jnp.float32)
    for tap_index in range(3):
        result = result + lax.dot_general(
            back_taps[:, tap_index * channels : (tap_index + 1) * channels],
            weight[tap_index],
            (((1,), (1,)), ((), ())),
            preferred_element_type=jnp.float32,
        )
    return result


def halve_sum(blocks, axis):
    size = lax.axis_size(axis)
    if size & (size - 1):
        flat = blocks.reshape((-1,) + blocks.shape[2:])
        return lax.psum_scatter(flat, axis, scatter_dimension=0, tiled=True).reshape(blocks.shape[1:])
    me = lax.axis_index(axis)
    bit = 1
    while bit < size:
        blocks = blocks.reshape((blocks.shape[0] // 2, 2) + blocks.shape[1:])
        mine = (me // bit) % 2
        keep = lax.dynamic_index_in_dim(blocks, mine, 1, keepdims=False)
        send = lax.dynamic_index_in_dim(blocks, 1 - mine, 1, keepdims=False)
        pairs = [(i, i ^ bit) for i in range(size)]
        blocks = keep + lax.ppermute(send, axis, pairs)
        bit *= 2
    return blocks[0]


def halve_step(values, dims, axis, bit, link_type):
    where = dims.index(f"{axis}{bit}")
    mine = (lax.axis_index(axis) // bit) % 2
    keep = lax.dynamic_index_in_dim(values, mine, where, keepdims=False)
    send = lax.dynamic_index_in_dim(values, 1 - mine, where, keepdims=False).astype(link_type)
    size = lax.axis_size(axis)
    got = lax.ppermute(send, axis, [(i, i ^ bit) for i in range(size)])
    return keep + got.astype(keep.dtype), dims[:where] + dims[where + 1 :]


def scatter_sum(term, channels):
    win_count = lax.axis_size("win")
    seq_count = lax.axis_size("seq")
    blocks = term.reshape(win_count, seq_count, -1, channels)
    rows = blocks.shape[2]
    if (win_count & (win_count - 1)) or (seq_count & (seq_count - 1)) or rows % 2:
        return halve_sum(halve_sum(blocks, "win"), "seq")
    win_bits = [("win", 1 << k) for k in range(win_count.bit_length() - 1)]
    seq_bits = [("seq", 1 << k) for k in range(seq_count.bit_length() - 1)]
    names = [f"{a}{b}" for a, b in reversed(win_bits)] + [f"{a}{b}" for a, b in reversed(seq_bits)]
    values = blocks.reshape([2] * len(names) + [rows, channels])
    first, middle, last = win_bits[:1], win_bits[1:], seq_bits
    ways = 2 if len(middle) >= 2 else 1
    dims = list(names)
    for axis, bit in first:
        values, dims = halve_step(values, dims, axis, bit, jnp.float32)
    lead = len(dims)
    parts = values.reshape(values.shape[:lead] + (ways, rows // ways, channels))
    states = [(lax.index_in_dim(parts, part, lead, keepdims=False), list(dims)) for part in range(ways)]
    for step in range(len(middle)):
        for part in range(ways):
            axis, bit = middle[(step + part) % len(middle)]
            states[part] = halve_step(states[part][0], states[part][1], axis, bit, jnp.bfloat16)
    values = jnp.concatenate([part for part, _ in states], axis=-2)
    dims = states[0][1]
    values = values.reshape((seq_count,) + values.shape[len(last) :])
    me = lax.axis_index("seq")
    total = lax.dynamic_index_in_dim(values, me, 0, keepdims=False)
    for shift in range(1, seq_count):
        send = lax.dynamic_index_in_dim(values, (me + shift) % seq_count, 0, keepdims=False)
        got = lax.ppermute(
            send.astype(jnp.bfloat16), "seq", [(i, (i + shift) % seq_count) for i in range(seq_count)]
        )
        total = total + got.astype(jnp.float32)
    return total


def gather_rows(block, axis):
    size = lax.axis_size(axis)
    me = lax.axis_index(axis)
    whole = jnp.zeros((size,) + block.shape, block.dtype)
    whole = lax.dynamic_update_index_in_dim(whole, block, me, 0)
    for shift in range(1, size):
        pairs = [(i, (i + shift) % size) for i in range(size)]
        got = lax.ppermute(block, axis, pairs)
        whole = lax.dynamic_update_index_in_dim(whole, got, (me - shift) % size, 0)
    return whole.reshape((-1,) + block.shape[1:])


def per_device(
    embeddings,
    norm_gain,
    conv_weight,
    conv_bias,
    dilation,
    donor_bins,
    acceptor_bins,
    junction_count,
    donor_proj,
    acceptor_proj,
    out_cotangent,
    score_cotangent,
):
    bin_count = embeddings.shape[1]
    channels = embeddings.shape[2]
    rim_width = bin_count // 2
    dilate = dilation[0]
    lanes = lax.broadcasted_iota(jnp.int32, (channels, channels), 0)
    mirror = (
        lanes + lax.broadcasted_iota(jnp.int32, (channels, channels), 1) == channels - 1
    ).astype(jnp.bfloat16)
    own = slice(rim_width, rim_width + bin_count)

    padded_in = with_halo(jnp.stack([embeddings[0], out_cotangent[0]]), (("seq", 1),), rim_width)
    emb = padded_in[0]
    emb_rev = flip_channels(emb, mirror)
    as_float = emb.astype(jnp.float32)
    inverse = lax.rsqrt(jnp.mean(as_float * as_float, axis=1, keepdims=True) + epsilon)
    normed = as_float * inverse
    normed_rev = emb_rev.astype(jnp.float32) * inverse
    pre_fwd = normed * norm_gain
    pre_rev = normed_rev * norm_gain
    act_fwd = gelu_value(pre_fwd).astype(jnp.bfloat16)
    act_rev = gelu_value(pre_rev).astype(jnp.bfloat16)

    taps_fwd = tap_stack(act_fwd, dilate, rim_width, bin_count, 1)
    taps_rev = tap_stack(act_rev, dilate, rim_width, bin_count, -1)
    conv_all = (
        jnp.dot(
            jnp.concatenate([taps_fwd, taps_rev], axis=0),
            conv_weight.reshape(3 * channels, channels),
            preferred_element_type=jnp.float32,
        )
        + conv_bias
    ).astype(jnp.bfloat16)
    conv_fwd = conv_all[:bin_count]
    conv_rev = flip_channels(conv_all[bin_count:], mirror)
    block_flat = (
        as_float[own] + 0.5 * (conv_fwd.astype(jnp.float32) + conv_rev.astype(jnp.float32))
    ).astype(jnp.bfloat16)

    both_proj = jnp.concatenate([donor_proj, acceptor_proj], axis=1)
    hidden = donor_proj.shape[1]
    window_out = gather_rows(block_flat, "seq")
    window_proj = jnp.dot(window_out, both_proj, preferred_element_type=jnp.float32).astype(
        jnp.bfloat16
    )
    rows_donor = jnp.take(window_proj[:, :hidden], donor_bins[0], axis=0).astype(jnp.float32)
    rows_acceptor = jnp.take(window_proj[:, hidden:], acceptor_bins[0], axis=0).astype(jnp.float32)
    pair_total = donor_bins.shape[1]
    pair_share = pair_total // lax.axis_size("seq")
    pair_first = lax.axis_index("seq") * pair_share
    live_mask = (jnp.arange(pair_total) < junction_count[0]).astype(jnp.float32)
    score_scale = hidden ** (-0.5)
    products = jnp.sum(
        lax.dynamic_slice_in_dim(rows_donor, pair_first, pair_share, 0)
        * lax.dynamic_slice_in_dim(rows_acceptor, pair_first, pair_share, 0),
        axis=1,
    )
    junction_scores = (
        lax.dynamic_slice_in_dim(live_mask, pair_first, pair_share, 0) * products * score_scale
    )[None]
    pair_weight = score_cotangent[0] * live_mask * score_scale
    positions = lax.axis_index("seq") * bin_count - rim_width + jnp.arange(emb.shape[0])
    pick_donor = (positions[:, None] == donor_bins[0][None, :]).astype(jnp.float32)
    pick_acceptor = (positions[:, None] == acceptor_bins[0][None, :]).astype(jnp.float32)
    grad_donor = jnp.dot(
        pick_donor, pair_weight[:, None] * rows_acceptor, precision=lax.Precision.HIGHEST
    ).astype(jnp.bfloat16)
    grad_acceptor = jnp.dot(
        pick_acceptor, pair_weight[:, None] * rows_donor, precision=lax.Precision.HIGHEST
    ).astype(jnp.bfloat16)
    out_grad = padded_in[1].astype(jnp.float32) + lax.dot_general(
        jnp.concatenate([grad_donor, grad_acceptor], axis=1),
        both_proj,
        (((1,), (1,)), ((), ())),
        preferred_element_type=jnp.float32,
    )
    conv_grad = (0.5 * out_grad).astype(jnp.bfloat16)
    conv_grad_rev = flip_channels(conv_grad, mirror)
    back_fwd = tap_stack(conv_grad, dilate, rim_width, bin_count, -1)
    back_rev = tap_stack(conv_grad_rev, dilate, rim_width, bin_count, 1)
    dact_all = spread_back(jnp.concatenate([back_fwd, back_rev], axis=0), conv_weight, channels)
    dact_fwd = dact_all[:bin_count]
    dact_rev = dact_all[bin_count:]
    norm_rev = flip_channels(
        (dact_rev * gelu_slope(pre_rev[own]) * norm_gain).astype(jnp.bfloat16), mirror
    )
    norm_grad = dact_fwd * gelu_slope(pre_fwd[own]) * norm_gain + norm_rev.astype(jnp.float32)
    normed_own = normed[own]
    input_grad = (
        out_grad[own]
        + inverse[own]
        * (norm_grad - normed_own * jnp.mean(norm_grad * normed_own, axis=1, keepdims=True))
    ).astype(jnp.bfloat16)[None]
    grad_term = lax.dot_general(
        jnp.concatenate([act_fwd[own], act_rev[own]], axis=0),
        jnp.concatenate([conv_grad[own], conv_grad_rev[own]], axis=0),
        (((0,), (0,)), ((), ())),
        preferred_element_type=jnp.float32,
    )
    grad_term = grad_term / lax.axis_size("win")
    weight_grad = scatter_sum(grad_term, channels).reshape(-1)
    return (block_flat[None], junction_scores, input_grad, weight_grad)


def solution(mesh):
    return jax.shard_map(
        per_device,
        mesh=mesh,
        in_specs=(
            P("win", "seq", None),
            P(),
            P(),
            P(),
            P("win"),
            P("win", None),
            P("win", None),
            P("win"),
            P(),
            P(),
            P("win", "seq", None),
            P("win", None),
        ),
        out_specs=(
            P("win", "seq", None),
            P("win", "seq"),
            P("win", "seq", None),
            P(("win", "seq")),
        ),
        check_vma=False,
    )
```

```python
import jax
import jax.numpy as jnp
from jax import lax
from jax.sharding import PartitionSpec as P

epsilon = 1e-06
gelu_scale = 0.7978845608028654
gelu_cubic = 0.044715


def with_halo(block, sides, width):
    for axis, dim in sides:
        count = lax.axis_size(axis)
        forward = [(i, i + 1) for i in range(count - 1)]
        backward = [(target, source) for source, target in forward]
        low = lax.ppermute(
            lax.slice_in_dim(block, block.shape[dim] - width, None, axis=dim), axis, forward
        )
        high = lax.ppermute(lax.slice_in_dim(block, 0, width, axis=dim), axis, backward)
        block = jnp.concatenate([low, block, high], axis=dim)
    return block


def halo_rows(block, axis, width):
    count = lax.axis_size(axis)
    forward = [(i, i + 1) for i in range(count - 1)]
    backward = [(target, source) for source, target in forward]
    low = lax.ppermute(lax.slice_in_dim(block, block.shape[1] - width, None, axis=1), axis, forward)
    high = lax.ppermute(lax.slice_in_dim(block, 0, width, axis=1), axis, backward)
    return low, high


def gelu_value(inputs):
    inner = gelu_scale * (inputs + gelu_cubic * inputs * inputs * inputs)
    return 0.5 * inputs * (1.0 + jnp.tanh(inner))


def gelu_slope(inputs):
    inner = gelu_scale * (inputs + gelu_cubic * inputs * inputs * inputs)
    tangent = jnp.tanh(inner)
    return 0.5 * (1.0 + tangent) + 0.5 * inputs * (1.0 - tangent * tangent) * gelu_scale * (
        1.0 + 3.0 * gelu_cubic * inputs * inputs
    )


def forward_rows(emb, mirror, norm_gain):
    emb_rev = flip_channels(emb, mirror)
    as_float = emb.astype(jnp.float32)
    inverse = lax.rsqrt(jnp.mean(as_float * as_float, axis=1, keepdims=True) + epsilon)
    normed = as_float * inverse
    normed_rev = emb_rev.astype(jnp.float32) * inverse
    pre_fwd = normed * norm_gain
    pre_rev = normed_rev * norm_gain
    act_fwd = gelu_value(pre_fwd).astype(jnp.bfloat16)
    act_rev = gelu_value(pre_rev).astype(jnp.bfloat16)
    return as_float, inverse, normed, pre_fwd, pre_rev, act_fwd, act_rev


def tap_stack(padded, dilate, rim_width, bin_count, sign):
    slices = [
        lax.dynamic_slice_in_dim(padded, rim_width + sign * (tap_index - 1) * dilate, bin_count, 0)
        for tap_index in range(3)
    ]
    return jnp.concatenate(slices, axis=1)


def flip_channels(values, mirror):
    return jnp.dot(values, mirror, preferred_element_type=jnp.float32).astype(jnp.bfloat16)


def spread_back(back_taps, weight, channels):
    result = jnp.zeros((back_taps.shape[0], channels), jnp.float32)
    for tap_index in range(3):
        result = result + lax.dot_general(
            back_taps[:, tap_index * channels : (tap_index + 1) * channels],
            weight[tap_index],
            (((1,), (1,)), ((), ())),
            preferred_element_type=jnp.float32,
        )
    return result


def halve_sum(blocks, axis):
    size = lax.axis_size(axis)
    if size & (size - 1):
        flat = blocks.reshape((-1,) + blocks.shape[2:])
        return lax.psum_scatter(flat, axis, scatter_dimension=0, tiled=True).reshape(blocks.shape[1:])
    me = lax.axis_index(axis)
    bit = 1
    while bit < size:
        blocks = blocks.reshape((blocks.shape[0] // 2, 2) + blocks.shape[1:])
        mine = (me // bit) % 2
        keep = lax.dynamic_index_in_dim(blocks, mine, 1, keepdims=False)
        send = lax.dynamic_index_in_dim(blocks, 1 - mine, 1, keepdims=False)
        pairs = [(i, i ^ bit) for i in range(size)]
        blocks = keep + lax.ppermute(send, axis, pairs)
        bit *= 2
    return blocks[0]


def halve_step(values, dims, axis, bit, link_type):
    where = dims.index(f"{axis}{bit}")
    mine = (lax.axis_index(axis) // bit) % 2
    keep = lax.dynamic_index_in_dim(values, mine, where, keepdims=False)
    send = lax.dynamic_index_in_dim(values, 1 - mine, where, keepdims=False).astype(link_type)
    size = lax.axis_size(axis)
    got = lax.ppermute(send, axis, [(i, i ^ bit) for i in range(size)])
    return keep + got.astype(keep.dtype), dims[:where] + dims[where + 1 :]


def scatter_sum(term, channels):
    win_count = lax.axis_size("win")
    seq_count = lax.axis_size("seq")
    blocks = term.reshape(win_count, seq_count, -1, channels)
    rows = blocks.shape[2]
    if (win_count & (win_count - 1)) or (seq_count & (seq_count - 1)) or rows % 2:
        return halve_sum(halve_sum(blocks, "win"), "seq")
    win_bits = [("win", 1 << k) for k in range(win_count.bit_length() - 1)]
    seq_bits = [("seq", 1 << k) for k in range(seq_count.bit_length() - 1)]
    names = [f"{a}{b}" for a, b in reversed(win_bits)] + [f"{a}{b}" for a, b in reversed(seq_bits)]
    values = blocks.reshape([2] * len(names) + [rows, channels])
    first, middle, last = win_bits[:1], win_bits[1:], seq_bits
    ways = 2 if len(middle) >= 2 else 1
    dims = list(names)
    for axis, bit in first:
        values, dims = halve_step(values, dims, axis, bit, jnp.float32)
    lead = len(dims)
    parts = values.reshape(values.shape[:lead] + (ways, rows // ways, channels))
    states = [(lax.index_in_dim(parts, part, lead, keepdims=False), list(dims)) for part in range(ways)]
    for step in range(len(middle)):
        for part in range(ways):
            axis, bit = middle[(step + part) % len(middle)]
            states[part] = halve_step(states[part][0], states[part][1], axis, bit, jnp.bfloat16)
    values = jnp.concatenate([part for part, _ in states], axis=-2)
    dims = states[0][1]
    values = values.reshape((seq_count,) + values.shape[len(last) :])
    me = lax.axis_index("seq")
    total = lax.dynamic_index_in_dim(values, me, 0, keepdims=False)
    for shift in range(1, seq_count):
        send = lax.dynamic_index_in_dim(values, (me + shift) % seq_count, 0, keepdims=False)
        got = lax.ppermute(
            send.astype(jnp.bfloat16), "seq", [(i, (i + shift) % seq_count) for i in range(seq_count)]
        )
        total = total + got.astype(jnp.float32)
    return total


def gather_rows(block, axis):
    size = lax.axis_size(axis)
    me = lax.axis_index(axis)
    whole = jnp.zeros((size,) + block.shape, block.dtype)
    whole = lax.dynamic_update_index_in_dim(whole, block, me, 0)
    for shift in range(1, size):
        pairs = [(i, (i + shift) % size) for i in range(size)]
        got = lax.ppermute(block, axis, pairs)
        whole = lax.dynamic_update_index_in_dim(whole, got, (me - shift) % size, 0)
    return whole.reshape((-1,) + block.shape[1:])


def per_device(
    embeddings,
    norm_gain,
    conv_weight,
    conv_bias,
    dilation,
    donor_bins,
    acceptor_bins,
    junction_count,
    donor_proj,
    acceptor_proj,
    out_cotangent,
    score_cotangent,
):
    bin_count = embeddings.shape[1]
    channels = embeddings.shape[2]
    rim_width = bin_count // 2
    dilate = dilation[0]
    lanes = lax.broadcasted_iota(jnp.int32, (channels, channels), 0)
    mirror = (
        lanes + lax.broadcasted_iota(jnp.int32, (channels, channels), 1) == channels - 1
    ).astype(jnp.bfloat16)
    own = slice(rim_width, rim_width + bin_count)

    window_bins = bin_count * lax.axis_size("seq")
    first_bin = lax.axis_index("seq") * bin_count
    window_emb = gather_rows(embeddings[0], "seq")
    low, high = halo_rows(out_cotangent[0][None], "seq", rim_width)
    cot_pad = jnp.concatenate([low[0], out_cotangent[0], high[0]])
    window_float, window_inverse, window_normed, window_fwd, window_rev, act_fwd, act_rev = (
        forward_rows(window_emb, mirror, norm_gain)
    )

    def own_rows(values):
        return lax.dynamic_slice_in_dim(values, first_bin, bin_count, 0)

    inverse, normed = own_rows(window_inverse), own_rows(window_normed)
    pre_fwd, pre_rev = own_rows(window_fwd), own_rows(window_rev)
    own_fwd, own_rev = own_rows(act_fwd), own_rows(act_rev)
    edge = ((rim_width, rim_width), (0, 0))
    taps_fwd = tap_stack(jnp.pad(act_fwd, edge), dilate, rim_width, window_bins, 1)
    taps_rev = tap_stack(jnp.pad(act_rev, edge), dilate, rim_width, window_bins, -1)
    taps_all = lax.optimization_barrier(jnp.concatenate([taps_fwd, taps_rev], axis=0))
    conv_all = (
        jnp.dot(
            taps_all,
            conv_weight.reshape(3 * channels, channels),
            preferred_element_type=jnp.float32,
        )
        + conv_bias
    ).astype(jnp.bfloat16)
    conv_fwd = conv_all[:window_bins]
    conv_rev = flip_channels(conv_all[window_bins:], mirror)
    window_out = (
        window_float + 0.5 * (conv_fwd.astype(jnp.float32) + conv_rev.astype(jnp.float32))
    ).astype(jnp.bfloat16)
    block_flat = own_rows(window_out)

    both_proj = jnp.concatenate([donor_proj, acceptor_proj], axis=1)
    hidden = donor_proj.shape[1]
    window_proj = jnp.dot(window_out, both_proj, preferred_element_type=jnp.float32).astype(
        jnp.bfloat16
    )
    rows_donor = jnp.take(window_proj[:, :hidden], donor_bins[0], axis=0).astype(jnp.float32)
    rows_acceptor = jnp.take(window_proj[:, hidden:], acceptor_bins[0], axis=0).astype(jnp.float32)
    pair_total = donor_bins.shape[1]
    pair_share = pair_total // lax.axis_size("seq")
    pair_first = lax.axis_index("seq") * pair_share
    live_mask = (jnp.arange(pair_total) < junction_count[0]).astype(jnp.float32)
    score_scale = hidden ** (-0.5)
    products = jnp.sum(
        lax.dynamic_slice_in_dim(rows_donor, pair_first, pair_share, 0)
        * lax.dynamic_slice_in_dim(rows_acceptor, pair_first, pair_share, 0),
        axis=1,
    )
    junction_scores = (
        lax.dynamic_slice_in_dim(live_mask, pair_first, pair_share, 0) * products * score_scale
    )[None]
    pair_weight = score_cotangent[0] * live_mask * score_scale
    positions = lax.axis_index("seq") * bin_count - rim_width + jnp.arange(cot_pad.shape[0])
    pick_donor = (positions[:, None] == donor_bins[0][None, :]).astype(jnp.float32)
    pick_acceptor = (positions[:, None] == acceptor_bins[0][None, :]).astype(jnp.float32)
    grad_donor = jnp.dot(
        pick_donor, pair_weight[:, None] * rows_acceptor, precision=lax.Precision.HIGHEST
    ).astype(jnp.bfloat16)
    grad_acceptor = jnp.dot(
        pick_acceptor, pair_weight[:, None] * rows_donor, precision=lax.Precision.HIGHEST
    ).astype(jnp.bfloat16)
    out_grad = cot_pad.astype(jnp.float32) + lax.dot_general(
        jnp.concatenate([grad_donor, grad_acceptor], axis=1),
        both_proj,
        (((1,), (1,)), ((), ())),
        preferred_element_type=jnp.float32,
    )
    conv_grad = (0.5 * out_grad).astype(jnp.bfloat16)
    conv_grad_rev = flip_channels(conv_grad, mirror)
    back_fwd = tap_stack(conv_grad, dilate, rim_width, bin_count, -1)
    back_rev = tap_stack(conv_grad_rev, dilate, rim_width, bin_count, 1)
    dact_all = spread_back(jnp.concatenate([back_fwd, back_rev], axis=0), conv_weight, channels)
    dact_fwd = dact_all[:bin_count]
    dact_rev = dact_all[bin_count:]
    norm_rev = flip_channels(
        (dact_rev * gelu_slope(pre_rev) * norm_gain).astype(jnp.bfloat16), mirror
    )
    norm_grad = dact_fwd * gelu_slope(pre_fwd) * norm_gain + norm_rev.astype(jnp.float32)
    input_grad = (
        out_grad[own]
        + inverse
        * (norm_grad - normed * jnp.mean(norm_grad * normed, axis=1, keepdims=True))
    ).astype(jnp.bfloat16)[None]
    grad_term = lax.dot_general(
        jnp.concatenate([own_fwd, own_rev], axis=0),
        jnp.concatenate([conv_grad[own], conv_grad_rev[own]], axis=0),
        (((0,), (0,)), ((), ())),
        preferred_element_type=jnp.float32,
    )
    grad_term = grad_term / lax.axis_size("win")
    weight_grad = scatter_sum(grad_term, channels).reshape(-1)
    return (block_flat[None], junction_scores, input_grad, weight_grad)


def solution(mesh):
    return jax.shard_map(
        per_device,
        mesh=mesh,
        in_specs=(
            P("win", "seq", None),
            P(),
            P(),
            P(),
            P("win"),
            P("win", None),
            P("win", None),
            P("win"),
            P(),
            P(),
            P("win", "seq", None),
            P("win", None),
        ),
        out_specs=(
            P("win", "seq", None),
            P("win", "seq"),
            P("win", "seq", None),
            P(("win", "seq")),
        ),
        check_vma=False,
    )
```

```python
import jax
import jax.numpy as jnp
from jax import lax
from jax.sharding import PartitionSpec as P

epsilon = 1e-06
gelu_scale = 0.7978845608028654
gelu_cubic = 0.044715


def with_halo(block, sides, width):
    for axis, dim in sides:
        count = lax.axis_size(axis)
        forward = [(i, i + 1) for i in range(count - 1)]
        backward = [(target, source) for source, target in forward]
        low = lax.ppermute(
            lax.slice_in_dim(block, block.shape[dim] - width, None, axis=dim), axis, forward
        )
        high = lax.ppermute(lax.slice_in_dim(block, 0, width, axis=dim), axis, backward)
        block = jnp.concatenate([low, block, high], axis=dim)
    return block


def gelu_value(inputs):
    inner = gelu_scale * (inputs + gelu_cubic * inputs * inputs * inputs)
    return 0.5 * inputs * (1.0 + jnp.tanh(inner))


def gelu_slope(inputs):
    inner = gelu_scale * (inputs + gelu_cubic * inputs * inputs * inputs)
    tangent = jnp.tanh(inner)
    return 0.5 * (1.0 + tangent) + 0.5 * inputs * (1.0 - tangent * tangent) * gelu_scale * (
        1.0 + 3.0 * gelu_cubic * inputs * inputs
    )


def tap_stack(padded, dilate, rim_width, bin_count, sign):
    slices = [
        lax.dynamic_slice_in_dim(padded, rim_width + sign * (tap_index - 1) * dilate, bin_count, 0)
        for tap_index in range(3)
    ]
    return jnp.concatenate(slices, axis=1)


def flip_channels(values, mirror):
    return jnp.dot(values, mirror, preferred_element_type=jnp.float32).astype(jnp.bfloat16)


def spread_back(back_taps, weight, channels):
    result = jnp.zeros((back_taps.shape[0], channels), jnp.float32)
    for tap_index in range(3):
        result = result + lax.dot_general(
            back_taps[:, tap_index * channels : (tap_index + 1) * channels],
            weight[tap_index],
            (((1,), (1,)), ((), ())),
            preferred_element_type=jnp.float32,
        )
    return result


def halve_sum(blocks, axis):
    size = lax.axis_size(axis)
    if size & (size - 1):
        flat = blocks.reshape((-1,) + blocks.shape[2:])
        return lax.psum_scatter(flat, axis, scatter_dimension=0, tiled=True).reshape(blocks.shape[1:])
    me = lax.axis_index(axis)
    bit = 1
    while bit < size:
        blocks = blocks.reshape((blocks.shape[0] // 2, 2) + blocks.shape[1:])
        mine = (me // bit) % 2
        keep = lax.dynamic_index_in_dim(blocks, mine, 1, keepdims=False)
        send = lax.dynamic_index_in_dim(blocks, 1 - mine, 1, keepdims=False)
        pairs = [(i, i ^ bit) for i in range(size)]
        blocks = keep + lax.ppermute(send, axis, pairs)
        bit *= 2
    return blocks[0]


def halve_step(values, dims, axis, bit, link_type):
    where = dims.index(f"{axis}{bit}")
    mine = (lax.axis_index(axis) // bit) % 2
    keep = lax.dynamic_index_in_dim(values, mine, where, keepdims=False)
    send = lax.dynamic_index_in_dim(values, 1 - mine, where, keepdims=False).astype(link_type)
    size = lax.axis_size(axis)
    got = lax.ppermute(send, axis, [(i, i ^ bit) for i in range(size)])
    return keep + got.astype(keep.dtype), dims[:where] + dims[where + 1 :]


def scatter_sum(term, channels):
    win_count = lax.axis_size("win")
    seq_count = lax.axis_size("seq")
    blocks = term.reshape(win_count, seq_count, -1, channels)
    rows = blocks.shape[2]
    if (win_count & (win_count - 1)) or (seq_count & (seq_count - 1)) or rows % 2:
        return halve_sum(halve_sum(blocks, "win"), "seq")
    win_bits = [("win", 1 << k) for k in range(win_count.bit_length() - 1)]
    seq_bits = [("seq", 1 << k) for k in range(seq_count.bit_length() - 1)]
    names = [f"{a}{b}" for a, b in reversed(win_bits)] + [f"{a}{b}" for a, b in reversed(seq_bits)]
    values = blocks.reshape([2] * len(names) + [rows, channels])
    first, middle, last = win_bits[:1], win_bits[1:], seq_bits
    ways = 2 if len(middle) >= 2 else 1
    dims = list(names)
    for axis, bit in first:
        values, dims = halve_step(values, dims, axis, bit, jnp.float32)
    lead = len(dims)
    parts = values.reshape(values.shape[:lead] + (ways, rows // ways, channels))
    states = [(lax.index_in_dim(parts, part, lead, keepdims=False), list(dims)) for part in range(ways)]
    for step in range(len(middle)):
        for part in range(ways):
            axis, bit = middle[(step + part) % len(middle)]
            states[part] = halve_step(states[part][0], states[part][1], axis, bit, jnp.bfloat16)
    values = jnp.concatenate([part for part, _ in states], axis=-2)
    dims = states[0][1]
    values = values.reshape((seq_count,) + values.shape[len(last) :])
    me = lax.axis_index("seq")
    total = lax.dynamic_index_in_dim(values, me, 0, keepdims=False)
    for shift in range(1, seq_count):
        send = lax.dynamic_index_in_dim(values, (me + shift) % seq_count, 0, keepdims=False)
        got = lax.ppermute(
            send.astype(jnp.bfloat16), "seq", [(i, (i + shift) % seq_count) for i in range(seq_count)]
        )
        total = total + got.astype(jnp.float32)
    return total


def gather_rows(block, axis):
    size = lax.axis_size(axis)
    me = lax.axis_index(axis)
    whole = jnp.zeros((size,) + block.shape, block.dtype)
    whole = lax.dynamic_update_index_in_dim(whole, block, me, 0)
    for shift in range(1, size):
        pairs = [(i, (i + shift) % size) for i in range(size)]
        got = lax.ppermute(block, axis, pairs)
        whole = lax.dynamic_update_index_in_dim(whole, got, (me - shift) % size, 0)
    return whole.reshape((-1,) + block.shape[1:])


def per_device(
    embeddings,
    norm_gain,
    conv_weight,
    conv_bias,
    dilation,
    donor_bins,
    acceptor_bins,
    junction_count,
    donor_proj,
    acceptor_proj,
    out_cotangent,
    score_cotangent,
):
    bin_count = embeddings.shape[1]
    channels = embeddings.shape[2]
    rim_width = bin_count // 2
    dilate = dilation[0]
    lanes = lax.broadcasted_iota(jnp.int32, (channels, channels), 0)
    mirror = (
        lanes + lax.broadcasted_iota(jnp.int32, (channels, channels), 1) == channels - 1
    ).astype(jnp.bfloat16)
    own = slice(rim_width, rim_width + bin_count)

    padded_in = with_halo(jnp.stack([embeddings[0], out_cotangent[0]]), (("seq", 1),), rim_width)
    emb = padded_in[0]
    emb_rev = flip_channels(emb, mirror)
    as_float = emb.astype(jnp.float32)
    inverse = lax.rsqrt(jnp.mean(as_float * as_float, axis=1, keepdims=True) + epsilon)
    normed = as_float * inverse
    normed_rev = emb_rev.astype(jnp.float32) * inverse
    pre_fwd = normed * norm_gain
    pre_rev = normed_rev * norm_gain
    act_fwd = gelu_value(pre_fwd).astype(jnp.bfloat16)
    act_rev = gelu_value(pre_rev).astype(jnp.bfloat16)

    taps_fwd = tap_stack(act_fwd, dilate, rim_width, bin_count, 1)
    taps_rev = tap_stack(act_rev, dilate, rim_width, bin_count, -1)
    conv_all = (
        jnp.dot(
            jnp.concatenate([taps_fwd, taps_rev], axis=0),
            conv_weight.reshape(3 * channels, channels),
            preferred_element_type=jnp.float32,
        )
        + conv_bias
    ).astype(jnp.bfloat16)
    conv_fwd = conv_all[:bin_count]
    conv_rev = flip_channels(conv_all[bin_count:], mirror)
    block_flat = (
        as_float[own] + 0.5 * (conv_fwd.astype(jnp.float32) + conv_rev.astype(jnp.float32))
    ).astype(jnp.bfloat16)

    both_proj = jnp.concatenate([donor_proj, acceptor_proj], axis=1)
    hidden = donor_proj.shape[1]
    window_out = gather_rows(block_flat, "seq")
    block_flat, donor_bins, acceptor_bins, junction_count, score_cotangent = (
        lax.optimization_barrier(
            (block_flat, donor_bins, acceptor_bins, junction_count, score_cotangent)
        )
    )
    window_proj = jnp.dot(window_out, both_proj, preferred_element_type=jnp.float32).astype(
        jnp.bfloat16
    )
    rows_donor = jnp.take(window_proj[:, :hidden], donor_bins[0], axis=0).astype(jnp.float32)
    rows_acceptor = jnp.take(window_proj[:, hidden:], acceptor_bins[0], axis=0).astype(jnp.float32)
    pair_total = donor_bins.shape[1]
    pair_share = pair_total // lax.axis_size("seq")
    pair_first = lax.axis_index("seq") * pair_share
    live_mask = (jnp.arange(pair_total) < junction_count[0]).astype(jnp.float32)
    score_scale = hidden ** (-0.5)
    products = jnp.sum(
        lax.dynamic_slice_in_dim(rows_donor, pair_first, pair_share, 0)
        * lax.dynamic_slice_in_dim(rows_acceptor, pair_first, pair_share, 0),
        axis=1,
    )
    junction_scores = (
        lax.dynamic_slice_in_dim(live_mask, pair_first, pair_share, 0) * products * score_scale
    )[None]
    pair_weight = score_cotangent[0] * live_mask * score_scale
    positions = lax.axis_index("seq") * bin_count - rim_width + jnp.arange(emb.shape[0])
    pick_donor = (positions[:, None] == donor_bins[0][None, :]).astype(jnp.float32)
    pick_acceptor = (positions[:, None] == acceptor_bins[0][None, :]).astype(jnp.float32)
    grad_donor = jnp.dot(
        pick_donor, pair_weight[:, None] * rows_acceptor, precision=lax.Precision.HIGHEST
    ).astype(jnp.bfloat16)
    grad_acceptor = jnp.dot(
        pick_acceptor, pair_weight[:, None] * rows_donor, precision=lax.Precision.HIGHEST
    ).astype(jnp.bfloat16)
    out_grad = padded_in[1].astype(jnp.float32) + lax.dot_general(
        jnp.concatenate([grad_donor, grad_acceptor], axis=1),
        both_proj,
        (((1,), (1,)), ((), ())),
        preferred_element_type=jnp.float32,
    )
    conv_grad = (0.5 * out_grad).astype(jnp.bfloat16)
    conv_grad_rev = flip_channels(conv_grad, mirror)
    back_fwd = tap_stack(conv_grad, dilate, rim_width, bin_count, -1)
    back_rev = tap_stack(conv_grad_rev, dilate, rim_width, bin_count, 1)
    dact_all = spread_back(jnp.concatenate([back_fwd, back_rev], axis=0), conv_weight, channels)
    dact_fwd = dact_all[:bin_count]
    dact_rev = dact_all[bin_count:]
    norm_rev = flip_channels(
        (dact_rev * gelu_slope(pre_rev[own]) * norm_gain).astype(jnp.bfloat16), mirror
    )
    norm_grad = dact_fwd * gelu_slope(pre_fwd[own]) * norm_gain + norm_rev.astype(jnp.float32)
    normed_own = normed[own]
    input_grad = (
        out_grad[own]
        + inverse[own]
        * (norm_grad - normed_own * jnp.mean(norm_grad * normed_own, axis=1, keepdims=True))
    ).astype(jnp.bfloat16)[None]
    grad_term = lax.dot_general(
        jnp.concatenate([act_fwd[own], act_rev[own]], axis=0),
        jnp.concatenate([conv_grad[own], conv_grad_rev[own]], axis=0),
        (((0,), (0,)), ((), ())),
        preferred_element_type=jnp.float32,
    )
    grad_term = grad_term / lax.axis_size("win")
    weight_grad = scatter_sum(grad_term, channels).reshape(-1)
    return (block_flat[None], junction_scores, input_grad, weight_grad)


def solution(mesh):
    return jax.shard_map(
        per_device,
        mesh=mesh,
        in_specs=(
            P("win", "seq", None),
            P(),
            P(),
            P(),
            P("win"),
            P("win", None),
            P("win", None),
            P("win"),
            P(),
            P(),
            P("win", "seq", None),
            P("win", None),
        ),
        out_specs=(
            P("win", "seq", None),
            P("win", "seq"),
            P("win", "seq", None),
            P(("win", "seq")),
        ),
        check_vma=False,
    )
```

```python
import jax
import jax.numpy as jnp
from jax import lax
from jax.sharding import PartitionSpec as P

epsilon = 1e-06
gelu_scale = 0.7978845608028654
gelu_cubic = 0.044715


def with_halo(block, sides, width):
    for axis, dim in sides:
        count = lax.axis_size(axis)
        forward = [(i, i + 1) for i in range(count - 1)]
        backward = [(target, source) for source, target in forward]
        low = lax.ppermute(
            lax.slice_in_dim(block, block.shape[dim] - width, None, axis=dim), axis, forward
        )
        high = lax.ppermute(lax.slice_in_dim(block, 0, width, axis=dim), axis, backward)
        block = jnp.concatenate([low, block, high], axis=dim)
    return block


def gelu_value(inputs):
    inner = gelu_scale * (inputs + gelu_cubic * inputs * inputs * inputs)
    return 0.5 * inputs * (1.0 + jnp.tanh(inner))


def gelu_slope(inputs):
    inner = gelu_scale * (inputs + gelu_cubic * inputs * inputs * inputs)
    tangent = jnp.tanh(inner)
    return 0.5 * (1.0 + tangent) + 0.5 * inputs * (1.0 - tangent * tangent) * gelu_scale * (
        1.0 + 3.0 * gelu_cubic * inputs * inputs
    )


def tap_stack(padded, dilate, rim_width, bin_count, sign):
    slices = [
        lax.dynamic_slice_in_dim(padded, rim_width + sign * (tap_index - 1) * dilate, bin_count, 0)
        for tap_index in range(3)
    ]
    return jnp.concatenate(slices, axis=1)


def flip_channels(values, mirror):
    return jnp.dot(values, mirror, preferred_element_type=jnp.float32).astype(jnp.bfloat16)


def spread_back(back_taps, weight, channels):
    result = jnp.zeros((back_taps.shape[0], channels), jnp.float32)
    for tap_index in range(3):
        result = result + lax.dot_general(
            back_taps[:, tap_index * channels : (tap_index + 1) * channels],
            weight[tap_index],
            (((1,), (1,)), ((), ())),
            preferred_element_type=jnp.float32,
        )
    return result


def halve_sum(blocks, axis):
    size = lax.axis_size(axis)
    if size & (size - 1):
        flat = blocks.reshape((-1,) + blocks.shape[2:])
        return lax.psum_scatter(flat, axis, scatter_dimension=0, tiled=True).reshape(blocks.shape[1:])
    me = lax.axis_index(axis)
    bit = 1
    while bit < size:
        blocks = blocks.reshape((blocks.shape[0] // 2, 2) + blocks.shape[1:])
        mine = (me // bit) % 2
        keep = lax.dynamic_index_in_dim(blocks, mine, 1, keepdims=False)
        send = lax.dynamic_index_in_dim(blocks, 1 - mine, 1, keepdims=False)
        pairs = [(i, i ^ bit) for i in range(size)]
        blocks = keep + lax.ppermute(send, axis, pairs)
        bit *= 2
    return blocks[0]


def halve_step(values, dims, axis, bit, link_type):
    where = dims.index(f"{axis}{bit}")
    mine = (lax.axis_index(axis) // bit) % 2
    keep = lax.dynamic_index_in_dim(values, mine, where, keepdims=False)
    send = lax.dynamic_index_in_dim(values, 1 - mine, where, keepdims=False).astype(link_type)
    size = lax.axis_size(axis)
    got = lax.ppermute(send, axis, [(i, i ^ bit) for i in range(size)])
    return keep + got.astype(keep.dtype), dims[:where] + dims[where + 1 :]


def scatter_sum(term, channels):
    win_count = lax.axis_size("win")
    seq_count = lax.axis_size("seq")
    blocks = term.reshape(win_count, seq_count, -1, channels)
    rows = blocks.shape[2]
    if (win_count & (win_count - 1)) or (seq_count & (seq_count - 1)) or rows % 2:
        return halve_sum(halve_sum(blocks, "win"), "seq")
    win_bits = [("win", 1 << k) for k in range(win_count.bit_length() - 1)]
    seq_bits = [("seq", 1 << k) for k in range(seq_count.bit_length() - 1)]
    names = [f"{a}{b}" for a, b in reversed(win_bits)] + [f"{a}{b}" for a, b in reversed(seq_bits)]
    values = blocks.reshape([2] * len(names) + [rows, channels])
    first, middle, last = win_bits[:1], win_bits[1:], seq_bits
    ways = 2 if len(middle) >= 2 else 1
    dims = list(names)
    for axis, bit in first:
        values, dims = halve_step(values, dims, axis, bit, jnp.float32)
    lead = len(dims)
    parts = values.reshape(values.shape[:lead] + (ways, rows // ways, channels))
    states = [(lax.index_in_dim(parts, part, lead, keepdims=False), list(dims)) for part in range(ways)]
    for step in range(len(middle)):
        for part in range(ways):
            axis, bit = middle[(step + part) % len(middle)]
            states[part] = halve_step(states[part][0], states[part][1], axis, bit, jnp.bfloat16)
    values = jnp.concatenate([part for part, _ in states], axis=-2)
    dims = states[0][1]
    for axis, bit in last:
        values, dims = halve_step(values, dims, axis, bit, jnp.bfloat16)
    return values


def gather_rows(block, axis):
    size = lax.axis_size(axis)
    me = lax.axis_index(axis)
    whole = jnp.zeros((size,) + block.shape, block.dtype)
    whole = lax.dynamic_update_index_in_dim(whole, block, me, 0)
    for shift in range(1, size):
        pairs = [(i, (i + shift) % size) for i in range(size)]
        got = lax.ppermute(block, axis, pairs)
        whole = lax.dynamic_update_index_in_dim(whole, got, (me - shift) % size, 0)
    return whole.reshape((-1,) + block.shape[1:])


def per_device(
    embeddings,
    norm_gain,
    conv_weight,
    conv_bias,
    dilation,
    donor_bins,
    acceptor_bins,
    junction_count,
    donor_proj,
    acceptor_proj,
    out_cotangent,
    score_cotangent,
):
    bin_count = embeddings.shape[1]
    channels = embeddings.shape[2]
    rim_width = bin_count // 2
    dilate = dilation[0]
    lanes = lax.broadcasted_iota(jnp.int32, (channels, channels), 0)
    mirror = (
        lanes + lax.broadcasted_iota(jnp.int32, (channels, channels), 1) == channels - 1
    ).astype(jnp.bfloat16)
    own = slice(rim_width, rim_width + bin_count)

    padded_in = with_halo(jnp.stack([embeddings[0], out_cotangent[0]]), (("seq", 1),), rim_width)
    emb = padded_in[0]
    emb_rev = flip_channels(emb, mirror)
    as_float = emb.astype(jnp.float32)
    inverse = lax.rsqrt(jnp.mean(as_float * as_float, axis=1, keepdims=True) + epsilon)
    normed = as_float * inverse
    normed_rev = emb_rev.astype(jnp.float32) * inverse
    pre_fwd = normed * norm_gain
    pre_rev = normed_rev * norm_gain
    act_fwd = gelu_value(pre_fwd).astype(jnp.bfloat16)
    act_rev = gelu_value(pre_rev).astype(jnp.bfloat16)

    taps_fwd = tap_stack(act_fwd, dilate, rim_width, bin_count, 1)
    taps_rev = tap_stack(act_rev, dilate, rim_width, bin_count, -1)
    conv_all = (
        jnp.dot(
            jnp.concatenate([taps_fwd, taps_rev], axis=0),
            conv_weight.reshape(3 * channels, channels),
            preferred_element_type=jnp.float32,
        )
        + conv_bias
    ).astype(jnp.bfloat16)
    conv_fwd = conv_all[:bin_count]
    conv_rev = flip_channels(conv_all[bin_count:], mirror)
    block_flat = (
        as_float[own] + 0.5 * (conv_fwd.astype(jnp.float32) + conv_rev.astype(jnp.float32))
    ).astype(jnp.bfloat16)

    both_proj = jnp.concatenate([donor_proj, acceptor_proj], axis=1)
    hidden = donor_proj.shape[1]
    window_out = gather_rows(block_flat, "seq")
    window_proj = jnp.dot(window_out, both_proj, preferred_element_type=jnp.float32).astype(
        jnp.bfloat16
    )
    rows_donor = jnp.take(window_proj[:, :hidden], donor_bins[0], axis=0).astype(jnp.float32)
    rows_acceptor = jnp.take(window_proj[:, hidden:], acceptor_bins[0], axis=0).astype(jnp.float32)
    pair_total = donor_bins.shape[1]
    pair_share = pair_total // lax.axis_size("seq")
    pair_first = lax.axis_index("seq") * pair_share
    live_mask = (jnp.arange(pair_total) < junction_count[0]).astype(jnp.float32)
    score_scale = hidden ** (-0.5)
    products = jnp.sum(
        lax.dynamic_slice_in_dim(rows_donor, pair_first, pair_share, 0)
        * lax.dynamic_slice_in_dim(rows_acceptor, pair_first, pair_share, 0),
        axis=1,
    )
    junction_scores = (
        lax.dynamic_slice_in_dim(live_mask, pair_first, pair_share, 0) * products * score_scale
    )[None]
    pair_weight = score_cotangent[0] * live_mask * score_scale
    positions = lax.axis_index("seq") * bin_count - rim_width + jnp.arange(emb.shape[0])
    pick_donor = (positions[:, None] == donor_bins[0][None, :]).astype(jnp.float32)
    pick_acceptor = (positions[:, None] == acceptor_bins[0][None, :]).astype(jnp.float32)
    grad_donor = jnp.dot(
        pick_donor, pair_weight[:, None] * rows_acceptor, precision=lax.Precision.HIGHEST
    ).astype(jnp.bfloat16)
    grad_acceptor = jnp.dot(
        pick_acceptor, pair_weight[:, None] * rows_donor, precision=lax.Precision.HIGHEST
    ).astype(jnp.bfloat16)
    out_grad = padded_in[1].astype(jnp.float32) + lax.dot_general(
        jnp.concatenate([grad_donor, grad_acceptor], axis=1),
        both_proj,
        (((1,), (1,)), ((), ())),
        preferred_element_type=jnp.float32,
    )
    conv_grad = (0.5 * out_grad).astype(jnp.bfloat16)
    conv_grad_rev = flip_channels(conv_grad, mirror)
    back_fwd = tap_stack(conv_grad, dilate, rim_width, bin_count, -1)
    back_rev = tap_stack(conv_grad_rev, dilate, rim_width, bin_count, 1)
    dact_all = spread_back(jnp.concatenate([back_fwd, back_rev], axis=0), conv_weight, channels)
    dact_fwd = dact_all[:bin_count]
    dact_rev = dact_all[bin_count:]
    norm_rev = flip_channels(
        (dact_rev * gelu_slope(pre_rev[own]) * norm_gain).astype(jnp.bfloat16), mirror
    )
    norm_grad = dact_fwd * gelu_slope(pre_fwd[own]) * norm_gain + norm_rev.astype(jnp.float32)
    normed_own = normed[own]
    input_grad = (
        out_grad[own]
        + inverse[own]
        * (norm_grad - normed_own * jnp.mean(norm_grad * normed_own, axis=1, keepdims=True))
    ).astype(jnp.bfloat16)[None]
    grad_term = lax.dot_general(
        jnp.concatenate([act_fwd[own], act_rev[own]], axis=0),
        jnp.concatenate([conv_grad[own], conv_grad_rev[own]], axis=0),
        (((0,), (0,)), ((), ())),
        preferred_element_type=jnp.float32,
    )
    grad_term = grad_term / lax.axis_size("win")
    weight_grad = scatter_sum(grad_term, channels).reshape(-1)
    return (block_flat[None], junction_scores, input_grad, weight_grad)


def solution(mesh):
    return jax.shard_map(
        per_device,
        mesh=mesh,
        in_specs=(
            P("win", "seq", None),
            P(),
            P(),
            P(),
            P("win"),
            P("win", None),
            P("win", None),
            P("win"),
            P(),
            P(),
            P("win", "seq", None),
            P("win", None),
        ),
        out_specs=(
            P("win", "seq", None),
            P("win", "seq"),
            P("win", "seq", None),
            P(("win", "seq")),
        ),
        check_vma=False,
    )
```

```python
import jax
import jax.numpy as jnp
from jax import lax
from jax.sharding import PartitionSpec as P

epsilon = 1e-06
gelu_scale = 0.7978845608028654
gelu_cubic = 0.044715


def with_halo(block, sides, width):
    for axis, dim in sides:
        count = lax.axis_size(axis)
        forward = [(i, i + 1) for i in range(count - 1)]
        backward = [(target, source) for source, target in forward]
        low = lax.ppermute(
            lax.slice_in_dim(block, block.shape[dim] - width, None, axis=dim), axis, forward
        )
        high = lax.ppermute(lax.slice_in_dim(block, 0, width, axis=dim), axis, backward)
        block = jnp.concatenate([low, block, high], axis=dim)
    return block


def gelu_value(inputs):
    inner = gelu_scale * (inputs + gelu_cubic * inputs * inputs * inputs)
    return 0.5 * inputs * (1.0 + jnp.tanh(inner))


def gelu_slope(inputs):
    inner = gelu_scale * (inputs + gelu_cubic * inputs * inputs * inputs)
    tangent = jnp.tanh(inner)
    return 0.5 * (1.0 + tangent) + 0.5 * inputs * (1.0 - tangent * tangent) * gelu_scale * (
        1.0 + 3.0 * gelu_cubic * inputs * inputs
    )


def tap_stack(padded, dilate, rim_width, bin_count, sign):
    slices = [
        lax.dynamic_slice_in_dim(padded, rim_width + sign * (tap_index - 1) * dilate, bin_count, 0)
        for tap_index in range(3)
    ]
    return jnp.concatenate(slices, axis=1)


def flip_channels(values, mirror):
    return jnp.dot(values, mirror, preferred_element_type=jnp.float32).astype(jnp.bfloat16)


def spread_back(back_taps, weight, channels):
    result = jnp.zeros((back_taps.shape[0], channels), jnp.float32)
    for tap_index in range(3):
        result = result + lax.dot_general(
            back_taps[:, tap_index * channels : (tap_index + 1) * channels],
            weight[tap_index],
            (((1,), (1,)), ((), ())),
            preferred_element_type=jnp.float32,
        )
    return result


def halve_sum(blocks, axis):
    size = lax.axis_size(axis)
    if size & (size - 1):
        flat = blocks.reshape((-1,) + blocks.shape[2:])
        return lax.psum_scatter(flat, axis, scatter_dimension=0, tiled=True).reshape(blocks.shape[1:])
    me = lax.axis_index(axis)
    bit = 1
    while bit < size:
        blocks = blocks.reshape((blocks.shape[0] // 2, 2) + blocks.shape[1:])
        mine = (me // bit) % 2
        keep = lax.dynamic_index_in_dim(blocks, mine, 1, keepdims=False)
        send = lax.dynamic_index_in_dim(blocks, 1 - mine, 1, keepdims=False)
        pairs = [(i, i ^ bit) for i in range(size)]
        blocks = keep + lax.ppermute(send, axis, pairs)
        bit *= 2
    return blocks[0]


def halve_step(values, dims, axis, bit, link_type):
    where = dims.index(f"{axis}{bit}")
    mine = (lax.axis_index(axis) // bit) % 2
    keep = lax.dynamic_index_in_dim(values, mine, where, keepdims=False)
    send = lax.dynamic_index_in_dim(values, 1 - mine, where, keepdims=False).astype(link_type)
    size = lax.axis_size(axis)
    got = lax.ppermute(send, axis, [(i, i ^ bit) for i in range(size)])
    return keep + got.astype(keep.dtype), dims[:where] + dims[where + 1 :]


def scatter_sum(term, channels):
    win_count = lax.axis_size("win")
    seq_count = lax.axis_size("seq")
    blocks = term.reshape(win_count, seq_count, -1, channels)
    rows = blocks.shape[2]
    if (win_count & (win_count - 1)) or (seq_count & (seq_count - 1)) or rows % 2:
        return halve_sum(halve_sum(blocks, "win"), "seq")
    win_bits = [("win", 1 << k) for k in range(win_count.bit_length() - 1)]
    seq_bits = [("seq", 1 << k) for k in range(seq_count.bit_length() - 1)]
    names = [f"{a}{b}" for a, b in reversed(win_bits)] + [f"{a}{b}" for a, b in reversed(seq_bits)]
    values = blocks.reshape([2] * len(names) + [rows, channels])
    first, middle, last = win_bits[:1], win_bits[1:], seq_bits
    ways = 2 if len(middle) >= 2 else 1
    dims = list(names)
    for axis, bit in first:
        values, dims = halve_step(values, dims, axis, bit, jnp.float32)
    lead = len(dims)
    parts = values.reshape(values.shape[:lead] + (ways, rows // ways, channels))
    states = [(lax.index_in_dim(parts, part, lead, keepdims=False), list(dims)) for part in range(ways)]
    for step in range(len(middle)):
        for part in range(ways):
            axis, bit = middle[(step + part) % len(middle)]
            states[part] = halve_step(states[part][0], states[part][1], axis, bit, jnp.bfloat16)
    values = jnp.concatenate([part for part, _ in states], axis=-2)
    dims = states[0][1]
    values = values.reshape((seq_count,) + values.shape[len(last) :])
    me = lax.axis_index("seq")
    total = lax.dynamic_index_in_dim(values, me, 0, keepdims=False)
    for shift in range(1, seq_count):
        send = lax.dynamic_index_in_dim(values, (me + shift) % seq_count, 0, keepdims=False)
        got = lax.ppermute(
            send.astype(jnp.bfloat16), "seq", [(i, (i + shift) % seq_count) for i in range(seq_count)]
        )
        total = total + got.astype(jnp.float32)
    return total


def gather_rows(block, axis):
    size = lax.axis_size(axis)
    me = lax.axis_index(axis)
    whole = jnp.zeros((size,) + block.shape, block.dtype)
    whole = lax.dynamic_update_index_in_dim(whole, block, me, 0)
    for shift in range(1, size):
        pairs = [(i, (i + shift) % size) for i in range(size)]
        got = lax.ppermute(block, axis, pairs)
        whole = lax.dynamic_update_index_in_dim(whole, got, (me - shift) % size, 0)
    return whole.reshape((-1,) + block.shape[1:])


def per_device(
    embeddings,
    norm_gain,
    conv_weight,
    conv_bias,
    dilation,
    donor_bins,
    acceptor_bins,
    junction_count,
    donor_proj,
    acceptor_proj,
    out_cotangent,
    score_cotangent,
):
    bin_count = embeddings.shape[1]
    channels = embeddings.shape[2]
    rim_width = bin_count // 2
    dilate = dilation[0]
    lanes = lax.broadcasted_iota(jnp.int32, (channels, channels), 0)
    mirror = (
        lanes + lax.broadcasted_iota(jnp.int32, (channels, channels), 1) == channels - 1
    ).astype(jnp.bfloat16)
    own = slice(rim_width, rim_width + bin_count)

    seq_count = lax.axis_size("seq")
    upward = [(i, i + 1) for i in range(seq_count - 1)]
    downward = [(target, source) for source, target in upward]
    low = lax.ppermute(
        jnp.stack([embeddings[0, -rim_width:], out_cotangent[0, -rim_width:]]), "seq", upward
    )
    high = lax.ppermute(
        jnp.stack([embeddings[0, :rim_width], out_cotangent[0, :rim_width]]), "seq", downward
    )
    emb = jnp.concatenate([low[0], embeddings[0], high[0]])
    cot_pad = jnp.concatenate([low[1], out_cotangent[0], high[1]])
    emb_rev = flip_channels(emb, mirror)
    as_float = emb.astype(jnp.float32)
    inverse = lax.rsqrt(jnp.mean(as_float * as_float, axis=1, keepdims=True) + epsilon)
    normed = as_float * inverse
    normed_rev = emb_rev.astype(jnp.float32) * inverse
    pre_fwd = normed * norm_gain
    pre_rev = normed_rev * norm_gain
    act_fwd = gelu_value(pre_fwd).astype(jnp.bfloat16)
    act_rev = gelu_value(pre_rev).astype(jnp.bfloat16)

    taps_fwd = tap_stack(act_fwd, dilate, rim_width, bin_count, 1)
    taps_rev = tap_stack(act_rev, dilate, rim_width, bin_count, -1)
    conv_all = (
        jnp.dot(
            jnp.concatenate([taps_fwd, taps_rev], axis=0),
            conv_weight.reshape(3 * channels, channels),
            preferred_element_type=jnp.float32,
        )
        + conv_bias
    ).astype(jnp.bfloat16)
    conv_fwd = conv_all[:bin_count]
    conv_rev = flip_channels(conv_all[bin_count:], mirror)
    block_flat = (
        as_float[own] + 0.5 * (conv_fwd.astype(jnp.float32) + conv_rev.astype(jnp.float32))
    ).astype(jnp.bfloat16)

    both_proj = jnp.concatenate([donor_proj, acceptor_proj], axis=1)
    hidden = donor_proj.shape[1]
    window_out = gather_rows(block_flat, "seq")
    window_proj = jnp.dot(window_out, both_proj, preferred_element_type=jnp.float32).astype(
        jnp.bfloat16
    )
    rows_donor = jnp.take(window_proj[:, :hidden], donor_bins[0], axis=0).astype(jnp.float32)
    rows_acceptor = jnp.take(window_proj[:, hidden:], acceptor_bins[0], axis=0).astype(jnp.float32)
    pair_total = donor_bins.shape[1]
    pair_share = pair_total // lax.axis_size("seq")
    pair_first = lax.axis_index("seq") * pair_share
    live_mask = (jnp.arange(pair_total) < junction_count[0]).astype(jnp.float32)
    score_scale = hidden ** (-0.5)
    products = jnp.sum(
        lax.dynamic_slice_in_dim(rows_donor, pair_first, pair_share, 0)
        * lax.dynamic_slice_in_dim(rows_acceptor, pair_first, pair_share, 0),
        axis=1,
    )
    junction_scores = (
        lax.dynamic_slice_in_dim(live_mask, pair_first, pair_share, 0) * products * score_scale
    )[None]
    pair_weight = score_cotangent[0] * live_mask * score_scale
    positions = lax.axis_index("seq") * bin_count - rim_width + jnp.arange(emb.shape[0])
    pick_donor = (positions[:, None] == donor_bins[0][None, :]).astype(jnp.float32)
    pick_acceptor = (positions[:, None] == acceptor_bins[0][None, :]).astype(jnp.float32)
    grad_donor = jnp.dot(
        pick_donor, pair_weight[:, None] * rows_acceptor, precision=lax.Precision.HIGHEST
    ).astype(jnp.bfloat16)
    grad_acceptor = jnp.dot(
        pick_acceptor, pair_weight[:, None] * rows_donor, precision=lax.Precision.HIGHEST
    ).astype(jnp.bfloat16)
    out_grad = cot_pad.astype(jnp.float32) + lax.dot_general(
        jnp.concatenate([grad_donor, grad_acceptor], axis=1),
        both_proj,
        (((1,), (1,)), ((), ())),
        preferred_element_type=jnp.float32,
    )
    conv_grad = (0.5 * out_grad).astype(jnp.bfloat16)
    conv_grad_rev = flip_channels(conv_grad, mirror)
    back_fwd = tap_stack(conv_grad, dilate, rim_width, bin_count, -1)
    back_rev = tap_stack(conv_grad_rev, dilate, rim_width, bin_count, 1)
    dact_all = spread_back(jnp.concatenate([back_fwd, back_rev], axis=0), conv_weight, channels)
    dact_fwd = dact_all[:bin_count]
    dact_rev = dact_all[bin_count:]
    norm_rev = flip_channels(
        (dact_rev * gelu_slope(pre_rev[own]) * norm_gain).astype(jnp.bfloat16), mirror
    )
    norm_grad = dact_fwd * gelu_slope(pre_fwd[own]) * norm_gain + norm_rev.astype(jnp.float32)
    normed_own = normed[own]
    input_grad = (
        out_grad[own]
        + inverse[own]
        * (norm_grad - normed_own * jnp.mean(norm_grad * normed_own, axis=1, keepdims=True))
    ).astype(jnp.bfloat16)[None]
    grad_term = lax.dot_general(
        jnp.concatenate([act_fwd[own], act_rev[own]], axis=0),
        jnp.concatenate([conv_grad[own], conv_grad_rev[own]], axis=0),
        (((0,), (0,)), ((), ())),
        preferred_element_type=jnp.float32,
    )
    grad_term = grad_term / lax.axis_size("win")
    weight_grad = scatter_sum(grad_term, channels).reshape(-1)
    return (block_flat[None], junction_scores, input_grad, weight_grad)


def solution(mesh):
    return jax.shard_map(
        per_device,
        mesh=mesh,
        in_specs=(
            P("win", "seq", None),
            P(),
            P(),
            P(),
            P("win"),
            P("win", None),
            P("win", None),
            P("win"),
            P(),
            P(),
            P("win", "seq", None),
            P("win", None),
        ),
        out_specs=(
            P("win", "seq", None),
            P("win", "seq"),
            P("win", "seq", None),
            P(("win", "seq")),
        ),
        check_vma=False,
    )
```

```python
import jax
import jax.numpy as jnp
from jax import lax
from jax.sharding import PartitionSpec as P

epsilon = 1e-06
gelu_scale = 0.7978845608028654
gelu_cubic = 0.044715


def with_halo(block, sides, width):
    for axis, dim in sides:
        count = lax.axis_size(axis)
        forward = [(i, i + 1) for i in range(count - 1)]
        backward = [(target, source) for source, target in forward]
        low = lax.ppermute(
            lax.slice_in_dim(block, block.shape[dim] - width, None, axis=dim), axis, forward
        )
        high = lax.ppermute(lax.slice_in_dim(block, 0, width, axis=dim), axis, backward)
        block = jnp.concatenate([low, block, high], axis=dim)
    return block


def gelu_value(inputs):
    inner = gelu_scale * (inputs + gelu_cubic * inputs * inputs * inputs)
    return 0.5 * inputs * (1.0 + jnp.tanh(inner))


def gelu_slope(inputs):
    inner = gelu_scale * (inputs + gelu_cubic * inputs * inputs * inputs)
    tangent = jnp.tanh(inner)
    return 0.5 * (1.0 + tangent) + 0.5 * inputs * (1.0 - tangent * tangent) * gelu_scale * (
        1.0 + 3.0 * gelu_cubic * inputs * inputs
    )


def tap_stack(padded, dilate, rim_width, bin_count, sign):
    slices = [
        lax.dynamic_slice_in_dim(padded, rim_width + sign * (tap_index - 1) * dilate, bin_count, 0)
        for tap_index in range(3)
    ]
    return jnp.concatenate(slices, axis=1)


def flip_channels(values, mirror):
    return jnp.dot(values, mirror, preferred_element_type=jnp.float32).astype(jnp.bfloat16)


def spread_back(back_taps, weight, channels):
    result = jnp.zeros((back_taps.shape[0], channels), jnp.float32)
    for tap_index in range(3):
        result = result + lax.dot_general(
            back_taps[:, tap_index * channels : (tap_index + 1) * channels],
            weight[tap_index],
            (((1,), (1,)), ((), ())),
            preferred_element_type=jnp.float32,
        )
    return result


def halve_sum(blocks, axis):
    size = lax.axis_size(axis)
    if size & (size - 1):
        flat = blocks.reshape((-1,) + blocks.shape[2:])
        return lax.psum_scatter(flat, axis, scatter_dimension=0, tiled=True).reshape(blocks.shape[1:])
    me = lax.axis_index(axis)
    bit = 1
    while bit < size:
        blocks = blocks.reshape((blocks.shape[0] // 2, 2) + blocks.shape[1:])
        mine = (me // bit) % 2
        keep = lax.dynamic_index_in_dim(blocks, mine, 1, keepdims=False)
        send = lax.dynamic_index_in_dim(blocks, 1 - mine, 1, keepdims=False)
        pairs = [(i, i ^ bit) for i in range(size)]
        blocks = keep + lax.ppermute(send, axis, pairs)
        bit *= 2
    return blocks[0]


def halve_step(values, dims, axis, bit, link_type):
    where = dims.index(f"{axis}{bit}")
    mine = (lax.axis_index(axis) // bit) % 2
    keep = lax.dynamic_index_in_dim(values, mine, where, keepdims=False)
    send = lax.dynamic_index_in_dim(values, 1 - mine, where, keepdims=False).astype(link_type)
    size = lax.axis_size(axis)
    got = lax.ppermute(send, axis, [(i, i ^ bit) for i in range(size)])
    return keep + got.astype(keep.dtype), dims[:where] + dims[where + 1 :]


def scatter_sum(term, channels):
    win_count = lax.axis_size("win")
    seq_count = lax.axis_size("seq")
    blocks = term.reshape(win_count, seq_count, -1, channels)
    rows = blocks.shape[2]
    if (win_count & (win_count - 1)) or (seq_count & (seq_count - 1)) or rows % 3:
        return halve_sum(halve_sum(blocks, "win"), "seq")
    win_bits = [("win", 1 << k) for k in range(win_count.bit_length() - 1)]
    seq_bits = [("seq", 1 << k) for k in range(seq_count.bit_length() - 1)]
    names = [f"{a}{b}" for a, b in reversed(win_bits)] + [f"{a}{b}" for a, b in reversed(seq_bits)]
    values = blocks.reshape([2] * len(names) + [rows, channels])
    first, middle = win_bits[:1], win_bits[1:] + seq_bits[:1]
    parts = values.reshape(values.shape[: len(names)] + (3, rows // 3, channels))
    states = [(lax.index_in_dim(parts, part, len(names), keepdims=False), list(names)) for part in range(3)]
    for part in range(3):
        for axis, bit in first:
            states[part] = halve_step(states[part][0], states[part][1], axis, bit, jnp.float32)
    for step in range(len(middle)):
        for part in range(3):
            axis, bit = middle[(step + part) % len(middle)]
            states[part] = halve_step(states[part][0], states[part][1], axis, bit, jnp.bfloat16)
    values = jnp.concatenate([part for part, _ in states], axis=-2)
    dims = states[0][1]
    last = seq_bits[1:]
    for axis, bit in last:
        values, dims = halve_step(values, dims, axis, bit, jnp.bfloat16)
    return values


def gather_rows(block, axis):
    size = lax.axis_size(axis)
    me = lax.axis_index(axis)
    whole = jnp.zeros((size,) + block.shape, block.dtype)
    whole = lax.dynamic_update_index_in_dim(whole, block, me, 0)
    for shift in range(1, size):
        pairs = [(i, (i + shift) % size) for i in range(size)]
        got = lax.ppermute(block, axis, pairs)
        whole = lax.dynamic_update_index_in_dim(whole, got, (me - shift) % size, 0)
    return whole.reshape((-1,) + block.shape[1:])


def per_device(
    embeddings,
    norm_gain,
    conv_weight,
    conv_bias,
    dilation,
    donor_bins,
    acceptor_bins,
    junction_count,
    donor_proj,
    acceptor_proj,
    out_cotangent,
    score_cotangent,
):
    bin_count = embeddings.shape[1]
    channels = embeddings.shape[2]
    rim_width = bin_count // 2
    dilate = dilation[0]
    lanes = lax.broadcasted_iota(jnp.int32, (channels, channels), 0)
    mirror = (
        lanes + lax.broadcasted_iota(jnp.int32, (channels, channels), 1) == channels - 1
    ).astype(jnp.bfloat16)
    own = slice(rim_width, rim_width + bin_count)

    padded_in = with_halo(jnp.stack([embeddings[0], out_cotangent[0]]), (("seq", 1),), rim_width)
    emb = padded_in[0]
    emb_rev = flip_channels(emb, mirror)
    as_float = emb.astype(jnp.float32)
    inverse = lax.rsqrt(jnp.mean(as_float * as_float, axis=1, keepdims=True) + epsilon)
    normed = as_float * inverse
    normed_rev = emb_rev.astype(jnp.float32) * inverse
    pre_fwd = normed * norm_gain
    pre_rev = normed_rev * norm_gain
    act_fwd = gelu_value(pre_fwd).astype(jnp.bfloat16)
    act_rev = gelu_value(pre_rev).astype(jnp.bfloat16)

    taps_fwd = tap_stack(act_fwd, dilate, rim_width, bin_count, 1)
    taps_rev = tap_stack(act_rev, dilate, rim_width, bin_count, -1)
    conv_all = (
        jnp.dot(
            jnp.concatenate([taps_fwd, taps_rev], axis=0),
            conv_weight.reshape(3 * channels, channels),
            preferred_element_type=jnp.float32,
        )
        + conv_bias
    ).astype(jnp.bfloat16)
    conv_fwd = conv_all[:bin_count]
    conv_rev = flip_channels(conv_all[bin_count:], mirror)
    block_flat = (
        as_float[own] + 0.5 * (conv_fwd.astype(jnp.float32) + conv_rev.astype(jnp.float32))
    ).astype(jnp.bfloat16)

    both_proj = jnp.concatenate([donor_proj, acceptor_proj], axis=1)
    hidden = donor_proj.shape[1]
    window_out = gather_rows(block_flat, "seq")
    window_proj = jnp.dot(window_out, both_proj, preferred_element_type=jnp.float32).astype(
        jnp.bfloat16
    )
    rows_donor = jnp.take(window_proj[:, :hidden], donor_bins[0], axis=0).astype(jnp.float32)
    rows_acceptor = jnp.take(window_proj[:, hidden:], acceptor_bins[0], axis=0).astype(jnp.float32)
    pair_total = donor_bins.shape[1]
    pair_share = pair_total // lax.axis_size("seq")
    pair_first = lax.axis_index("seq") * pair_share
    live_mask = (jnp.arange(pair_total) < junction_count[0]).astype(jnp.float32)
    score_scale = hidden ** (-0.5)
    products = jnp.sum(
        lax.dynamic_slice_in_dim(rows_donor, pair_first, pair_share, 0)
        * lax.dynamic_slice_in_dim(rows_acceptor, pair_first, pair_share, 0),
        axis=1,
    )
    junction_scores = (
        lax.dynamic_slice_in_dim(live_mask, pair_first, pair_share, 0) * products * score_scale
    )[None]
    pair_weight = score_cotangent[0] * live_mask * score_scale
    positions = lax.axis_index("seq") * bin_count - rim_width + jnp.arange(emb.shape[0])
    pick_donor = (positions[:, None] == donor_bins[0][None, :]).astype(jnp.float32)
    pick_acceptor = (positions[:, None] == acceptor_bins[0][None, :]).astype(jnp.float32)
    grad_donor = jnp.dot(
        pick_donor, pair_weight[:, None] * rows_acceptor, precision=lax.Precision.HIGHEST
    ).astype(jnp.bfloat16)
    grad_acceptor = jnp.dot(
        pick_acceptor, pair_weight[:, None] * rows_donor, precision=lax.Precision.HIGHEST
    ).astype(jnp.bfloat16)
    out_grad = padded_in[1].astype(jnp.float32) + lax.dot_general(
        jnp.concatenate([grad_donor, grad_acceptor], axis=1),
        both_proj,
        (((1,), (1,)), ((), ())),
        preferred_element_type=jnp.float32,
    )
    conv_grad = (0.5 * out_grad).astype(jnp.bfloat16)
    conv_grad_rev = flip_channels(conv_grad, mirror)
    back_fwd = tap_stack(conv_grad, dilate, rim_width, bin_count, -1)
    back_rev = tap_stack(conv_grad_rev, dilate, rim_width, bin_count, 1)
    dact_all = spread_back(jnp.concatenate([back_fwd, back_rev], axis=0), conv_weight, channels)
    dact_fwd = dact_all[:bin_count]
    dact_rev = dact_all[bin_count:]
    norm_rev = flip_channels(
        (dact_rev * gelu_slope(pre_rev[own]) * norm_gain).astype(jnp.bfloat16), mirror
    )
    norm_grad = dact_fwd * gelu_slope(pre_fwd[own]) * norm_gain + norm_rev.astype(jnp.float32)
    normed_own = normed[own]
    input_grad = (
        out_grad[own]
        + inverse[own]
        * (norm_grad - normed_own * jnp.mean(norm_grad * normed_own, axis=1, keepdims=True))
    ).astype(jnp.bfloat16)[None]
    grad_term = lax.dot_general(
        jnp.concatenate([act_fwd[own], act_rev[own]], axis=0),
        jnp.concatenate([conv_grad[own], conv_grad_rev[own]], axis=0),
        (((0,), (0,)), ((), ())),
        preferred_element_type=jnp.float32,
    )
    grad_term = grad_term / lax.axis_size("win")
    weight_grad = scatter_sum(grad_term, channels).reshape(-1)
    return (block_flat[None], junction_scores, input_grad, weight_grad)


def solution(mesh):
    return jax.shard_map(
        per_device,
        mesh=mesh,
        in_specs=(
            P("win", "seq", None),
            P(),
            P(),
            P(),
            P("win"),
            P("win", None),
            P("win", None),
            P("win"),
            P(),
            P(),
            P("win", "seq", None),
            P("win", None),
        ),
        out_specs=(
            P("win", "seq", None),
            P("win", "seq"),
            P("win", "seq", None),
            P(("win", "seq")),
        ),
        check_vma=False,
    )
```

```python
import jax
import jax.numpy as jnp
from jax import lax
from jax.sharding import PartitionSpec as P

epsilon = 1e-06
gelu_scale = 0.7978845608028654
gelu_cubic = 0.044715


def with_halo(block, sides, width):
    for axis, dim in sides:
        count = lax.axis_size(axis)
        forward = [(i, i + 1) for i in range(count - 1)]
        backward = [(target, source) for source, target in forward]
        low = lax.ppermute(
            lax.slice_in_dim(block, block.shape[dim] - width, None, axis=dim), axis, forward
        )
        high = lax.ppermute(lax.slice_in_dim(block, 0, width, axis=dim), axis, backward)
        block = jnp.concatenate([low, block, high], axis=dim)
    return block


def gelu_value(inputs):
    inner = gelu_scale * (inputs + gelu_cubic * inputs * inputs * inputs)
    return 0.5 * inputs * (1.0 + jnp.tanh(inner))


def gelu_slope(inputs):
    inner = gelu_scale * (inputs + gelu_cubic * inputs * inputs * inputs)
    tangent = jnp.tanh(inner)
    return 0.5 * (1.0 + tangent) + 0.5 * inputs * (1.0 - tangent * tangent) * gelu_scale * (
        1.0 + 3.0 * gelu_cubic * inputs * inputs
    )


def tap_stack(padded, dilate, rim_width, bin_count, sign):
    slices = [
        lax.dynamic_slice_in_dim(padded, rim_width + sign * (tap_index - 1) * dilate, bin_count, 0)
        for tap_index in range(3)
    ]
    return jnp.concatenate(slices, axis=1)


def flip_channels(values, mirror):
    return jnp.dot(values, mirror, preferred_element_type=jnp.float32).astype(jnp.bfloat16)


def spread_back(back_taps, weight, channels):
    result = jnp.zeros((back_taps.shape[0], channels), jnp.float32)
    for tap_index in range(3):
        result = result + lax.dot_general(
            back_taps[:, tap_index * channels : (tap_index + 1) * channels],
            weight[tap_index],
            (((1,), (1,)), ((), ())),
            preferred_element_type=jnp.float32,
        )
    return result


def halve_sum(blocks, axis):
    size = lax.axis_size(axis)
    if size & (size - 1):
        flat = blocks.reshape((-1,) + blocks.shape[2:])
        return lax.psum_scatter(flat, axis, scatter_dimension=0, tiled=True).reshape(blocks.shape[1:])
    me = lax.axis_index(axis)
    bit = 1
    while bit < size:
        blocks = blocks.reshape((blocks.shape[0] // 2, 2) + blocks.shape[1:])
        mine = (me // bit) % 2
        keep = lax.dynamic_index_in_dim(blocks, mine, 1, keepdims=False)
        send = lax.dynamic_index_in_dim(blocks, 1 - mine, 1, keepdims=False)
        pairs = [(i, i ^ bit) for i in range(size)]
        blocks = keep + lax.ppermute(send, axis, pairs)
        bit *= 2
    return blocks[0]


def halve_step(values, dims, axis, bit, link_type):
    where = dims.index(f"{axis}{bit}")
    mine = (lax.axis_index(axis) // bit) % 2
    keep = lax.dynamic_index_in_dim(values, mine, where, keepdims=False)
    send = lax.dynamic_index_in_dim(values, 1 - mine, where, keepdims=False).astype(link_type)
    size = lax.axis_size(axis)
    got = lax.ppermute(send, axis, [(i, i ^ bit) for i in range(size)])
    return keep + got.astype(keep.dtype), dims[:where] + dims[where + 1 :]


def scatter_sum(term, channels):
    win_count = lax.axis_size("win")
    seq_count = lax.axis_size("seq")
    blocks = term.reshape(win_count, seq_count, -1, channels)
    rows = blocks.shape[2]
    if (win_count & (win_count - 1)) or (seq_count & (seq_count - 1)) or rows % 2:
        return halve_sum(halve_sum(blocks, "win"), "seq")
    win_bits = [("win", 1 << k) for k in range(win_count.bit_length() - 1)]
    seq_bits = [("seq", 1 << k) for k in range(seq_count.bit_length() - 1)]
    names = [f"{a}{b}" for a, b in reversed(win_bits)] + [f"{a}{b}" for a, b in reversed(seq_bits)]
    values = blocks.reshape([2] * len(names) + [rows, channels])
    first, middle, last = win_bits[:1], win_bits[1:], seq_bits
    ways = 2 if len(middle) >= 2 else 1
    dims = list(names)
    for axis, bit in first:
        values, dims = halve_step(values, dims, axis, bit, jnp.float32)
    lead = len(dims)
    parts = values.reshape(values.shape[:lead] + (ways, rows // ways, channels))
    states = [(lax.index_in_dim(parts, part, lead, keepdims=False), list(dims)) for part in range(ways)]
    for step in range(len(middle)):
        for part in range(ways):
            axis, bit = middle[(step + part) % len(middle)]
            states[part] = halve_step(states[part][0], states[part][1], axis, bit, jnp.bfloat16)
    values = jnp.concatenate([part for part, _ in states], axis=-2)
    dims = states[0][1]
    values = values.reshape((seq_count,) + values.shape[len(last) :])
    me = lax.axis_index("seq")
    total = lax.dynamic_index_in_dim(values, me, 0, keepdims=False)
    for shift in range(1, seq_count):
        send = lax.dynamic_index_in_dim(values, (me + shift) % seq_count, 0, keepdims=False)
        got = lax.ppermute(
            send.astype(jnp.bfloat16), "seq", [(i, (i + shift) % seq_count) for i in range(seq_count)]
        )
        total = total + got.astype(jnp.float32)
    return total


def gather_rows(block, axis):
    size = lax.axis_size(axis)
    me = lax.axis_index(axis)
    whole = jnp.zeros((size,) + block.shape, block.dtype)
    whole = lax.dynamic_update_index_in_dim(whole, block, me, 0)
    for shift in range(1, size):
        pairs = [(i, (i + shift) % size) for i in range(size)]
        got = lax.ppermute(block, axis, pairs)
        whole = lax.dynamic_update_index_in_dim(whole, got, (me - shift) % size, 0)
    return whole.reshape((-1,) + block.shape[1:])


def per_device(
    embeddings,
    norm_gain,
    conv_weight,
    conv_bias,
    dilation,
    donor_bins,
    acceptor_bins,
    junction_count,
    donor_proj,
    acceptor_proj,
    out_cotangent,
    score_cotangent,
):
    bin_count = embeddings.shape[1]
    channels = embeddings.shape[2]
    rim_width = bin_count // 2
    dilate = dilation[0]
    lanes = lax.broadcasted_iota(jnp.int32, (channels, channels), 0)
    mirror = (
        lanes + lax.broadcasted_iota(jnp.int32, (channels, channels), 1) == channels - 1
    ).astype(jnp.bfloat16)
    own = slice(rim_width, rim_width + bin_count)

    padded_in = with_halo(jnp.stack([embeddings[0], out_cotangent[0]]), (("seq", 1),), rim_width)
    emb = padded_in[0]
    emb_rev = flip_channels(emb, mirror)
    as_float = emb.astype(jnp.float32)
    inverse = lax.rsqrt(jnp.mean(as_float * as_float, axis=1, keepdims=True) + epsilon)
    normed = as_float * inverse
    normed_rev = emb_rev.astype(jnp.float32) * inverse
    pre_fwd = normed * norm_gain
    pre_rev = normed_rev * norm_gain
    act_fwd = gelu_value(pre_fwd).astype(jnp.bfloat16)
    act_rev = gelu_value(pre_rev).astype(jnp.bfloat16)

    taps_fwd = tap_stack(act_fwd, dilate, rim_width, bin_count, 1)
    taps_rev = tap_stack(act_rev, dilate, rim_width, bin_count, -1)
    conv_all = (
        jnp.dot(
            jnp.concatenate([taps_fwd, taps_rev], axis=0),
            conv_weight.reshape(3 * channels, channels),
            preferred_element_type=jnp.float32,
        )
        + conv_bias
    ).astype(jnp.bfloat16)
    conv_fwd = conv_all[:bin_count]
    conv_rev = flip_channels(conv_all[bin_count:], mirror)
    block_flat = (
        as_float[own] + 0.5 * (conv_fwd.astype(jnp.float32) + conv_rev.astype(jnp.float32))
    ).astype(jnp.bfloat16)

    both_proj = jnp.concatenate([donor_proj, acceptor_proj], axis=1)
    hidden = donor_proj.shape[1]
    window_out = gather_rows(block_flat, "seq")
    window_proj = jnp.dot(window_out, both_proj, preferred_element_type=jnp.float32).astype(
        jnp.bfloat16
    )
    slots = lax.broadcasted_iota(jnp.int32, (donor_bins.shape[1], window_proj.shape[0]), 1)
    rows_donor = jnp.dot(
        (donor_bins[0][:, None] == slots).astype(jnp.bfloat16),
        window_proj[:, :hidden],
        preferred_element_type=jnp.float32,
    )
    rows_acceptor = jnp.dot(
        (acceptor_bins[0][:, None] == slots).astype(jnp.bfloat16),
        window_proj[:, hidden:],
        preferred_element_type=jnp.float32,
    )
    pair_total = donor_bins.shape[1]
    pair_share = pair_total // lax.axis_size("seq")
    pair_first = lax.axis_index("seq") * pair_share
    live_mask = (jnp.arange(pair_total) < junction_count[0]).astype(jnp.float32)
    score_scale = hidden ** (-0.5)
    products = jnp.sum(
        lax.dynamic_slice_in_dim(rows_donor, pair_first, pair_share, 0)
        * lax.dynamic_slice_in_dim(rows_acceptor, pair_first, pair_share, 0),
        axis=1,
    )
    junction_scores = (
        lax.dynamic_slice_in_dim(live_mask, pair_first, pair_share, 0) * products * score_scale
    )[None]
    pair_weight = score_cotangent[0] * live_mask * score_scale
    positions = lax.axis_index("seq") * bin_count - rim_width + jnp.arange(emb.shape[0])
    pick_donor = (positions[:, None] == donor_bins[0][None, :]).astype(jnp.float32)
    pick_acceptor = (positions[:, None] == acceptor_bins[0][None, :]).astype(jnp.float32)
    grad_donor = jnp.dot(
        pick_donor, pair_weight[:, None] * rows_acceptor, precision=lax.Precision.HIGHEST
    ).astype(jnp.bfloat16)
    grad_acceptor = jnp.dot(
        pick_acceptor, pair_weight[:, None] * rows_donor, precision=lax.Precision.HIGHEST
    ).astype(jnp.bfloat16)
    out_grad = padded_in[1].astype(jnp.float32) + lax.dot_general(
        jnp.concatenate([grad_donor, grad_acceptor], axis=1),
        both_proj,
        (((1,), (1,)), ((), ())),
        preferred_element_type=jnp.float32,
    )
    conv_grad = (0.5 * out_grad).astype(jnp.bfloat16)
    conv_grad_rev = flip_channels(conv_grad, mirror)
    back_fwd = tap_stack(conv_grad, dilate, rim_width, bin_count, -1)
    back_rev = tap_stack(conv_grad_rev, dilate, rim_width, bin_count, 1)
    dact_all = spread_back(jnp.concatenate([back_fwd, back_rev], axis=0), conv_weight, channels)
    dact_fwd = dact_all[:bin_count]
    dact_rev = dact_all[bin_count:]
    norm_rev = flip_channels(
        (dact_rev * gelu_slope(pre_rev[own]) * norm_gain).astype(jnp.bfloat16), mirror
    )
    norm_grad = dact_fwd * gelu_slope(pre_fwd[own]) * norm_gain + norm_rev.astype(jnp.float32)
    normed_own = normed[own]
    input_grad = (
        out_grad[own]
        + inverse[own]
        * (norm_grad - normed_own * jnp.mean(norm_grad * normed_own, axis=1, keepdims=True))
    ).astype(jnp.bfloat16)[None]
    grad_term = lax.dot_general(
        jnp.concatenate([act_fwd[own], act_rev[own]], axis=0),
        jnp.concatenate([conv_grad[own], conv_grad_rev[own]], axis=0),
        (((0,), (0,)), ((), ())),
        preferred_element_type=jnp.float32,
    )
    grad_term = grad_term / lax.axis_size("win")
    weight_grad = scatter_sum(grad_term, channels).reshape(-1)
    return (block_flat[None], junction_scores, input_grad, weight_grad)


def solution(mesh):
    return jax.shard_map(
        per_device,
        mesh=mesh,
        in_specs=(
            P("win", "seq", None),
            P(),
            P(),
            P(),
            P("win"),
            P("win", None),
            P("win", None),
            P("win"),
            P(),
            P(),
            P("win", "seq", None),
            P("win", None),
        ),
        out_specs=(
            P("win", "seq", None),
            P("win", "seq"),
            P("win", "seq", None),
            P(("win", "seq")),
        ),
        check_vma=False,
    )
```

```python
import jax
import jax.numpy as jnp
from jax import lax
from jax.sharding import PartitionSpec as P

epsilon = 1e-06
gelu_scale = 0.7978845608028654
gelu_cubic = 0.044715


def with_halo(block, sides, width):
    for axis, dim in sides:
        count = lax.axis_size(axis)
        forward = [(i, i + 1) for i in range(count - 1)]
        backward = [(target, source) for source, target in forward]
        low = lax.ppermute(
            lax.slice_in_dim(block, block.shape[dim] - width, None, axis=dim), axis, forward
        )
        high = lax.ppermute(lax.slice_in_dim(block, 0, width, axis=dim), axis, backward)
        block = jnp.concatenate([low, block, high], axis=dim)
    return block


def gelu_value(inputs):
    inner = gelu_scale * (inputs + gelu_cubic * inputs * inputs * inputs)
    return 0.5 * inputs * (1.0 + jnp.tanh(inner))


def gelu_slope(inputs):
    inner = gelu_scale * (inputs + gelu_cubic * inputs * inputs * inputs)
    tangent = jnp.tanh(inner)
    return 0.5 * (1.0 + tangent) + 0.5 * inputs * (1.0 - tangent * tangent) * gelu_scale * (
        1.0 + 3.0 * gelu_cubic * inputs * inputs
    )


def tap_stack(padded, dilate, rim_width, bin_count, sign):
    shape = (bin_count, padded.shape[0])
    target = lax.broadcasted_iota(jnp.int32, shape, 0)
    source = lax.broadcasted_iota(jnp.int32, shape, 1)
    slices = []
    for tap_index in range(3):
        pick = (source == target + rim_width + sign * (tap_index - 1) * dilate).astype(padded.dtype)
        slices.append(
            jnp.dot(pick, padded, preferred_element_type=jnp.float32).astype(padded.dtype)
        )
    return jnp.concatenate(slices, axis=1)


def flip_channels(values, mirror):
    return jnp.dot(values, mirror, preferred_element_type=jnp.float32).astype(jnp.bfloat16)


def spread_back(back_taps, weight, channels):
    result = jnp.zeros((back_taps.shape[0], channels), jnp.float32)
    for tap_index in range(3):
        result = result + lax.dot_general(
            back_taps[:, tap_index * channels : (tap_index + 1) * channels],
            weight[tap_index],
            (((1,), (1,)), ((), ())),
            preferred_element_type=jnp.float32,
        )
    return result


def halve_sum(blocks, axis):
    size = lax.axis_size(axis)
    if size & (size - 1):
        flat = blocks.reshape((-1,) + blocks.shape[2:])
        return lax.psum_scatter(flat, axis, scatter_dimension=0, tiled=True).reshape(blocks.shape[1:])
    me = lax.axis_index(axis)
    bit = 1
    while bit < size:
        blocks = blocks.reshape((blocks.shape[0] // 2, 2) + blocks.shape[1:])
        mine = (me // bit) % 2
        keep = lax.dynamic_index_in_dim(blocks, mine, 1, keepdims=False)
        send = lax.dynamic_index_in_dim(blocks, 1 - mine, 1, keepdims=False)
        pairs = [(i, i ^ bit) for i in range(size)]
        blocks = keep + lax.ppermute(send, axis, pairs)
        bit *= 2
    return blocks[0]


def halve_step(values, dims, axis, bit, link_type):
    where = dims.index(f"{axis}{bit}")
    mine = (lax.axis_index(axis) // bit) % 2
    keep = lax.dynamic_index_in_dim(values, mine, where, keepdims=False)
    send = lax.dynamic_index_in_dim(values, 1 - mine, where, keepdims=False).astype(link_type)
    size = lax.axis_size(axis)
    got = lax.ppermute(send, axis, [(i, i ^ bit) for i in range(size)])
    return keep + got.astype(keep.dtype), dims[:where] + dims[where + 1 :]


def scatter_sum(term, channels):
    win_count = lax.axis_size("win")
    seq_count = lax.axis_size("seq")
    blocks = term.reshape(win_count, seq_count, -1, channels)
    rows = blocks.shape[2]
    if (win_count & (win_count - 1)) or (seq_count & (seq_count - 1)) or rows % 2:
        return halve_sum(halve_sum(blocks, "win"), "seq")
    win_bits = [("win", 1 << k) for k in range(win_count.bit_length() - 1)]
    seq_bits = [("seq", 1 << k) for k in range(seq_count.bit_length() - 1)]
    names = [f"{a}{b}" for a, b in reversed(win_bits)] + [f"{a}{b}" for a, b in reversed(seq_bits)]
    values = blocks.reshape([2] * len(names) + [rows, channels])
    first, middle, last = win_bits[:1], win_bits[1:], seq_bits
    ways = 2 if len(middle) >= 2 else 1
    dims = list(names)
    for axis, bit in first:
        values, dims = halve_step(values, dims, axis, bit, jnp.float32)
    lead = len(dims)
    parts = values.reshape(values.shape[:lead] + (ways, rows // ways, channels))
    states = [(lax.index_in_dim(parts, part, lead, keepdims=False), list(dims)) for part in range(ways)]
    for step in range(len(middle)):
        for part in range(ways):
            axis, bit = middle[(step + part) % len(middle)]
            states[part] = halve_step(states[part][0], states[part][1], axis, bit, jnp.bfloat16)
    values = jnp.concatenate([part for part, _ in states], axis=-2)
    dims = states[0][1]
    values = values.reshape((seq_count,) + values.shape[len(last) :])
    me = lax.axis_index("seq")
    total = lax.dynamic_index_in_dim(values, me, 0, keepdims=False)
    for shift in range(1, seq_count):
        send = lax.dynamic_index_in_dim(values, (me + shift) % seq_count, 0, keepdims=False)
        got = lax.ppermute(
            send.astype(jnp.bfloat16), "seq", [(i, (i + shift) % seq_count) for i in range(seq_count)]
        )
        total = total + got.astype(jnp.float32)
    return total


def gather_rows(block, axis):
    size = lax.axis_size(axis)
    me = lax.axis_index(axis)
    whole = jnp.zeros((size,) + block.shape, block.dtype)
    whole = lax.dynamic_update_index_in_dim(whole, block, me, 0)
    for shift in range(1, size):
        pairs = [(i, (i + shift) % size) for i in range(size)]
        got = lax.ppermute(block, axis, pairs)
        whole = lax.dynamic_update_index_in_dim(whole, got, (me - shift) % size, 0)
    return whole.reshape((-1,) + block.shape[1:])


def per_device(
    embeddings,
    norm_gain,
    conv_weight,
    conv_bias,
    dilation,
    donor_bins,
    acceptor_bins,
    junction_count,
    donor_proj,
    acceptor_proj,
    out_cotangent,
    score_cotangent,
):
    bin_count = embeddings.shape[1]
    channels = embeddings.shape[2]
    rim_width = bin_count // 2
    dilate = dilation[0]
    lanes = lax.broadcasted_iota(jnp.int32, (channels, channels), 0)
    mirror = (
        lanes + lax.broadcasted_iota(jnp.int32, (channels, channels), 1) == channels - 1
    ).astype(jnp.bfloat16)
    own = slice(rim_width, rim_width + bin_count)

    padded_in = with_halo(jnp.stack([embeddings[0], out_cotangent[0]]), (("seq", 1),), rim_width)
    emb = padded_in[0]
    emb_rev = flip_channels(emb, mirror)
    as_float = emb.astype(jnp.float32)
    inverse = lax.rsqrt(jnp.mean(as_float * as_float, axis=1, keepdims=True) + epsilon)
    normed = as_float * inverse
    normed_rev = emb_rev.astype(jnp.float32) * inverse
    pre_fwd = normed * norm_gain
    pre_rev = normed_rev * norm_gain
    act_fwd = gelu_value(pre_fwd).astype(jnp.bfloat16)
    act_rev = gelu_value(pre_rev).astype(jnp.bfloat16)

    taps_fwd = tap_stack(act_fwd, dilate, rim_width, bin_count, 1)
    taps_rev = tap_stack(act_rev, dilate, rim_width, bin_count, -1)
    conv_all = (
        jnp.dot(
            jnp.concatenate([taps_fwd, taps_rev], axis=0),
            conv_weight.reshape(3 * channels, channels),
            preferred_element_type=jnp.float32,
        )
        + conv_bias
    ).astype(jnp.bfloat16)
    conv_fwd = conv_all[:bin_count]
    conv_rev = flip_channels(conv_all[bin_count:], mirror)
    block_flat = (
        as_float[own] + 0.5 * (conv_fwd.astype(jnp.float32) + conv_rev.astype(jnp.float32))
    ).astype(jnp.bfloat16)

    both_proj = jnp.concatenate([donor_proj, acceptor_proj], axis=1)
    hidden = donor_proj.shape[1]
    window_out = gather_rows(block_flat, "seq")
    window_proj = jnp.dot(window_out, both_proj, preferred_element_type=jnp.float32).astype(
        jnp.bfloat16
    )
    slots = lax.broadcasted_iota(jnp.int32, (donor_bins.shape[1], window_proj.shape[0]), 1)
    rows_donor = jnp.dot(
        (donor_bins[0][:, None] == slots).astype(jnp.bfloat16),
        window_proj[:, :hidden],
        preferred_element_type=jnp.float32,
    )
    rows_acceptor = jnp.dot(
        (acceptor_bins[0][:, None] == slots).astype(jnp.bfloat16),
        window_proj[:, hidden:],
        preferred_element_type=jnp.float32,
    )
    pair_total = donor_bins.shape[1]
    pair_share = pair_total // lax.axis_size("seq")
    pair_first = lax.axis_index("seq") * pair_share
    live_mask = (jnp.arange(pair_total) < junction_count[0]).astype(jnp.float32)
    score_scale = hidden ** (-0.5)
    products = jnp.sum(
        lax.dynamic_slice_in_dim(rows_donor, pair_first, pair_share, 0)
        * lax.dynamic_slice_in_dim(rows_acceptor, pair_first, pair_share, 0),
        axis=1,
    )
    junction_scores = (
        lax.dynamic_slice_in_dim(live_mask, pair_first, pair_share, 0) * products * score_scale
    )[None]
    pair_weight = score_cotangent[0] * live_mask * score_scale
    positions = lax.axis_index("seq") * bin_count - rim_width + jnp.arange(emb.shape[0])
    pick_donor = (positions[:, None] == donor_bins[0][None, :]).astype(jnp.float32)
    pick_acceptor = (positions[:, None] == acceptor_bins[0][None, :]).astype(jnp.float32)
    grad_donor = jnp.dot(
        pick_donor, pair_weight[:, None] * rows_acceptor, precision=lax.Precision.HIGHEST
    ).astype(jnp.bfloat16)
    grad_acceptor = jnp.dot(
        pick_acceptor, pair_weight[:, None] * rows_donor, precision=lax.Precision.HIGHEST
    ).astype(jnp.bfloat16)
    out_grad = padded_in[1].astype(jnp.float32) + lax.dot_general(
        jnp.concatenate([grad_donor, grad_acceptor], axis=1),
        both_proj,
        (((1,), (1,)), ((), ())),
        preferred_element_type=jnp.float32,
    )
    conv_grad = (0.5 * out_grad).astype(jnp.bfloat16)
    conv_grad_rev = flip_channels(conv_grad, mirror)
    back_fwd = tap_stack(conv_grad, dilate, rim_width, bin_count, -1)
    back_rev = tap_stack(conv_grad_rev, dilate, rim_width, bin_count, 1)
    dact_all = spread_back(jnp.concatenate([back_fwd, back_rev], axis=0), conv_weight, channels)
    dact_fwd = dact_all[:bin_count]
    dact_rev = dact_all[bin_count:]
    norm_rev = flip_channels(
        (dact_rev * gelu_slope(pre_rev[own]) * norm_gain).astype(jnp.bfloat16), mirror
    )
    norm_grad = dact_fwd * gelu_slope(pre_fwd[own]) * norm_gain + norm_rev.astype(jnp.float32)
    normed_own = normed[own]
    input_grad = (
        out_grad[own]
        + inverse[own]
        * (norm_grad - normed_own * jnp.mean(norm_grad * normed_own, axis=1, keepdims=True))
    ).astype(jnp.bfloat16)[None]
    grad_term = lax.dot_general(
        jnp.concatenate([act_fwd[own], act_rev[own]], axis=0),
        jnp.concatenate([conv_grad[own], conv_grad_rev[own]], axis=0),
        (((0,), (0,)), ((), ())),
        preferred_element_type=jnp.float32,
    )
    grad_term = grad_term / lax.axis_size("win")
    weight_grad = scatter_sum(grad_term, channels).reshape(-1)
    return (block_flat[None], junction_scores, input_grad, weight_grad)


def solution(mesh):
    return jax.shard_map(
        per_device,
        mesh=mesh,
        in_specs=(
            P("win", "seq", None),
            P(),
            P(),
            P(),
            P("win"),
            P("win", None),
            P("win", None),
            P("win"),
            P(),
            P(),
            P("win", "seq", None),
            P("win", None),
        ),
        out_specs=(
            P("win", "seq", None),
            P("win", "seq"),
            P("win", "seq", None),
            P(("win", "seq")),
        ),
        check_vma=False,
    )
```

```python
import jax
import jax.numpy as jnp
from jax import lax
from jax.sharding import PartitionSpec as P

epsilon = 1e-06
gelu_scale = 0.7978845608028654
gelu_cubic = 0.044715


def with_halo(block, sides, width):
    for axis, dim in sides:
        count = lax.axis_size(axis)
        forward = [(i, i + 1) for i in range(count - 1)]
        backward = [(target, source) for source, target in forward]
        low = lax.ppermute(
            lax.slice_in_dim(block, block.shape[dim] - width, None, axis=dim), axis, forward
        )
        high = lax.ppermute(lax.slice_in_dim(block, 0, width, axis=dim), axis, backward)
        block = jnp.concatenate([low, block, high], axis=dim)
    return block


def gelu_value(inputs):
    inner = gelu_scale * (inputs + gelu_cubic * inputs * inputs * inputs)
    return 0.5 * inputs * (1.0 + jnp.tanh(inner))


def gelu_slope(inputs):
    inner = gelu_scale * (inputs + gelu_cubic * inputs * inputs * inputs)
    tangent = jnp.tanh(inner)
    return 0.5 * (1.0 + tangent) + 0.5 * inputs * (1.0 - tangent * tangent) * gelu_scale * (
        1.0 + 3.0 * gelu_cubic * inputs * inputs
    )


def tap_stack(padded, dilate, rim_width, bin_count, sign):
    slices = [
        lax.dynamic_slice_in_dim(padded, rim_width + sign * (tap_index - 1) * dilate, bin_count, 0)
        for tap_index in range(3)
    ]
    return jnp.concatenate(slices, axis=1)


def flip_channels(values, mirror):
    return jnp.dot(values, mirror, preferred_element_type=jnp.float32).astype(jnp.bfloat16)


def spread_back(back_taps, weight, channels):
    result = jnp.zeros((back_taps.shape[0], channels), jnp.float32)
    for tap_index in range(3):
        result = result + lax.dot_general(
            back_taps[:, tap_index * channels : (tap_index + 1) * channels],
            weight[tap_index],
            (((1,), (1,)), ((), ())),
            preferred_element_type=jnp.float32,
        )
    return result


def halve_sum(blocks, axis):
    size = lax.axis_size(axis)
    if size & (size - 1):
        flat = blocks.reshape((-1,) + blocks.shape[2:])
        return lax.psum_scatter(flat, axis, scatter_dimension=0, tiled=True).reshape(blocks.shape[1:])
    me = lax.axis_index(axis)
    bit = 1
    while bit < size:
        blocks = blocks.reshape((blocks.shape[0] // 2, 2) + blocks.shape[1:])
        mine = (me // bit) % 2
        keep = lax.dynamic_index_in_dim(blocks, mine, 1, keepdims=False)
        send = lax.dynamic_index_in_dim(blocks, 1 - mine, 1, keepdims=False)
        pairs = [(i, i ^ bit) for i in range(size)]
        blocks = keep + lax.ppermute(send, axis, pairs)
        bit *= 2
    return blocks[0]


def halve_step(values, dims, axis, bit, link_type):
    where = dims.index(f"{axis}{bit}")
    mine = (lax.axis_index(axis) // bit) % 2
    keep = lax.dynamic_index_in_dim(values, mine, where, keepdims=False)
    send = lax.dynamic_index_in_dim(values, 1 - mine, where, keepdims=False).astype(link_type)
    size = lax.axis_size(axis)
    got = lax.ppermute(send, axis, [(i, i ^ bit) for i in range(size)])
    return keep + got.astype(keep.dtype), dims[:where] + dims[where + 1 :]


def scatter_sum(term, channels):
    win_count = lax.axis_size("win")
    seq_count = lax.axis_size("seq")
    blocks = term.reshape(win_count, seq_count, -1, channels)
    rows = blocks.shape[2]
    if (win_count & (win_count - 1)) or (seq_count & (seq_count - 1)) or rows % 2:
        return halve_sum(halve_sum(blocks, "win"), "seq")
    win_bits = [("win", 1 << k) for k in range(win_count.bit_length() - 1)]
    seq_bits = [("seq", 1 << k) for k in range(seq_count.bit_length() - 1)]
    names = [f"{a}{b}" for a, b in reversed(win_bits)] + [f"{a}{b}" for a, b in reversed(seq_bits)]
    values = blocks.reshape([2] * len(names) + [rows, channels])
    first, middle, last = win_bits[:1], win_bits[1:], seq_bits
    ways = 2 if len(middle) >= 2 else 1
    dims = list(names)
    for axis, bit in first:
        values, dims = halve_step(values, dims, axis, bit, jnp.float32)
    lead = len(dims)
    parts = values.reshape(values.shape[:lead] + (ways, rows // ways, channels))
    states = [(lax.index_in_dim(parts, part, lead, keepdims=False), list(dims)) for part in range(ways)]
    for step in range(len(middle)):
        for part in range(ways):
            axis, bit = middle[(step + part) % len(middle)]
            states[part] = halve_step(states[part][0], states[part][1], axis, bit, jnp.bfloat16)
    values = jnp.concatenate([part for part, _ in states], axis=-2)
    dims = states[0][1]
    values = values.reshape((seq_count,) + values.shape[len(last) :])
    me = lax.axis_index("seq")
    total = lax.dynamic_index_in_dim(values, me, 0, keepdims=False)
    for shift in range(1, seq_count):
        send = lax.dynamic_index_in_dim(values, (me + shift) % seq_count, 0, keepdims=False)
        got = lax.ppermute(
            send.astype(jnp.bfloat16), "seq", [(i, (i + shift) % seq_count) for i in range(seq_count)]
        )
        total = total + got.astype(jnp.float32)
    return total


def gather_rows(block, axis):
    size = lax.axis_size(axis)
    me = lax.axis_index(axis)
    whole = jnp.zeros((size,) + block.shape, block.dtype)
    whole = lax.dynamic_update_index_in_dim(whole, block, me, 0)
    for shift in range(1, size):
        pairs = [(i, (i + shift) % size) for i in range(size)]
        got = lax.ppermute(block, axis, pairs)
        whole = lax.dynamic_update_index_in_dim(whole, got, (me - shift) % size, 0)
    return whole.reshape((-1,) + block.shape[1:])


def per_device(
    embeddings,
    norm_gain,
    conv_weight,
    conv_bias,
    dilation,
    donor_bins,
    acceptor_bins,
    junction_count,
    donor_proj,
    acceptor_proj,
    out_cotangent,
    score_cotangent,
):
    bin_count = embeddings.shape[1]
    channels = embeddings.shape[2]
    rim_width = bin_count // 2
    dilate = dilation[0]
    lanes = lax.broadcasted_iota(jnp.int32, (channels, channels), 0)
    mirror = (
        lanes + lax.broadcasted_iota(jnp.int32, (channels, channels), 1) == channels - 1
    ).astype(jnp.bfloat16)
    own = slice(rim_width, rim_width + bin_count)

    padded_in = with_halo(jnp.stack([embeddings[0], out_cotangent[0]]), (("seq", 1),), rim_width)
    emb = padded_in[0]
    emb_rev = flip_channels(emb, mirror)
    as_float = emb.astype(jnp.float32)
    inverse = lax.rsqrt(jnp.mean(as_float * as_float, axis=1, keepdims=True) + epsilon)
    normed = as_float * inverse
    normed_rev = emb_rev.astype(jnp.float32) * inverse
    pre_fwd = normed * norm_gain
    pre_rev = normed_rev * norm_gain
    act_fwd = gelu_value(pre_fwd).astype(jnp.bfloat16)
    act_rev = gelu_value(pre_rev).astype(jnp.bfloat16)

    taps_fwd = tap_stack(act_fwd, dilate, rim_width, bin_count, 1)
    taps_rev = tap_stack(act_rev, dilate, rim_width, bin_count, -1)
    conv_all = (
        jnp.dot(
            jnp.concatenate([taps_fwd, taps_rev], axis=0),
            conv_weight.reshape(3 * channels, channels),
            preferred_element_type=jnp.float32,
        )
        + conv_bias
    ).astype(jnp.bfloat16)
    conv_fwd = conv_all[:bin_count]
    conv_rev = flip_channels(conv_all[bin_count:], mirror)
    block_flat = (
        as_float[own] + 0.5 * (conv_fwd.astype(jnp.float32) + conv_rev.astype(jnp.float32))
    ).astype(jnp.bfloat16)

    both_proj = jnp.concatenate([donor_proj, acceptor_proj], axis=1)
    hidden = donor_proj.shape[1]
    window_out = gather_rows(block_flat, "seq")
    window_proj = jnp.dot(window_out, both_proj, preferred_element_type=jnp.float32).astype(
        jnp.bfloat16
    )
    slots = lax.broadcasted_iota(jnp.int32, (donor_bins.shape[1], window_proj.shape[0]), 1)
    rows_donor = jnp.dot(
        (donor_bins[0][:, None] == slots).astype(jnp.bfloat16),
        window_proj[:, :hidden],
        preferred_element_type=jnp.float32,
    )
    rows_acceptor = jnp.dot(
        (acceptor_bins[0][:, None] == slots).astype(jnp.bfloat16),
        window_proj[:, hidden:],
        preferred_element_type=jnp.float32,
    )
    pair_total = donor_bins.shape[1]
    pair_share = pair_total // lax.axis_size("seq")
    pair_first = lax.axis_index("seq") * pair_share
    live_mask = (jnp.arange(pair_total) < junction_count[0]).astype(jnp.float32)
    score_scale = hidden ** (-0.5)
    products = jnp.sum(
        lax.dynamic_slice_in_dim(rows_donor, pair_first, pair_share, 0)
        * lax.dynamic_slice_in_dim(rows_acceptor, pair_first, pair_share, 0),
        axis=1,
    )
    junction_scores = (
        lax.dynamic_slice_in_dim(live_mask, pair_first, pair_share, 0) * products * score_scale
    )[None]
    pair_weight = score_cotangent[0] * live_mask * score_scale
    positions = lax.axis_index("seq") * bin_count - rim_width + jnp.arange(emb.shape[0])
    pick_donor = (positions[:, None] == donor_bins[0][None, :]).astype(jnp.float32)
    pick_acceptor = (positions[:, None] == acceptor_bins[0][None, :]).astype(jnp.float32)
    grad_donor = jnp.dot(
        pick_donor, pair_weight[:, None] * rows_acceptor, precision=lax.Precision.HIGH
    ).astype(jnp.bfloat16)
    grad_acceptor = jnp.dot(
        pick_acceptor, pair_weight[:, None] * rows_donor, precision=lax.Precision.HIGH
    ).astype(jnp.bfloat16)
    out_grad = padded_in[1].astype(jnp.float32) + lax.dot_general(
        jnp.concatenate([grad_donor, grad_acceptor], axis=1),
        both_proj,
        (((1,), (1,)), ((), ())),
        preferred_element_type=jnp.float32,
    )
    conv_grad = (0.5 * out_grad).astype(jnp.bfloat16)
    conv_grad_rev = flip_channels(conv_grad, mirror)
    back_fwd = tap_stack(conv_grad, dilate, rim_width, bin_count, -1)
    back_rev = tap_stack(conv_grad_rev, dilate, rim_width, bin_count, 1)
    dact_all = spread_back(jnp.concatenate([back_fwd, back_rev], axis=0), conv_weight, channels)
    dact_fwd = dact_all[:bin_count]
    dact_rev = dact_all[bin_count:]
    norm_rev = flip_channels(
        (dact_rev * gelu_slope(pre_rev[own]) * norm_gain).astype(jnp.bfloat16), mirror
    )
    norm_grad = dact_fwd * gelu_slope(pre_fwd[own]) * norm_gain + norm_rev.astype(jnp.float32)
    normed_own = normed[own]
    input_grad = (
        out_grad[own]
        + inverse[own]
        * (norm_grad - normed_own * jnp.mean(norm_grad * normed_own, axis=1, keepdims=True))
    ).astype(jnp.bfloat16)[None]
    grad_term = lax.dot_general(
        jnp.concatenate([act_fwd[own], act_rev[own]], axis=0),
        jnp.concatenate([conv_grad[own], conv_grad_rev[own]], axis=0),
        (((0,), (0,)), ((), ())),
        preferred_element_type=jnp.float32,
    )
    grad_term = grad_term / lax.axis_size("win")
    weight_grad = scatter_sum(grad_term, channels).reshape(-1)
    return (block_flat[None], junction_scores, input_grad, weight_grad)


def solution(mesh):
    return jax.shard_map(
        per_device,
        mesh=mesh,
        in_specs=(
            P("win", "seq", None),
            P(),
            P(),
            P(),
            P("win"),
            P("win", None),
            P("win", None),
            P("win"),
            P(),
            P(),
            P("win", "seq", None),
            P("win", None),
        ),
        out_specs=(
            P("win", "seq", None),
            P("win", "seq"),
            P("win", "seq", None),
            P(("win", "seq")),
        ),
        check_vma=False,
    )
```

```python
import jax
import jax.numpy as jnp
from jax import lax
from jax.sharding import PartitionSpec as P

epsilon = 1e-06
gelu_scale = 0.7978845608028654
gelu_cubic = 0.044715


def with_halo(block, sides, width):
    for axis, dim in sides:
        count = lax.axis_size(axis)
        forward = [(i, i + 1) for i in range(count - 1)]
        backward = [(target, source) for source, target in forward]
        low = lax.ppermute(
            lax.slice_in_dim(block, block.shape[dim] - width, None, axis=dim), axis, forward
        )
        high = lax.ppermute(lax.slice_in_dim(block, 0, width, axis=dim), axis, backward)
        block = jnp.concatenate([low, block, high], axis=dim)
    return block


def gelu_value(inputs):
    inner = gelu_scale * (inputs + gelu_cubic * inputs * inputs * inputs)
    return 0.5 * inputs * (1.0 + jnp.tanh(inner))


def gelu_slope(inputs):
    inner = gelu_scale * (inputs + gelu_cubic * inputs * inputs * inputs)
    tangent = jnp.tanh(inner)
    return 0.5 * (1.0 + tangent) + 0.5 * inputs * (1.0 - tangent * tangent) * gelu_scale * (
        1.0 + 3.0 * gelu_cubic * inputs * inputs
    )


def tap_stack(padded, dilate, rim_width, bin_count, sign):
    slices = [
        lax.dynamic_slice_in_dim(padded, rim_width + sign * (tap_index - 1) * dilate, bin_count, 0)
        for tap_index in range(3)
    ]
    return jnp.concatenate(slices, axis=1)


def flip_channels(values, mirror):
    return jnp.dot(values, mirror, preferred_element_type=jnp.float32).astype(jnp.bfloat16)


def spread_back(back_taps, weight, channels):
    result = jnp.zeros((back_taps.shape[0], channels), jnp.float32)
    for tap_index in range(3):
        result = result + lax.dot_general(
            back_taps[:, tap_index * channels : (tap_index + 1) * channels],
            weight[tap_index],
            (((1,), (1,)), ((), ())),
            preferred_element_type=jnp.float32,
        )
    return result


def halve_sum(blocks, axis):
    size = lax.axis_size(axis)
    if size & (size - 1):
        flat = blocks.reshape((-1,) + blocks.shape[2:])
        return lax.psum_scatter(flat, axis, scatter_dimension=0, tiled=True).reshape(blocks.shape[1:])
    me = lax.axis_index(axis)
    bit = 1
    while bit < size:
        blocks = blocks.reshape((blocks.shape[0] // 2, 2) + blocks.shape[1:])
        mine = (me // bit) % 2
        keep = lax.dynamic_index_in_dim(blocks, mine, 1, keepdims=False)
        send = lax.dynamic_index_in_dim(blocks, 1 - mine, 1, keepdims=False)
        pairs = [(i, i ^ bit) for i in range(size)]
        blocks = keep + lax.ppermute(send, axis, pairs)
        bit *= 2
    return blocks[0]


def halve_step(values, dims, axis, bit, link_type):
    where = dims.index(f"{axis}{bit}")
    mine = (lax.axis_index(axis) // bit) % 2
    keep = lax.dynamic_index_in_dim(values, mine, where, keepdims=False)
    send = lax.dynamic_index_in_dim(values, 1 - mine, where, keepdims=False).astype(link_type)
    size = lax.axis_size(axis)
    got = lax.ppermute(send, axis, [(i, i ^ bit) for i in range(size)])
    return keep + got.astype(keep.dtype), dims[:where] + dims[where + 1 :]


def scatter_sum(term, channels):
    win_count = lax.axis_size("win")
    seq_count = lax.axis_size("seq")
    blocks = term.reshape(win_count, seq_count, -1, channels)
    rows = blocks.shape[2]
    if (win_count & (win_count - 1)) or (seq_count & (seq_count - 1)) or rows % 2:
        return halve_sum(halve_sum(blocks, "win"), "seq")
    win_bits = [("win", 1 << k) for k in range(win_count.bit_length() - 1)]
    seq_bits = [("seq", 1 << k) for k in range(seq_count.bit_length() - 1)]
    names = [f"{a}{b}" for a, b in reversed(win_bits)] + [f"{a}{b}" for a, b in reversed(seq_bits)]
    values = blocks.reshape([2] * len(names) + [rows, channels])
    first, middle, last = win_bits[:1], win_bits[1:], seq_bits
    ways = 2 if len(middle) >= 2 else 1
    dims = list(names)
    for axis, bit in first:
        values, dims = halve_step(values, dims, axis, bit, jnp.float32)
    lead = len(dims)
    parts = values.reshape(values.shape[:lead] + (ways, rows // ways, channels))
    states = [(lax.index_in_dim(parts, part, lead, keepdims=False), list(dims)) for part in range(ways)]
    for step in range(len(middle)):
        for part in range(ways):
            axis, bit = middle[(step + part) % len(middle)]
            states[part] = halve_step(states[part][0], states[part][1], axis, bit, jnp.bfloat16)
    values = jnp.concatenate([part for part, _ in states], axis=-2)
    dims = states[0][1]
    values = values.reshape((seq_count,) + values.shape[len(last) :])
    me = lax.axis_index("seq")
    total = lax.dynamic_index_in_dim(values, me, 0, keepdims=False)
    for shift in range(1, seq_count):
        send = lax.dynamic_index_in_dim(values, (me + shift) % seq_count, 0, keepdims=False)
        got = lax.ppermute(
            send.astype(jnp.bfloat16), "seq", [(i, (i + shift) % seq_count) for i in range(seq_count)]
        )
        total = total + got.astype(jnp.float32)
    return total


def gather_rows(block, axis):
    size = lax.axis_size(axis)
    me = lax.axis_index(axis)
    whole = jnp.zeros((size,) + block.shape, block.dtype)
    whole = lax.dynamic_update_index_in_dim(whole, block, me, 0)
    for shift in range(1, size):
        pairs = [(i, (i + shift) % size) for i in range(size)]
        got = lax.ppermute(block, axis, pairs)
        whole = lax.dynamic_update_index_in_dim(whole, got, (me - shift) % size, 0)
    return whole.reshape((-1,) + block.shape[1:])


def per_device(
    embeddings,
    norm_gain,
    conv_weight,
    conv_bias,
    dilation,
    donor_bins,
    acceptor_bins,
    junction_count,
    donor_proj,
    acceptor_proj,
    out_cotangent,
    score_cotangent,
):
    bin_count = embeddings.shape[1]
    channels = embeddings.shape[2]
    rim_width = bin_count // 2
    dilate = dilation[0]
    lanes = lax.broadcasted_iota(jnp.int32, (channels, channels), 0)
    mirror = (
        lanes + lax.broadcasted_iota(jnp.int32, (channels, channels), 1) == channels - 1
    ).astype(jnp.bfloat16)
    own = slice(rim_width, rim_width + bin_count)

    padded_in = with_halo(jnp.stack([embeddings[0], out_cotangent[0]]), (("seq", 1),), rim_width)
    emb = padded_in[0]
    emb_rev = flip_channels(emb, mirror)
    as_float = emb.astype(jnp.float32)
    inverse = lax.rsqrt(jnp.mean(as_float * as_float, axis=1, keepdims=True) + epsilon)
    normed = as_float * inverse
    normed_rev = emb_rev.astype(jnp.float32) * inverse
    pre_fwd = normed * norm_gain
    pre_rev = normed_rev * norm_gain
    act_fwd = gelu_value(pre_fwd).astype(jnp.bfloat16)
    act_rev = gelu_value(pre_rev).astype(jnp.bfloat16)

    taps_fwd = tap_stack(act_fwd, dilate, rim_width, bin_count, 1)
    taps_rev = tap_stack(act_rev, dilate, rim_width, bin_count, -1)
    conv_all = (
        jnp.dot(
            jnp.concatenate([taps_fwd, taps_rev], axis=0),
            conv_weight.reshape(3 * channels, channels),
            preferred_element_type=jnp.float32,
        )
        + conv_bias
    ).astype(jnp.bfloat16)
    conv_fwd = conv_all[:bin_count]
    conv_rev = flip_channels(conv_all[bin_count:], mirror)
    block_flat = (
        as_float[own] + 0.5 * (conv_fwd.astype(jnp.float32) + conv_rev.astype(jnp.float32))
    ).astype(jnp.bfloat16)

    both_proj = jnp.concatenate([donor_proj, acceptor_proj], axis=1)
    hidden = donor_proj.shape[1]
    window_out = gather_rows(block_flat, "seq")
    window_proj = jnp.dot(window_out, both_proj, preferred_element_type=jnp.float32).astype(
        jnp.bfloat16
    )
    slots = lax.broadcasted_iota(jnp.int32, (donor_bins.shape[1], window_proj.shape[0]), 1)
    rows_donor = jnp.dot(
        (donor_bins[0][:, None] == slots).astype(jnp.bfloat16),
        window_proj[:, :hidden],
        preferred_element_type=jnp.float32,
    )
    rows_acceptor = jnp.dot(
        (acceptor_bins[0][:, None] == slots).astype(jnp.bfloat16),
        window_proj[:, hidden:],
        preferred_element_type=jnp.float32,
    )
    pair_total = donor_bins.shape[1]
    pair_share = pair_total // lax.axis_size("seq")
    pair_first = lax.axis_index("seq") * pair_share
    live_mask = (jnp.arange(pair_total) < junction_count[0]).astype(jnp.float32)
    score_scale = hidden ** (-0.5)
    products = jnp.sum(rows_donor * rows_acceptor, axis=1)
    junction_scores = lax.dynamic_slice_in_dim(
        live_mask * products * score_scale, pair_first, pair_share, 0
    )[None]
    pair_weight = score_cotangent[0] * live_mask * score_scale
    positions = lax.axis_index("seq") * bin_count - rim_width + jnp.arange(emb.shape[0])
    pick_donor = (positions[:, None] == donor_bins[0][None, :]).astype(jnp.float32)
    pick_acceptor = (positions[:, None] == acceptor_bins[0][None, :]).astype(jnp.float32)
    grad_donor = jnp.dot(
        pick_donor, pair_weight[:, None] * rows_acceptor, precision=lax.Precision.HIGHEST
    ).astype(jnp.bfloat16)
    grad_acceptor = jnp.dot(
        pick_acceptor, pair_weight[:, None] * rows_donor, precision=lax.Precision.HIGHEST
    ).astype(jnp.bfloat16)
    out_grad = padded_in[1].astype(jnp.float32) + lax.dot_general(
        jnp.concatenate([grad_donor, grad_acceptor], axis=1),
        both_proj,
        (((1,), (1,)), ((), ())),
        preferred_element_type=jnp.float32,
    )
    conv_grad = (0.5 * out_grad).astype(jnp.bfloat16)
    conv_grad_rev = flip_channels(conv_grad, mirror)
    back_fwd = tap_stack(conv_grad, dilate, rim_width, bin_count, -1)
    back_rev = tap_stack(conv_grad_rev, dilate, rim_width, bin_count, 1)
    dact_all = spread_back(jnp.concatenate([back_fwd, back_rev], axis=0), conv_weight, channels)
    dact_fwd = dact_all[:bin_count]
    dact_rev = dact_all[bin_count:]
    norm_rev = flip_channels(
        (dact_rev * gelu_slope(pre_rev[own]) * norm_gain).astype(jnp.bfloat16), mirror
    )
    norm_grad = dact_fwd * gelu_slope(pre_fwd[own]) * norm_gain + norm_rev.astype(jnp.float32)
    normed_own = normed[own]
    input_grad = (
        out_grad[own]
        + inverse[own]
        * (norm_grad - normed_own * jnp.mean(norm_grad * normed_own, axis=1, keepdims=True))
    ).astype(jnp.bfloat16)[None]
    grad_term = lax.dot_general(
        jnp.concatenate([act_fwd[own], act_rev[own]], axis=0),
        jnp.concatenate([conv_grad[own], conv_grad_rev[own]], axis=0),
        (((0,), (0,)), ((), ())),
        preferred_element_type=jnp.float32,
    )
    grad_term = grad_term / lax.axis_size("win")
    weight_grad = scatter_sum(grad_term, channels).reshape(-1)
    return (block_flat[None], junction_scores, input_grad, weight_grad)


def solution(mesh):
    return jax.shard_map(
        per_device,
        mesh=mesh,
        in_specs=(
            P("win", "seq", None),
            P(),
            P(),
            P(),
            P("win"),
            P("win", None),
            P("win", None),
            P("win"),
            P(),
            P(),
            P("win", "seq", None),
            P("win", None),
        ),
        out_specs=(
            P("win", "seq", None),
            P("win", "seq"),
            P("win", "seq", None),
            P(("win", "seq")),
        ),
        check_vma=False,
    )
```

```python
import jax
import jax.numpy as jnp
from jax import lax
from jax.sharding import PartitionSpec as P

epsilon = 1e-06
gelu_scale = 0.7978845608028654
gelu_cubic = 0.044715


def with_halo(block, sides, width):
    for axis, dim in sides:
        count = lax.axis_size(axis)
        forward = [(i, i + 1) for i in range(count - 1)]
        backward = [(target, source) for source, target in forward]
        low = lax.ppermute(
            lax.slice_in_dim(block, block.shape[dim] - width, None, axis=dim), axis, forward
        )
        high = lax.ppermute(lax.slice_in_dim(block, 0, width, axis=dim), axis, backward)
        block = jnp.concatenate([low, block, high], axis=dim)
    return block


def gelu_value(inputs):
    inner = gelu_scale * (inputs + gelu_cubic * inputs * inputs * inputs)
    return 0.5 * inputs * (1.0 + jnp.tanh(inner))


def gelu_slope(inputs):
    inner = gelu_scale * (inputs + gelu_cubic * inputs * inputs * inputs)
    tangent = jnp.tanh(inner)
    return 0.5 * (1.0 + tangent) + 0.5 * inputs * (1.0 - tangent * tangent) * gelu_scale * (
        1.0 + 3.0 * gelu_cubic * inputs * inputs
    )


def tap_stack(padded, dilate, rim_width, bin_count, sign):
    slices = [
        lax.dynamic_slice_in_dim(padded, rim_width + sign * (tap_index - 1) * dilate, bin_count, 0)
        for tap_index in range(3)
    ]
    return jnp.concatenate(slices, axis=1)


def flip_channels(values, mirror):
    return jnp.dot(values, mirror, preferred_element_type=jnp.float32).astype(jnp.bfloat16)


def spread_back(back_taps, weight, channels):
    result = jnp.zeros((back_taps.shape[0], channels), jnp.float32)
    for tap_index in range(3):
        result = result + lax.dot_general(
            back_taps[:, tap_index * channels : (tap_index + 1) * channels],
            weight[tap_index],
            (((1,), (1,)), ((), ())),
            preferred_element_type=jnp.float32,
        )
    return result


def halve_sum(blocks, axis):
    size = lax.axis_size(axis)
    if size & (size - 1):
        flat = blocks.reshape((-1,) + blocks.shape[2:])
        return lax.psum_scatter(flat, axis, scatter_dimension=0, tiled=True).reshape(blocks.shape[1:])
    me = lax.axis_index(axis)
    bit = 1
    while bit < size:
        blocks = blocks.reshape((blocks.shape[0] // 2, 2) + blocks.shape[1:])
        mine = (me // bit) % 2
        keep = lax.dynamic_index_in_dim(blocks, mine, 1, keepdims=False)
        send = lax.dynamic_index_in_dim(blocks, 1 - mine, 1, keepdims=False)
        pairs = [(i, i ^ bit) for i in range(size)]
        blocks = keep + lax.ppermute(send, axis, pairs)
        bit *= 2
    return blocks[0]


def halve_step(values, dims, axis, bit, link_type):
    where = dims.index(f"{axis}{bit}")
    mine = (lax.axis_index(axis) // bit) % 2
    keep = lax.dynamic_index_in_dim(values, mine, where, keepdims=False)
    send = lax.dynamic_index_in_dim(values, 1 - mine, where, keepdims=False).astype(link_type)
    size = lax.axis_size(axis)
    got = lax.ppermute(send, axis, [(i, i ^ bit) for i in range(size)])
    return keep + got.astype(keep.dtype), dims[:where] + dims[where + 1 :]


def scatter_sum(term, channels):
    win_count = lax.axis_size("win")
    seq_count = lax.axis_size("seq")
    blocks = term.reshape(win_count, seq_count, -1, channels)
    rows = blocks.shape[2]
    if (win_count & (win_count - 1)) or (seq_count & (seq_count - 1)) or rows % 2:
        return halve_sum(halve_sum(blocks, "win"), "seq")
    win_bits = [("win", 1 << k) for k in range(win_count.bit_length() - 1)]
    seq_bits = [("seq", 1 << k) for k in range(seq_count.bit_length() - 1)]
    names = [f"{a}{b}" for a, b in reversed(win_bits)] + [f"{a}{b}" for a, b in reversed(seq_bits)]
    values = blocks.reshape([2] * len(names) + [rows, channels])
    first, middle, last = win_bits[:1], win_bits[1:], seq_bits
    ways = 2 if len(middle) >= 2 else 1
    dims = list(names)
    for axis, bit in first:
        values, dims = halve_step(values, dims, axis, bit, jnp.float32)
    lead = len(dims)
    parts = values.reshape(values.shape[:lead] + (ways, rows // ways, channels))
    states = [(lax.index_in_dim(parts, part, lead, keepdims=False), list(dims)) for part in range(ways)]
    for step in range(len(middle)):
        for part in range(ways):
            axis, bit = middle[(step + part) % len(middle)]
            states[part] = halve_step(states[part][0], states[part][1], axis, bit, jnp.bfloat16)
    values = jnp.concatenate([part for part, _ in states], axis=-2)
    dims = states[0][1]
    values = values.reshape((seq_count,) + values.shape[len(last) :])
    me = lax.axis_index("seq")
    total = lax.dynamic_index_in_dim(values, me, 0, keepdims=False)
    for shift in range(1, seq_count):
        send = lax.dynamic_index_in_dim(values, (me + shift) % seq_count, 0, keepdims=False)
        got = lax.ppermute(
            send.astype(jnp.bfloat16), "seq", [(i, (i + shift) % seq_count) for i in range(seq_count)]
        )
        total = total + got.astype(jnp.float32)
    return total


def gather_rows(block, axis):
    size = lax.axis_size(axis)
    me = lax.axis_index(axis)
    whole = jnp.zeros((size,) + block.shape, block.dtype)
    whole = lax.dynamic_update_index_in_dim(whole, block, me, 0)
    for shift in range(1, size):
        pairs = [(i, (i + shift) % size) for i in range(size)]
        got = lax.ppermute(block, axis, pairs)
        whole = lax.dynamic_update_index_in_dim(whole, got, (me - shift) % size, 0)
    return whole.reshape((-1,) + block.shape[1:])


def per_device(
    embeddings,
    norm_gain,
    conv_weight,
    conv_bias,
    dilation,
    donor_bins,
    acceptor_bins,
    junction_count,
    donor_proj,
    acceptor_proj,
    out_cotangent,
    score_cotangent,
):
    bin_count = embeddings.shape[1]
    channels = embeddings.shape[2]
    rim_width = bin_count // 2
    dilate = dilation[0]
    lanes = lax.broadcasted_iota(jnp.int32, (channels, channels), 0)
    mirror = (
        lanes + lax.broadcasted_iota(jnp.int32, (channels, channels), 1) == channels - 1
    ).astype(jnp.bfloat16)
    mirror = lax.optimization_barrier(mirror)
    own = slice(rim_width, rim_width + bin_count)

    padded_in = with_halo(jnp.stack([embeddings[0], out_cotangent[0]]), (("seq", 1),), rim_width)
    emb = padded_in[0]
    emb_rev = flip_channels(emb, mirror)
    as_float = emb.astype(jnp.float32)
    inverse = lax.rsqrt(jnp.mean(as_float * as_float, axis=1, keepdims=True) + epsilon)
    normed = as_float * inverse
    normed_rev = emb_rev.astype(jnp.float32) * inverse
    pre_fwd = normed * norm_gain
    pre_rev = normed_rev * norm_gain
    act_fwd = gelu_value(pre_fwd).astype(jnp.bfloat16)
    act_rev = gelu_value(pre_rev).astype(jnp.bfloat16)

    taps_fwd = tap_stack(act_fwd, dilate, rim_width, bin_count, 1)
    taps_rev = tap_stack(act_rev, dilate, rim_width, bin_count, -1)
    conv_all = (
        jnp.dot(
            jnp.concatenate([taps_fwd, taps_rev], axis=0),
            conv_weight.reshape(3 * channels, channels),
            preferred_element_type=jnp.float32,
        )
        + conv_bias
    ).astype(jnp.bfloat16)
    conv_fwd = conv_all[:bin_count]
    conv_rev = flip_channels(conv_all[bin_count:], mirror)
    block_flat = (
        as_float[own] + 0.5 * (conv_fwd.astype(jnp.float32) + conv_rev.astype(jnp.float32))
    ).astype(jnp.bfloat16)

    both_proj = jnp.concatenate([donor_proj, acceptor_proj], axis=1)
    hidden = donor_proj.shape[1]
    window_out = gather_rows(block_flat, "seq")
    window_proj = jnp.dot(window_out, both_proj, preferred_element_type=jnp.float32).astype(
        jnp.bfloat16
    )
    slots = lax.broadcasted_iota(jnp.int32, (donor_bins.shape[1], window_proj.shape[0]), 1)
    rows_donor = jnp.dot(
        (donor_bins[0][:, None] == slots).astype(jnp.bfloat16),
        window_proj[:, :hidden],
        preferred_element_type=jnp.float32,
    )
    rows_acceptor = jnp.dot(
        (acceptor_bins[0][:, None] == slots).astype(jnp.bfloat16),
        window_proj[:, hidden:],
        preferred_element_type=jnp.float32,
    )
    pair_total = donor_bins.shape[1]
    pair_share = pair_total // lax.axis_size("seq")
    pair_first = lax.axis_index("seq") * pair_share
    live_mask = (jnp.arange(pair_total) < junction_count[0]).astype(jnp.float32)
    score_scale = hidden ** (-0.5)
    products = jnp.sum(
        lax.dynamic_slice_in_dim(rows_donor, pair_first, pair_share, 0)
        * lax.dynamic_slice_in_dim(rows_acceptor, pair_first, pair_share, 0),
        axis=1,
    )
    junction_scores = (
        lax.dynamic_slice_in_dim(live_mask, pair_first, pair_share, 0) * products * score_scale
    )[None]
    pair_weight = score_cotangent[0] * live_mask * score_scale
    positions = lax.axis_index("seq") * bin_count - rim_width + jnp.arange(emb.shape[0])
    pick_donor = (positions[:, None] == donor_bins[0][None, :]).astype(jnp.float32)
    pick_acceptor = (positions[:, None] == acceptor_bins[0][None, :]).astype(jnp.float32)
    grad_donor = jnp.dot(
        pick_donor, pair_weight[:, None] * rows_acceptor, precision=lax.Precision.HIGHEST
    ).astype(jnp.bfloat16)
    grad_acceptor = jnp.dot(
        pick_acceptor, pair_weight[:, None] * rows_donor, precision=lax.Precision.HIGHEST
    ).astype(jnp.bfloat16)
    out_grad = padded_in[1].astype(jnp.float32) + lax.dot_general(
        jnp.concatenate([grad_donor, grad_acceptor], axis=1),
        both_proj,
        (((1,), (1,)), ((), ())),
        preferred_element_type=jnp.float32,
    )
    conv_grad = (0.5 * out_grad).astype(jnp.bfloat16)
    conv_grad_rev = flip_channels(conv_grad, mirror)
    back_fwd = tap_stack(conv_grad, dilate, rim_width, bin_count, -1)
    back_rev = tap_stack(conv_grad_rev, dilate, rim_width, bin_count, 1)
    dact_all = spread_back(jnp.concatenate([back_fwd, back_rev], axis=0), conv_weight, channels)
    dact_fwd = dact_all[:bin_count]
    dact_rev = dact_all[bin_count:]
    norm_rev = flip_channels(
        (dact_rev * gelu_slope(pre_rev[own]) * norm_gain).astype(jnp.bfloat16), mirror
    )
    norm_grad = dact_fwd * gelu_slope(pre_fwd[own]) * norm_gain + norm_rev.astype(jnp.float32)
    normed_own = normed[own]
    input_grad = (
        out_grad[own]
        + inverse[own]
        * (norm_grad - normed_own * jnp.mean(norm_grad * normed_own, axis=1, keepdims=True))
    ).astype(jnp.bfloat16)[None]
    grad_term = lax.dot_general(
        jnp.concatenate([act_fwd[own], act_rev[own]], axis=0),
        jnp.concatenate([conv_grad[own], conv_grad_rev[own]], axis=0),
        (((0,), (0,)), ((), ())),
        preferred_element_type=jnp.float32,
    )
    grad_term = grad_term / lax.axis_size("win")
    weight_grad = scatter_sum(grad_term, channels).reshape(-1)
    return (block_flat[None], junction_scores, input_grad, weight_grad)


def solution(mesh):
    return jax.shard_map(
        per_device,
        mesh=mesh,
        in_specs=(
            P("win", "seq", None),
            P(),
            P(),
            P(),
            P("win"),
            P("win", None),
            P("win", None),
            P("win"),
            P(),
            P(),
            P("win", "seq", None),
            P("win", None),
        ),
        out_specs=(
            P("win", "seq", None),
            P("win", "seq"),
            P("win", "seq", None),
            P(("win", "seq")),
        ),
        check_vma=False,
    )
```

```python
import jax
import jax.numpy as jnp
from jax import lax
from jax.sharding import PartitionSpec as P

epsilon = 1e-06
gelu_scale = 0.7978845608028654
gelu_cubic = 0.044715


def with_halo(block, sides, width):
    for axis, dim in sides:
        count = lax.axis_size(axis)
        forward = [(i, i + 1) for i in range(count - 1)]
        backward = [(target, source) for source, target in forward]
        low = lax.ppermute(
            lax.slice_in_dim(block, block.shape[dim] - width, None, axis=dim), axis, forward
        )
        high = lax.ppermute(lax.slice_in_dim(block, 0, width, axis=dim), axis, backward)
        block = jnp.concatenate([low, block, high], axis=dim)
    return block


def gelu_value(inputs):
    inner = gelu_scale * (inputs + gelu_cubic * inputs * inputs * inputs)
    return 0.5 * inputs * (1.0 + jnp.tanh(inner))


def gelu_slope(inputs):
    inner = gelu_scale * (inputs + gelu_cubic * inputs * inputs * inputs)
    tangent = jnp.tanh(inner)
    return 0.5 * (1.0 + tangent) + 0.5 * inputs * (1.0 - tangent * tangent) * gelu_scale * (
        1.0 + 3.0 * gelu_cubic * inputs * inputs
    )


def tap_stack(padded, dilate, rim_width, bin_count, sign):
    slices = [
        lax.dynamic_slice_in_dim(padded, rim_width + sign * (tap_index - 1) * dilate, bin_count, 0)
        for tap_index in range(3)
    ]
    return jnp.concatenate(slices, axis=1)


def flip_channels(values, mirror):
    return jnp.dot(values, mirror, preferred_element_type=jnp.float32).astype(jnp.bfloat16)


def spread_back(back_taps, weight, channels):
    result = jnp.zeros((back_taps.shape[0], channels), jnp.float32)
    for tap_index in range(3):
        result = result + lax.dot_general(
            back_taps[:, tap_index * channels : (tap_index + 1) * channels],
            weight[tap_index],
            (((1,), (1,)), ((), ())),
            preferred_element_type=jnp.float32,
        )
    return result


def halve_sum(blocks, axis):
    size = lax.axis_size(axis)
    if size & (size - 1):
        flat = blocks.reshape((-1,) + blocks.shape[2:])
        return lax.psum_scatter(flat, axis, scatter_dimension=0, tiled=True).reshape(blocks.shape[1:])
    me = lax.axis_index(axis)
    bit = 1
    while bit < size:
        blocks = blocks.reshape((blocks.shape[0] // 2, 2) + blocks.shape[1:])
        mine = (me // bit) % 2
        keep = lax.dynamic_index_in_dim(blocks, mine, 1, keepdims=False)
        send = lax.dynamic_index_in_dim(blocks, 1 - mine, 1, keepdims=False)
        pairs = [(i, i ^ bit) for i in range(size)]
        blocks = keep + lax.ppermute(send, axis, pairs)
        bit *= 2
    return blocks[0]


def halve_step(values, dims, axis, bit, link_type):
    where = dims.index(f"{axis}{bit}")
    mine = (lax.axis_index(axis) // bit) % 2
    keep = lax.dynamic_index_in_dim(values, mine, where, keepdims=False)
    send = lax.dynamic_index_in_dim(values, 1 - mine, where, keepdims=False).astype(link_type)
    size = lax.axis_size(axis)
    got = lax.ppermute(send, axis, [(i, i ^ bit) for i in range(size)])
    return keep + got.astype(keep.dtype), dims[:where] + dims[where + 1 :]


def scatter_sum(term, channels):
    win_count = lax.axis_size("win")
    seq_count = lax.axis_size("seq")
    blocks = term.reshape(win_count, seq_count, -1, channels)
    rows = blocks.shape[2]
    if (win_count & (win_count - 1)) or (seq_count & (seq_count - 1)) or rows % 2:
        return halve_sum(halve_sum(blocks, "win"), "seq")
    win_bits = [("win", 1 << k) for k in range(win_count.bit_length() - 1)]
    seq_bits = [("seq", 1 << k) for k in range(seq_count.bit_length() - 1)]
    names = [f"{a}{b}" for a, b in reversed(win_bits)] + [f"{a}{b}" for a, b in reversed(seq_bits)]
    values = blocks.reshape([2] * len(names) + [rows, channels])
    first, middle, last = win_bits[:1], win_bits[1:], seq_bits
    ways = 2 if len(middle) >= 2 else 1
    dims = list(names)
    for axis, bit in first:
        values, dims = halve_step(values, dims, axis, bit, jnp.float32)
    lead = len(dims)
    parts = values.reshape(values.shape[:lead] + (ways, rows // ways, channels))
    states = [(lax.index_in_dim(parts, part, lead, keepdims=False), list(dims)) for part in range(ways)]
    for step in range(len(middle)):
        for part in range(ways):
            axis, bit = middle[(step + part) % len(middle)]
            states[part] = halve_step(states[part][0], states[part][1], axis, bit, jnp.bfloat16)
    values = jnp.concatenate([part for part, _ in states], axis=-2)
    dims = states[0][1]
    values = values.reshape((seq_count,) + values.shape[len(last) :])
    me = lax.axis_index("seq")
    total = lax.dynamic_index_in_dim(values, me, 0, keepdims=False)
    for shift in range(1, seq_count):
        send = lax.dynamic_index_in_dim(values, (me + shift) % seq_count, 0, keepdims=False)
        got = lax.ppermute(
            send.astype(jnp.bfloat16), "seq", [(i, (i + shift) % seq_count) for i in range(seq_count)]
        )
        total = total + got.astype(jnp.float32)
    return total


def gather_rows(block, axis):
    size = lax.axis_size(axis)
    me = lax.axis_index(axis)
    whole = jnp.zeros((size,) + block.shape, block.dtype)
    whole = lax.dynamic_update_index_in_dim(whole, block, me, 0)
    for shift in range(1, size):
        pairs = [(i, (i + shift) % size) for i in range(size)]
        got = lax.ppermute(block, axis, pairs)
        whole = lax.dynamic_update_index_in_dim(whole, got, (me - shift) % size, 0)
    return whole.reshape((-1,) + block.shape[1:])


def per_device(
    embeddings,
    norm_gain,
    conv_weight,
    conv_bias,
    dilation,
    donor_bins,
    acceptor_bins,
    junction_count,
    donor_proj,
    acceptor_proj,
    out_cotangent,
    score_cotangent,
):
    bin_count = embeddings.shape[1]
    channels = embeddings.shape[2]
    rim_width = bin_count // 2
    dilate = dilation[0]
    lanes = lax.broadcasted_iota(jnp.int32, (channels, channels), 0)
    mirror = (
        lanes + lax.broadcasted_iota(jnp.int32, (channels, channels), 1) == channels - 1
    ).astype(jnp.bfloat16)
    mirror = lax.optimization_barrier(mirror)
    own = slice(rim_width, rim_width + bin_count)

    padded_in = with_halo(jnp.stack([embeddings[0], out_cotangent[0]]), (("seq", 1),), rim_width)
    emb = padded_in[0]
    emb_rev = flip_channels(emb, mirror)
    as_float = emb.astype(jnp.float32)
    inverse = lax.rsqrt(jnp.mean(as_float * as_float, axis=1, keepdims=True) + epsilon)
    normed = as_float * inverse
    normed_rev = emb_rev.astype(jnp.float32) * inverse
    pre_fwd = normed * norm_gain
    pre_rev = normed_rev * norm_gain
    act_fwd = gelu_value(pre_fwd).astype(jnp.bfloat16)
    act_rev = gelu_value(pre_rev).astype(jnp.bfloat16)

    taps_fwd = tap_stack(act_fwd, dilate, rim_width, bin_count, 1)
    taps_rev = tap_stack(act_rev, dilate, rim_width, bin_count, -1)
    conv_all = (
        jnp.dot(
            jnp.concatenate([taps_fwd, taps_rev], axis=0),
            conv_weight.reshape(3 * channels, channels),
            preferred_element_type=jnp.float32,
        )
        + conv_bias
    ).astype(jnp.bfloat16)
    conv_fwd = conv_all[:bin_count]
    conv_rev = flip_channels(conv_all[bin_count:], mirror)
    block_flat = (
        as_float[own] + 0.5 * (conv_fwd.astype(jnp.float32) + conv_rev.astype(jnp.float32))
    ).astype(jnp.bfloat16)

    both_proj = jnp.concatenate([donor_proj, acceptor_proj], axis=1)
    hidden = donor_proj.shape[1]
    window_out = gather_rows(block_flat, "seq")
    window_proj = jnp.dot(window_out, both_proj, preferred_element_type=jnp.float32).astype(
        jnp.bfloat16
    )
    slots = lax.broadcasted_iota(jnp.int32, (donor_bins.shape[1], window_proj.shape[0]), 1)
    select_donor, select_acceptor = lax.optimization_barrier(
        (
            (donor_bins[0][:, None] == slots).astype(jnp.bfloat16),
            (acceptor_bins[0][:, None] == slots).astype(jnp.bfloat16),
        )
    )
    rows_donor = jnp.dot(
        select_donor,
        window_proj[:, :hidden],
        preferred_element_type=jnp.float32,
    )
    rows_acceptor = jnp.dot(
        select_acceptor,
        window_proj[:, hidden:],
        preferred_element_type=jnp.float32,
    )
    pair_total = donor_bins.shape[1]
    pair_share = pair_total // lax.axis_size("seq")
    pair_first = lax.axis_index("seq") * pair_share
    live_mask = (jnp.arange(pair_total) < junction_count[0]).astype(jnp.float32)
    score_scale = hidden ** (-0.5)
    products = jnp.sum(
        lax.dynamic_slice_in_dim(rows_donor, pair_first, pair_share, 0)
        * lax.dynamic_slice_in_dim(rows_acceptor, pair_first, pair_share, 0),
        axis=1,
    )
    junction_scores = (
        lax.dynamic_slice_in_dim(live_mask, pair_first, pair_share, 0) * products * score_scale
    )[None]
    pair_weight = score_cotangent[0] * live_mask * score_scale
    positions = lax.axis_index("seq") * bin_count - rim_width + jnp.arange(emb.shape[0])
    pick_donor = (positions[:, None] == donor_bins[0][None, :]).astype(jnp.float32)
    pick_acceptor = (positions[:, None] == acceptor_bins[0][None, :]).astype(jnp.float32)
    grad_donor = jnp.dot(
        pick_donor, pair_weight[:, None] * rows_acceptor, precision=lax.Precision.HIGHEST
    ).astype(jnp.bfloat16)
    grad_acceptor = jnp.dot(
        pick_acceptor, pair_weight[:, None] * rows_donor, precision=lax.Precision.HIGHEST
    ).astype(jnp.bfloat16)
    out_grad = padded_in[1].astype(jnp.float32) + lax.dot_general(
        jnp.concatenate([grad_donor, grad_acceptor], axis=1),
        both_proj,
        (((1,), (1,)), ((), ())),
        preferred_element_type=jnp.float32,
    )
    conv_grad = (0.5 * out_grad).astype(jnp.bfloat16)
    conv_grad_rev = flip_channels(conv_grad, mirror)
    back_fwd = tap_stack(conv_grad, dilate, rim_width, bin_count, -1)
    back_rev = tap_stack(conv_grad_rev, dilate, rim_width, bin_count, 1)
    dact_all = spread_back(jnp.concatenate([back_fwd, back_rev], axis=0), conv_weight, channels)
    dact_fwd = dact_all[:bin_count]
    dact_rev = dact_all[bin_count:]
    norm_rev = flip_channels(
        (dact_rev * gelu_slope(pre_rev[own]) * norm_gain).astype(jnp.bfloat16), mirror
    )
    norm_grad = dact_fwd * gelu_slope(pre_fwd[own]) * norm_gain + norm_rev.astype(jnp.float32)
    normed_own = normed[own]
    input_grad = (
        out_grad[own]
        + inverse[own]
        * (norm_grad - normed_own * jnp.mean(norm_grad * normed_own, axis=1, keepdims=True))
    ).astype(jnp.bfloat16)[None]
    grad_term = lax.dot_general(
        jnp.concatenate([act_fwd[own], act_rev[own]], axis=0),
        jnp.concatenate([conv_grad[own], conv_grad_rev[own]], axis=0),
        (((0,), (0,)), ((), ())),
        preferred_element_type=jnp.float32,
    )
    grad_term = grad_term / lax.axis_size("win")
    weight_grad = scatter_sum(grad_term, channels).reshape(-1)
    return (block_flat[None], junction_scores, input_grad, weight_grad)


def solution(mesh):
    return jax.shard_map(
        per_device,
        mesh=mesh,
        in_specs=(
            P("win", "seq", None),
            P(),
            P(),
            P(),
            P("win"),
            P("win", None),
            P("win", None),
            P("win"),
            P(),
            P(),
            P("win", "seq", None),
            P("win", None),
        ),
        out_specs=(
            P("win", "seq", None),
            P("win", "seq"),
            P("win", "seq", None),
            P(("win", "seq")),
        ),
        check_vma=False,
    )
```
